32 devices in a mesh: snd: 8 (over z, y), rcv: 4 (over x, core).
Axes of the slice: x: 2, y: 2, z: 4, core: 2. Of those that a mesh axis runs over, the one named last changes fastest.
Arguments:
- tile_counts: bfloat16 [8, 4, 32, 256, 256], P('snd', 'rcv'), may hold values from 0 to 10, as said below
- tile_sender: int32 [8, 4, 32], P('snd', 'rcv'), may hold values from 0 to 1
- tile_receiver: int32 [8, 4, 32], P('snd', 'rcv'), may hold values from 0 to 3
- tile_action: int32 [8, 4, 32], P('snd', 'rcv'), may hold values from 0 to 255
- tile_fill: int32 [8, 4], P('snd', 'rcv'), may hold values from 1 to 32, as said below
- sender_log_shape: float32 [8, 96, 512], P('snd', None, 'rcv'), may hold values from -0.5 to 3
- sender_log_rate: float32 [8, 96, 512], P('snd', None, 'rcv')
- receiver_log_shape: float32 [4, 96, 1024], P('rcv', None, 'snd'), may hold values from -0.5 to 3
- receiver_log_rate: float32 [4, 96, 1024], P('rcv', None, 'snd')
- action_log_shape: float32 [96, 256], replicated, may hold values from -0.5 to 3
- action_log_rate: float32 [96, 256], replicated
Outputs:
- new_sender_log_shape: float32 [8, 96, 512], P('snd', None, 'rcv')
- new_sender_log_rate: float32 [8, 96, 512], P('snd', None, 'rcv')
- new_receiver_log_shape: float32 [4, 96, 1024], P('rcv', None, 'snd')
- new_receiver_log_rate: float32 [4, 96, 1024], P('rcv', None, 'snd')
- new_action_log_shape: float32 [96, 256], replicated
- new_action_log_rate: float32 [96, 256], replicated
The draws below stay inside these ranges and needn't reach their ends.
Inputs may be any that keep to these rules, and one draw needn't show every extreme that they name: tile_fill[p, q] is the number of live slots of that device, its first slots; slots beyond it are ignored. In every draw some device has all 32 slots live. `tile_counts`: non-negative weighted counts; many entries are zero.
All inputs are finite; a program needn't handle non-finite values.
Results may differ from the reference program's by a relative error of at most 0.004.
Values may be sent and summed in bfloat16 or wider, within the bound.
No kernel may reach another device: no remote copies, remote signals or barrier semaphores. Data moves between devices by JAX's collectives and lax.ppermute only.
A program may use at most 64 MiB of HBM per device.

```python
import math
import jax
import jax.numpy as jnp
import numpy as np
from jax import lax

K = 96
A = 256
BLK = 256
TILE_DEV = 32
SG = 512
RG = 1024
SB_GRP = 2
RB_GRP = 4
NS = 4096
NR = 4096
N_SND = 8
N_RCV = 4


def ramp_rates(key, lead_size, span_cols, by_lead):
    jitter = jax.random.uniform(key, (lead_size, K, span_cols), jnp.float32, -1.0, 1.0)
    rise_log = math.log(3.0)
    lead_pos = jnp.arange(lead_size, dtype=jnp.float32)[:, None, None]
    col_pos = jnp.arange(span_cols, dtype=jnp.float32)[None, None, :]
    if by_lead:
        position = (lead_pos * span_cols + col_pos) / (lead_size * span_cols)
    else:
        position = col_pos / span_cols + 0.0 * lead_pos
    return jitter - rise_log * position


def draw_sender_log_rate(key, part):
    return math.log(NS) + ramp_rates(jax.random.fold_in(key, 11), N_SND, SG, True)


def draw_receiver_log_rate(key, part):
    return math.log(NR) + ramp_rates(jax.random.fold_in(key, 13), N_RCV, RG, False)


def draw_action_log_rate(key, part):
    jitter = jax.random.uniform(jax.random.fold_in(key, 17), (K, A), jnp.float32, -1.0, 1.0)
    log_base = math.log(64.0 * A) - 0.5 * math.log(float(NS) * float(NR))
    return log_base + jitter


def draw_tile_counts(key, part):
    full_shape = (N_SND, N_RCV, TILE_DEV, BLK, BLK)
    tile_scale = jnp.exp(jax.random.uniform(jax.random.fold_in(key, 21), (N_SND, N_RCV, TILE_DEV, 1, 1), jnp.float32, math.log(0.05), math.log(5.0)))
    uniform_base = jax.random.uniform(jax.random.fold_in(key, 23), full_shape, jnp.float32, 0.0, 2.0)
    values = jnp.maximum(uniform_base - 1.0, 0.0) * 2.0
    return (values * tile_scale).astype(jnp.bfloat16)


def draw_tile_fill(key, part):
    live_counts = jax.random.randint(jax.random.fold_in(key, 31), (N_SND * N_RCV,), 1, TILE_DEV + 1)
    full_slot = jax.random.randint(jax.random.fold_in(key, 37), (), 0, N_SND * N_RCV)
    flat_counts = jnp.where(jnp.arange(N_SND * N_RCV) == full_slot, TILE_DEV, live_counts)
    return flat_counts.reshape(N_SND, N_RCV).astype(jnp.int32)


def touch_ends(values, own_key, low, top_value):
    place = [jax.random.randint(jax.random.fold_in(own_key, axis), (), 0, length) for axis, length in enumerate(values.shape)]
    main_axis = values.shape.index(max(values.shape))
    beside = place[:main_axis] + [(place[main_axis] + 1) % values.shape[main_axis]] + place[main_axis + 1:]
    return values.at[tuple(place)].set(low).at[tuple(beside)].set(top_value)


def block_scale(own_key, extent, cuts, least, high):
    factor_of, own = 1.0, jax.random.fold_in(own_key, 6)
    for dim, blocks in cuts:
        heights = jnp.exp(jax.random.uniform(jax.random.fold_in(own, dim), (blocks,), jnp.float32, least / len(cuts), high / len(cuts)))
        factor_of = factor_of * jnp.repeat(heights, extent[dim] // blocks).reshape([-1 if axis == dim else 1 for axis in range(len(extent))])
    return factor_of


def rank_bounds(count, slope):
    portions = [(1 << 20) // math.isqrt(grade ** slope) + 1 for grade in range(1, count + 1)]
    width = 1 + sum(portions) // (1 << 30)
    return np.cumsum(np.array([max(1, weight // width) for weight in portions]))


def ranked(own_key, extent, count, skew):
    table = rank_bounds(count, skew)
    pick = jax.random.randint(jax.random.fold_in(own_key, 1), extent, 0, int(table[count - 1]))
    rank = jnp.searchsorted(jnp.asarray(table, jnp.int32), pick, side="right")
    return jax.random.permutation(jax.random.fold_in(own_key, 2), count)[rank].astype(jnp.int32)


def setup_inputs(seed: int = 0) -> dict:
    seeds = jax.random.split(jax.random.key(seed), 12)
    return {
        "tile_counts": draw_tile_counts(jax.random.fold_in(seeds[11], 71), 0),
        "tile_sender": touch_ends(jax.random.randint(seeds[1], (N_SND, N_RCV, TILE_DEV), 0, SB_GRP), jax.random.fold_in(seeds[1], 1), 0, SB_GRP - 1).astype(jnp.int32),
        "tile_receiver": touch_ends(ranked(seeds[2], (N_SND, N_RCV, TILE_DEV), RB_GRP, 2), jax.random.fold_in(seeds[2], 3), 0, RB_GRP - 1).astype(jnp.int32),
        "tile_action": touch_ends(ranked(seeds[3], (N_SND, N_RCV, TILE_DEV), A, 2), jax.random.fold_in(seeds[3], 3), 0, A - 1).astype(jnp.int32),
        "tile_fill": draw_tile_fill(jax.random.fold_in(seeds[11], 71), 0),
        "sender_log_shape": jnp.clip(-0.5 + 3.5 * jax.random.uniform(seeds[5], (N_SND, K, SG), jnp.float32) ** block_scale(seeds[5], (N_SND, K, SG), ((0, 8), (2, 4)), -0.2, 0.2), -0.5, 3.0),
        "sender_log_rate": draw_sender_log_rate(jax.random.fold_in(seeds[11], 71), 0),
        "receiver_log_shape": jnp.clip(-0.5 + 3.5 * jax.random.uniform(seeds[7], (N_RCV, K, RG), jnp.float32) ** block_scale(seeds[7], (N_RCV, K, RG), ((0, 4), (2, 8)), -0.2, 0.2), -0.5, 3.0),
        "receiver_log_rate": draw_receiver_log_rate(jax.random.fold_in(seeds[11], 71), 0),
        "action_log_shape": jnp.clip(jax.random.uniform(seeds[9], (K, A), jnp.float32, -0.5, 3.0), -0.5, 3.0),
        "action_log_rate": draw_action_log_rate(jax.random.fold_in(seeds[11], 71), 0),
    }


prior_shape = 0.3
prior_rate = 0.3
step_size = 0.5


def digamma_series(value):
    shift_sum = jnp.zeros_like(value)
    for offset in range(6):
        shift_sum = shift_sum + 1.0 / (value + float(offset))
    moved = value + 6.0
    inverse = 1.0 / moved
    inv_square = inverse * inverse
    series = jnp.log(moved) - 0.5 * inverse - inv_square * (1.0 / 12.0 - inv_square * (1.0 / 120.0 - inv_square / 252.0))
    return series - shift_sum


def geometric(log_shape, log_rate):
    return jnp.exp(digamma_series(jnp.exp(log_shape)) - log_rate)


def refresh(log_value, target):
    return jnp.log((1.0 - step_size) * jnp.exp(log_value) + step_size * target)


def add_columns(running, addend, start_col):
    span_cols = addend.shape[1]
    current = lax.dynamic_slice_in_dim(running, start_col, span_cols, 1)
    return lax.dynamic_update_slice_in_dim(running, current + addend, start_col, 1)


def reference(tile_counts, tile_sender, tile_receiver, tile_action, tile_fill, sender_log_shape, sender_log_rate, receiver_log_shape, receiver_log_rate, action_log_shape, action_log_rate):
    sender_geo = geometric(sender_log_shape, sender_log_rate).astype(jnp.bfloat16)
    receiver_geo = geometric(receiver_log_shape, receiver_log_rate).astype(jnp.bfloat16)
    action_geo = geometric(action_log_shape, action_log_rate)

    def per_device(totals, device_id):
        send_stat, recv_stat, act_stat = totals
        snd_index = device_id // N_RCV
        rcv_index = device_id % N_RCV
        group_send = sender_geo[snd_index]
        group_recv = receiver_geo[rcv_index]
        live_count = tile_fill[snd_index, rcv_index]

        def per_tile(tile_totals, tile_item):
            send_term, recv_term, act_term = tile_totals
            count_tile, send_id, recv_id, act_id, slot_id = tile_item
            live_flag = (slot_id < live_count).astype(jnp.float32)
            send_cols = lax.dynamic_slice_in_dim(group_send, send_id * BLK, BLK, 1)
            recv_cols = lax.dynamic_slice_in_dim(group_recv, recv_id * BLK, BLK, 1)
            act_col = lax.dynamic_slice_in_dim(action_geo, act_id, 1, 1)
            scaled = (send_cols.astype(jnp.float32) * act_col).astype(jnp.bfloat16)
            expected = jnp.dot(scaled.T, recv_cols, preferred_element_type=jnp.float32)
            ratios = (count_tile.astype(jnp.float32) * live_flag / expected).astype(jnp.bfloat16)
            toward_send = jnp.dot(recv_cols, ratios.T, preferred_element_type=jnp.float32)
            toward_recv = jnp.dot(scaled, ratios, preferred_element_type=jnp.float32)
            send_part = scaled.astype(jnp.float32) * toward_send
            recv_part = recv_cols.astype(jnp.float32) * toward_recv
            act_part = jnp.sum(send_part, axis=1, keepdims=True)
            send_term = add_columns(send_term, send_part, send_id * BLK)
            recv_term = add_columns(recv_term, recv_part, recv_id * BLK)
            act_term = add_columns(act_term, act_part, act_id)
            return (send_term, recv_term, act_term), None

        initial = (jnp.zeros((K, SG), jnp.float32), jnp.zeros((K, RG), jnp.float32), jnp.zeros((K, A), jnp.float32))
        items = (tile_counts[snd_index, rcv_index], tile_sender[snd_index, rcv_index], tile_receiver[snd_index, rcv_index], tile_action[snd_index, rcv_index], jnp.arange(TILE_DEV, dtype=jnp.int32))
        (send_term, recv_term, act_term), unused = lax.scan(per_tile, initial, items)
        send_stat = send_stat.at[snd_index].add(send_term)
        recv_stat = recv_stat.at[rcv_index].add(recv_term)
        return (send_stat, recv_stat, act_stat + act_term), None

    start_totals = (jnp.zeros((N_SND, K, SG), jnp.float32), jnp.zeros((N_RCV, K, RG), jnp.float32), jnp.zeros((K, A), jnp.float32))
    (send_stat, recv_stat, act_stat), unused = lax.scan(per_device, start_totals, jnp.arange(N_SND * N_RCV, dtype=jnp.int32))
    sender_total = jnp.sum(jnp.exp(sender_log_shape - sender_log_rate), axis=(0, 2))
    receiver_total = jnp.sum(jnp.exp(receiver_log_shape - receiver_log_rate), axis=(0, 2))
    action_total = jnp.sum(jnp.exp(action_log_shape - action_log_rate), axis=1)
    new_sender_log_shape = refresh(sender_log_shape, prior_shape + send_stat)
    new_sender_log_rate = refresh(sender_log_rate, (prior_rate + receiver_total * action_total)[None, :, None])
    new_receiver_log_shape = refresh(receiver_log_shape, prior_shape + recv_stat)
    new_receiver_log_rate = refresh(receiver_log_rate, (prior_rate + sender_total * action_total)[None, :, None])
    new_action_log_shape = refresh(action_log_shape, prior_shape + act_stat)
    new_action_log_rate = refresh(action_log_rate, (prior_rate + sender_total * receiver_total)[:, None])
    return (new_sender_log_shape, new_sender_log_rate, new_receiver_log_shape, new_receiver_log_rate, new_action_log_shape, new_action_log_rate)
```

```python
import jax
import jax.numpy as jnp
from jax import lax
from jax.experimental import pallas as pl
from jax.experimental.pallas import tpu as pltpu
from jax.sharding import PartitionSpec as P

prior_shape = 0.3
prior_rate = 0.3
step_size = 0.5


def digamma_series(value):
    shift_sum = jnp.zeros_like(value)
    for offset in range(6):
        shift_sum = shift_sum + 1.0 / (value + float(offset))
    moved = value + 6.0
    inverse = 1.0 / moved
    inv_square = inverse * inverse
    series = (
        jnp.log(moved)
        - 0.5 * inverse
        - inv_square * (1.0 / 12.0 - inv_square * (1.0 / 120.0 - inv_square / 252.0))
    )
    return series - shift_sum


def geometric(log_shape, log_rate):
    return jnp.exp(digamma_series(jnp.exp(log_shape)) - log_rate)


def refresh(log_value, target):
    return jnp.log((1.0 - step_size) * jnp.exp(log_value) + step_size * target)


def tile_kernel(snd_ref, rcv_ref, act_ref, fill_ref, counts_ref, sgeo_ref, rgeo_ref, ageo_ref,
                sacc_ref, racc_ref, aacc_ref):
    t = pl.program_id(0)
    edge = counts_ref.shape[-1]
    n_sb = sgeo_ref.shape[1] // edge
    n_rb = rgeo_ref.shape[1] // edge
    n_act = ageo_ref.shape[1]

    @pl.when(t == 0)
    def _():
        sacc_ref[...] = jnp.zeros_like(sacc_ref)
        racc_ref[...] = jnp.zeros_like(racc_ref)
        aacc_ref[...] = jnp.zeros_like(aacc_ref)

    @pl.when(t < fill_ref[0])
    def _():
        b = jnp.clip(snd_ref[t], 0, n_sb - 1)
        c = jnp.clip(rcv_ref[t], 0, n_rb - 1)
        a = jnp.clip(act_ref[t], 0, n_act - 1)
        s0 = pl.multiple_of(b * edge, edge)
        r0 = pl.multiple_of(c * edge, edge)
        send_cols = sgeo_ref[:, pl.ds(s0, edge)]
        recv_cols = rgeo_ref[:, pl.ds(r0, edge)]
        ageo = ageo_ref[...]
        hit = lax.broadcasted_iota(jnp.int32, ageo.shape, 1) == a
        act_col = jnp.sum(jnp.where(hit, ageo, 0.0), axis=1, keepdims=True)
        scaled = (send_cols.astype(jnp.float32) * act_col).astype(jnp.bfloat16)
        expected = lax.dot_general(
            scaled, recv_cols, (((0,), (0,)), ((), ())), preferred_element_type=jnp.float32
        )
        ratios = (counts_ref[0].astype(jnp.float32) / expected).astype(jnp.bfloat16)
        toward_send = lax.dot_general(
            recv_cols, ratios, (((1,), (1,)), ((), ())), preferred_element_type=jnp.float32
        )
        toward_recv = jnp.dot(scaled, ratios, preferred_element_type=jnp.float32)
        send_part = scaled.astype(jnp.float32) * toward_send
        recv_part = recv_cols.astype(jnp.float32) * toward_recv
        act_part = jnp.sum(send_part, axis=1, keepdims=True)
        sacc_ref[:, pl.ds(s0, edge)] += send_part
        racc_ref[:, pl.ds(r0, edge)] += recv_part
        aacc_ref[...] += jnp.where(hit, act_part, 0.0)


def tile_pass(counts, senders, receivers, actions, fill, sender_geo, receiver_geo, action_geo):
    n_slots, edge = counts.shape[0], counts.shape[1]
    rank = sender_geo.shape[0]
    full = lambda shape: pl.BlockSpec(shape, lambda t, *_: (0,) * len(shape))
    grid_spec = pltpu.PrefetchScalarGridSpec(
        num_scalar_prefetch=4,
        grid=(n_slots,),
        in_specs=[
            pl.BlockSpec(
                (1, edge, edge),
                lambda t, s, r, a, f: (jnp.maximum(jnp.minimum(t, f[0] - 1), 0), 0, 0),
            ),
            full(sender_geo.shape),
            full(receiver_geo.shape),
            full(action_geo.shape),
        ],
        out_specs=[
            full((rank, sender_geo.shape[1])),
            full((rank, receiver_geo.shape[1])),
            full((rank, action_geo.shape[1])),
        ],
    )
    return pl.pallas_call(
        tile_kernel,
        grid_spec=grid_spec,
        out_shape=[
            jax.ShapeDtypeStruct((rank, sender_geo.shape[1]), jnp.float32),
            jax.ShapeDtypeStruct((rank, receiver_geo.shape[1]), jnp.float32),
            jax.ShapeDtypeStruct((rank, action_geo.shape[1]), jnp.float32),
        ],
        compiler_params=pltpu.CompilerParams(dimension_semantics=("arbitrary",)),
    )(senders, receivers, actions, fill, counts, sender_geo, receiver_geo, action_geo)


def per_device(
    tile_counts,
    tile_sender,
    tile_receiver,
    tile_action,
    tile_fill,
    sender_log_shape,
    sender_log_rate,
    receiver_log_shape,
    receiver_log_rate,
    action_log_shape,
    action_log_rate,
):
    own_send_shape = sender_log_shape[0]
    own_send_rate = sender_log_rate[0]
    own_recv_shape = receiver_log_shape[0]
    own_recv_rate = receiver_log_rate[0]
    own_send_geo = geometric(own_send_shape, own_send_rate).astype(jnp.bfloat16)
    own_recv_geo = geometric(own_recv_shape, own_recv_rate).astype(jnp.bfloat16)
    sender_geo = lax.all_gather(own_send_geo, "rcv", axis=1, tiled=True)
    receiver_geo = lax.all_gather(own_recv_geo, "snd", axis=1, tiled=True)
    action_geo = geometric(action_log_shape, action_log_rate)

    send_term, recv_term, act_term = tile_pass(
        tile_counts[0, 0],
        tile_sender[0, 0],
        tile_receiver[0, 0],
        tile_action[0, 0],
        tile_fill[0],
        sender_geo,
        receiver_geo,
        action_geo,
    )
    sender_part = jnp.sum(jnp.exp(own_send_shape - own_send_rate), axis=1)
    receiver_part = jnp.sum(jnp.exp(own_recv_shape - own_recv_rate), axis=1)
    sender_stat = lax.psum_scatter(
        send_term.astype(jnp.bfloat16), "rcv", scatter_dimension=1, tiled=True
    ).astype(jnp.float32)
    receiver_stat = lax.psum_scatter(recv_term, "snd", scatter_dimension=1, tiled=True)
    n_act = act_term.shape[1]
    stacked = jnp.concatenate([act_term, sender_part[:, None], receiver_part[:, None]], axis=1)
    stacked = lax.psum(stacked, ("snd", "rcv"))
    action_stat = stacked[:, :n_act]
    sender_total = stacked[:, n_act]
    receiver_total = stacked[:, n_act + 1]
    action_total = jnp.sum(jnp.exp(action_log_shape - action_log_rate), axis=1)
    new_send_shape = refresh(own_send_shape, prior_shape + sender_stat)
    new_send_rate = refresh(own_send_rate, (prior_rate + receiver_total * action_total)[:, None])
    new_recv_shape = refresh(own_recv_shape, prior_shape + receiver_stat)
    new_recv_rate = refresh(own_recv_rate, (prior_rate + sender_total * action_total)[:, None])
    new_act_shape = refresh(action_log_shape, prior_shape + action_stat)
    new_act_rate = refresh(action_log_rate, (prior_rate + sender_total * receiver_total)[:, None])
    return (
        new_send_shape[None],
        new_send_rate[None],
        new_recv_shape[None],
        new_recv_rate[None],
        new_act_shape,
        new_act_rate,
    )


def solution(mesh):
    return jax.shard_map(
        per_device,
        mesh=mesh,
        in_specs=(
            P("snd", "rcv", None, None, None),
            P("snd", "rcv", None),
            P("snd", "rcv", None),
            P("snd", "rcv", None),
            P("snd", "rcv"),
            P("snd", None, "rcv"),
            P("snd", None, "rcv"),
            P("rcv", None, "snd"),
            P("rcv", None, "snd"),
            P(),
            P(),
        ),
        out_specs=(
            P("snd", None, "rcv"),
            P("snd", None, "rcv"),
            P("rcv", None, "snd"),
            P("rcv", None, "snd"),
            P(),
            P(),
        ),
        check_vma=False,
    )
```

```python
import jax
import jax.numpy as jnp
from jax import lax
from jax.experimental import pallas as pl
from jax.experimental.pallas import tpu as pltpu
from jax.sharding import PartitionSpec as P

prior_shape = 0.3
prior_rate = 0.3
step_size = 0.5


def digamma_series(value):
    shift_sum = jnp.zeros_like(value)
    for offset in range(6):
        shift_sum = shift_sum + 1.0 / (value + float(offset))
    moved = value + 6.0
    inverse = 1.0 / moved
    inv_square = inverse * inverse
    series = (
        jnp.log(moved)
        - 0.5 * inverse
        - inv_square * (1.0 / 12.0 - inv_square * (1.0 / 120.0 - inv_square / 252.0))
    )
    return series - shift_sum


def geometric(log_shape, log_rate):
    return jnp.exp(digamma_series(jnp.exp(log_shape)) - log_rate)


def refresh(log_value, target):
    return jnp.log((1.0 - step_size) * jnp.exp(log_value) + step_size * target)


def is_pow2(n):
    return n > 0 and n & (n - 1) == 0


def swap(x, axis, n, dist):
    return lax.ppermute(x, axis, [(i, i ^ dist) for i in range(n)])


def gather_cols(x, axis, n):
    if not is_pow2(n):
        return lax.all_gather(x, axis, axis=1, tiled=True)
    me = lax.axis_index(axis)
    dist = 1
    while dist < n:
        theirs = swap(x, axis, n, dist)
        low = (me & dist) == 0
        x = jnp.where(low, jnp.concatenate([x, theirs], axis=1), jnp.concatenate([theirs, x], axis=1))
        dist *= 2
    return x


def sum_all(x, axes):
    for axis, n in axes:
        if not is_pow2(n):
            x = lax.psum(x, axis)
            continue
        dist = 1
        while dist < n:
            x = x + swap(x, axis, n, dist)
            dist *= 2
    return x


def scatter_cols(x, axis, n, extra=None):
    if not is_pow2(n):
        out = lax.psum_scatter(x, axis, scatter_dimension=1, tiled=True)
        return out, (None if extra is None else lax.psum(extra, axis))
    me = lax.axis_index(axis)
    dist = n // 2
    while dist >= 1:
        width = x.shape[1] // 2
        first, second = x[:, :width], x[:, width:]
        high = (me & dist) != 0
        keep = jnp.where(high, second, first)
        give = jnp.where(high, first, second)
        if extra is None:
            x = keep + swap(give, axis, n, dist)
        else:
            got, got_extra = swap((give, extra), axis, n, dist)
            x = keep + got
            extra = extra + got_extra
        dist //= 2
    return x, extra


def tile_kernel(snd_ref, rcv_ref, act_ref, fill_ref, counts_ref, sgeo_ref, rgeo_ref, ageo_ref,
                sacc_ref, racc_ref, aacc_ref):
    t = pl.program_id(0)
    edge = counts_ref.shape[-1]
    n_sb = sgeo_ref.shape[1] // edge
    n_rb = rgeo_ref.shape[1] // edge
    n_act = ageo_ref.shape[1]

    @pl.when(t == 0)
    def _():
        sacc_ref[...] = jnp.zeros_like(sacc_ref)
        racc_ref[...] = jnp.zeros_like(racc_ref)
        aacc_ref[...] = jnp.zeros_like(aacc_ref)

    @pl.when(t < fill_ref[0])
    def _():
        b = jnp.clip(snd_ref[t], 0, n_sb - 1)
        c = jnp.clip(rcv_ref[t], 0, n_rb - 1)
        a = jnp.clip(act_ref[t], 0, n_act - 1)
        s0 = pl.multiple_of(b * edge, edge)
        r0 = pl.multiple_of(c * edge, edge)
        send_cols = sgeo_ref[:, pl.ds(s0, edge)]
        recv_cols = rgeo_ref[:, pl.ds(r0, edge)]
        ageo = ageo_ref[...]
        hit = lax.broadcasted_iota(jnp.int32, ageo.shape, 1) == a
        act_col = jnp.sum(jnp.where(hit, ageo, 0.0), axis=1, keepdims=True)
        scaled = (send_cols.astype(jnp.float32) * act_col).astype(jnp.bfloat16)
        expected = lax.dot_general(
            scaled, recv_cols, (((0,), (0,)), ((), ())), preferred_element_type=jnp.float32
        )
        ratios = (counts_ref[0].astype(jnp.float32) / expected).astype(jnp.bfloat16)
        toward_send = lax.dot_general(
            recv_cols, ratios, (((1,), (1,)), ((), ())), preferred_element_type=jnp.float32
        )
        toward_recv = jnp.dot(scaled, ratios, preferred_element_type=jnp.float32)
        send_part = scaled.astype(jnp.float32) * toward_send
        recv_part = recv_cols.astype(jnp.float32) * toward_recv
        act_part = jnp.sum(send_part, axis=1, keepdims=True)
        sacc_ref[:, pl.ds(s0, edge)] += send_part
        racc_ref[:, pl.ds(r0, edge)] += recv_part
        aacc_ref[...] += jnp.where(hit, act_part, 0.0)


def tile_pass(counts, senders, receivers, actions, fill, sender_geo, receiver_geo, action_geo):
    n_slots, edge = counts.shape[0], counts.shape[1]
    rank = sender_geo.shape[0]
    full = lambda shape: pl.BlockSpec(shape, lambda t, *_: (0,) * len(shape))
    grid_spec = pltpu.PrefetchScalarGridSpec(
        num_scalar_prefetch=4,
        grid=(n_slots,),
        in_specs=[
            pl.BlockSpec(
                (1, edge, edge),
                lambda t, s, r, a, f: (jnp.maximum(jnp.minimum(t, f[0] - 1), 0), 0, 0),
            ),
            full(sender_geo.shape),
            full(receiver_geo.shape),
            full(action_geo.shape),
        ],
        out_specs=[
            full((rank, sender_geo.shape[1])),
            full((rank, receiver_geo.shape[1])),
            full((rank, action_geo.shape[1])),
        ],
    )
    return pl.pallas_call(
        tile_kernel,
        grid_spec=grid_spec,
        out_shape=[
            jax.ShapeDtypeStruct((rank, sender_geo.shape[1]), jnp.float32),
            jax.ShapeDtypeStruct((rank, receiver_geo.shape[1]), jnp.float32),
            jax.ShapeDtypeStruct((rank, action_geo.shape[1]), jnp.float32),
        ],
        compiler_params=pltpu.CompilerParams(dimension_semantics=("arbitrary",)),
    )(senders, receivers, actions, fill, counts, sender_geo, receiver_geo, action_geo)


def per_device(
    tile_counts,
    tile_sender,
    tile_receiver,
    tile_action,
    tile_fill,
    sender_log_shape,
    sender_log_rate,
    receiver_log_shape,
    receiver_log_rate,
    action_log_shape,
    action_log_rate,
):
    own_send_shape = sender_log_shape[0]
    own_send_rate = sender_log_rate[0]
    own_recv_shape = receiver_log_shape[0]
    own_recv_rate = receiver_log_rate[0]
    own_send_geo = geometric(own_send_shape, own_send_rate).astype(jnp.bfloat16)
    own_recv_geo = geometric(own_recv_shape, own_recv_rate).astype(jnp.bfloat16)
    n_snd = lax.psum(1, "snd")
    n_rcv = lax.psum(1, "rcv")
    sender_geo = gather_cols(own_send_geo, "rcv", n_rcv)
    receiver_geo = gather_cols(own_recv_geo, "snd", n_snd)
    action_geo = geometric(action_log_shape, action_log_rate)

    send_term, recv_term, act_term = tile_pass(
        tile_counts[0, 0],
        tile_sender[0, 0],
        tile_receiver[0, 0],
        tile_action[0, 0],
        tile_fill[0],
        sender_geo,
        receiver_geo,
        action_geo,
    )
    sender_part = jnp.sum(jnp.exp(own_send_shape - own_send_rate), axis=1)
    receiver_part = jnp.sum(jnp.exp(own_recv_shape - own_recv_rate), axis=1)
    n_act = act_term.shape[1]
    stacked = jnp.concatenate([act_term, sender_part[:, None], receiver_part[:, None]], axis=1)
    sender_stat, stacked = scatter_cols(send_term, "rcv", n_rcv, stacked)
    receiver_stat, stacked = scatter_cols(recv_term, "snd", n_snd, stacked)
    action_stat = stacked[:, :n_act]
    sender_total = stacked[:, n_act]
    receiver_total = stacked[:, n_act + 1]
    action_total = jnp.sum(jnp.exp(action_log_shape - action_log_rate), axis=1)
    new_send_shape = refresh(own_send_shape, prior_shape + sender_stat)
    new_send_rate = refresh(own_send_rate, (prior_rate + receiver_total * action_total)[:, None])
    new_recv_shape = refresh(own_recv_shape, prior_shape + receiver_stat)
    new_recv_rate = refresh(own_recv_rate, (prior_rate + sender_total * action_total)[:, None])
    new_act_shape = refresh(action_log_shape, prior_shape + action_stat)
    new_act_rate = refresh(action_log_rate, (prior_rate + sender_total * receiver_total)[:, None])
    return (
        new_send_shape[None],
        new_send_rate[None],
        new_recv_shape[None],
        new_recv_rate[None],
        new_act_shape,
        new_act_rate,
    )


def solution(mesh):
    return jax.shard_map(
        per_device,
        mesh=mesh,
        in_specs=(
            P("snd", "rcv", None, None, None),
            P("snd", "rcv", None),
            P("snd", "rcv", None),
            P("snd", "rcv", None),
            P("snd", "rcv"),
            P("snd", None, "rcv"),
            P("snd", None, "rcv"),
            P("rcv", None, "snd"),
            P("rcv", None, "snd"),
            P(),
            P(),
        ),
        out_specs=(
            P("snd", None, "rcv"),
            P("snd", None, "rcv"),
            P("rcv", None, "snd"),
            P("rcv", None, "snd"),
            P(),
            P(),
        ),
        check_vma=False,
    )
```

```python
import jax
import jax.numpy as jnp
from jax import lax
from jax.experimental import pallas as pl
from jax.experimental.pallas import tpu as pltpu
from jax.sharding import PartitionSpec as P

prior_shape = 0.3
prior_rate = 0.3
step_size = 0.5


def digamma_series(value):
    shift_sum = jnp.zeros_like(value)
    for offset in range(6):
        shift_sum = shift_sum + 1.0 / (value + float(offset))
    moved = value + 6.0
    inverse = 1.0 / moved
    inv_square = inverse * inverse
    series = (
        jnp.log(moved)
        - 0.5 * inverse
        - inv_square * (1.0 / 12.0 - inv_square * (1.0 / 120.0 - inv_square / 252.0))
    )
    return series - shift_sum


def geometric(log_shape, log_rate):
    return jnp.exp(digamma_series(jnp.exp(log_shape)) - log_rate)


def refresh(log_value, target):
    return jnp.log((1.0 - step_size) * jnp.exp(log_value) + step_size * target)


def is_pow2(n):
    return n > 0 and n & (n - 1) == 0


def swap(x, axis, n, dist):
    return lax.ppermute(x, axis, [(i, i ^ dist) for i in range(n)])


def gather_cols(x, axis, n):
    if not is_pow2(n):
        return lax.all_gather(x, axis, axis=1, tiled=True)
    me = lax.axis_index(axis)
    dist = 1
    while dist < n:
        theirs = swap(x, axis, n, dist)
        low = (me & dist) == 0
        x = jnp.where(low, jnp.concatenate([x, theirs], axis=1), jnp.concatenate([theirs, x], axis=1))
        dist *= 2
    return x


def sum_all(x, axes):
    for axis, n in axes:
        if not is_pow2(n):
            x = lax.psum(x, axis)
            continue
        dist = 1
        while dist < n:
            x = x + swap(x, axis, n, dist)
            dist *= 2
    return x


def scatter_cols(x, axis, n, extra=None):
    if not is_pow2(n):
        out = lax.psum_scatter(x, axis, scatter_dimension=1, tiled=True)
        return out, (None if extra is None else lax.psum(extra, axis))
    me = lax.axis_index(axis)
    dist = n // 2
    while dist >= 1:
        width = x.shape[1] // 2
        first, second = x[:, :width], x[:, width:]
        high = (me & dist) != 0
        keep = jnp.where(high, second, first)
        give = jnp.where(high, first, second)
        if extra is None:
            x = keep + swap(give, axis, n, dist)
        else:
            got, got_extra = swap((give, extra), axis, n, dist)
            x = keep + got
            extra = extra + got_extra
        dist //= 2
    return x, extra


def tile_kernel(snd_ref, rcv_ref, act_ref, fill_ref, counts_ref, sgeo_ref, sgeo_t_ref,
                rgeo_ref, rgeo_t_ref, ageo_ref, ageo_t_ref, sacc_t_ref, racc_ref, aacc_t_ref):
    t = pl.program_id(0)
    edge = counts_ref.shape[-1]
    n_sb = sgeo_ref.shape[1] // edge
    n_rb = rgeo_ref.shape[1] // edge
    n_act = ageo_ref.shape[1]

    @pl.when(t == 0)
    def _():
        sacc_t_ref[...] = jnp.zeros_like(sacc_t_ref)
        racc_ref[...] = jnp.zeros_like(racc_ref)
        aacc_t_ref[...] = jnp.zeros_like(aacc_t_ref)

    @pl.when(t < fill_ref[0])
    def _():
        b = jnp.clip(snd_ref[t], 0, n_sb - 1)
        c = jnp.clip(rcv_ref[t], 0, n_rb - 1)
        a = jnp.clip(act_ref[t], 0, n_act - 1)
        s0 = pl.multiple_of(b * edge, edge)
        r0 = pl.multiple_of(c * edge, edge)
        send_cols = sgeo_ref[:, pl.ds(s0, edge)]
        send_rows = sgeo_t_ref[pl.ds(s0, edge), :]
        recv_cols = rgeo_ref[:, pl.ds(r0, edge)]
        recv_rows = rgeo_t_ref[pl.ds(r0, edge), :]
        ageo = ageo_ref[...]
        ageo_t = ageo_t_ref[...]
        hit_col = lax.broadcasted_iota(jnp.int32, ageo.shape, 1) == a
        hit_row = lax.broadcasted_iota(jnp.int32, ageo_t.shape, 0) == a
        act_col = jnp.sum(jnp.where(hit_col, ageo, 0.0), axis=1, keepdims=True)
        act_row = jnp.sum(jnp.where(hit_row, ageo_t, 0.0), axis=0, keepdims=True)
        scaled = (send_cols.astype(jnp.float32) * act_col).astype(jnp.bfloat16)
        scaled_t = (send_rows.astype(jnp.float32) * act_row).astype(jnp.bfloat16)
        expected = jnp.dot(scaled_t, recv_cols, preferred_element_type=jnp.float32)
        ratios = (counts_ref[0].astype(jnp.float32) / expected).astype(jnp.bfloat16)
        toward_send_t = jnp.dot(ratios, recv_rows, preferred_element_type=jnp.float32)
        toward_recv = jnp.dot(scaled, ratios, preferred_element_type=jnp.float32)
        send_part_t = scaled_t.astype(jnp.float32) * toward_send_t
        recv_part = recv_cols.astype(jnp.float32) * toward_recv
        act_part = jnp.sum(send_part_t, axis=0, keepdims=True)
        sacc_t_ref[pl.ds(s0, edge), :] += send_part_t
        racc_ref[:, pl.ds(r0, edge)] += recv_part
        aacc_t_ref[...] += jnp.where(hit_row, act_part, 0.0)


def tile_pass(counts, senders, receivers, actions, fill, sender_geo, receiver_geo, action_geo):
    n_slots, edge = counts.shape[0], counts.shape[1]
    rank = sender_geo.shape[0]
    operands = (sender_geo, sender_geo.T, receiver_geo, receiver_geo.T, action_geo, action_geo.T)
    full = lambda shape: pl.BlockSpec(shape, lambda t, *_: (0,) * len(shape))
    out_shapes = [
        (sender_geo.shape[1], rank),
        (rank, receiver_geo.shape[1]),
        (action_geo.shape[1], rank),
    ]
    grid_spec = pltpu.PrefetchScalarGridSpec(
        num_scalar_prefetch=4,
        grid=(n_slots,),
        in_specs=[
            pl.BlockSpec(
                (1, edge, edge),
                lambda t, s, r, a, f: (jnp.maximum(jnp.minimum(t, f[0] - 1), 0), 0, 0),
            )
        ]
        + [full(x.shape) for x in operands],
        out_specs=[full(shape) for shape in out_shapes],
    )
    return pl.pallas_call(
        tile_kernel,
        grid_spec=grid_spec,
        out_shape=[jax.ShapeDtypeStruct(shape, jnp.float32) for shape in out_shapes],
        compiler_params=pltpu.CompilerParams(dimension_semantics=("arbitrary",)),
    )(senders, receivers, actions, fill, counts, *operands)


def per_device(
    tile_counts,
    tile_sender,
    tile_receiver,
    tile_action,
    tile_fill,
    sender_log_shape,
    sender_log_rate,
    receiver_log_shape,
    receiver_log_rate,
    action_log_shape,
    action_log_rate,
):
    own_send_shape = sender_log_shape[0]
    own_send_rate = sender_log_rate[0]
    own_recv_shape = receiver_log_shape[0]
    own_recv_rate = receiver_log_rate[0]
    own_send_geo = geometric(own_send_shape, own_send_rate).astype(jnp.bfloat16)
    own_recv_geo = geometric(own_recv_shape, own_recv_rate).astype(jnp.bfloat16)
    n_snd = lax.psum(1, "snd")
    n_rcv = lax.psum(1, "rcv")
    sender_geo = gather_cols(own_send_geo, "rcv", n_rcv)
    receiver_geo = gather_cols(own_recv_geo, "snd", n_snd)
    action_geo = geometric(action_log_shape, action_log_rate)

    send_term_t, recv_term, act_term_t = tile_pass(
        tile_counts[0, 0],
        tile_sender[0, 0],
        tile_receiver[0, 0],
        tile_action[0, 0],
        tile_fill[0],
        sender_geo,
        receiver_geo,
        action_geo,
    )
    sender_part = jnp.sum(jnp.exp(own_send_shape - own_send_rate), axis=1)
    receiver_part = jnp.sum(jnp.exp(own_recv_shape - own_recv_rate), axis=1)
    act_term = act_term_t.T
    send_term = send_term_t.T
    n_act = act_term.shape[1]
    stacked = jnp.concatenate([act_term, sender_part[:, None], receiver_part[:, None]], axis=1)
    sender_stat, stacked = scatter_cols(send_term, "rcv", n_rcv, stacked)
    receiver_stat, stacked = scatter_cols(recv_term, "snd", n_snd, stacked)
    action_stat = stacked[:, :n_act]
    sender_total = stacked[:, n_act]
    receiver_total = stacked[:, n_act + 1]
    action_total = jnp.sum(jnp.exp(action_log_shape - action_log_rate), axis=1)
    new_send_shape = refresh(own_send_shape, prior_shape + sender_stat)
    new_send_rate = refresh(own_send_rate, (prior_rate + receiver_total * action_total)[:, None])
    new_recv_shape = refresh(own_recv_shape, prior_shape + receiver_stat)
    new_recv_rate = refresh(own_recv_rate, (prior_rate + sender_total * action_total)[:, None])
    new_act_shape = refresh(action_log_shape, prior_shape + action_stat)
    new_act_rate = refresh(action_log_rate, (prior_rate + sender_total * receiver_total)[:, None])
    return (
        new_send_shape[None],
        new_send_rate[None],
        new_recv_shape[None],
        new_recv_rate[None],
        new_act_shape,
        new_act_rate,
    )


def solution(mesh):
    return jax.shard_map(
        per_device,
        mesh=mesh,
        in_specs=(
            P("snd", "rcv", None, None, None),
            P("snd", "rcv", None),
            P("snd", "rcv", None),
            P("snd", "rcv", None),
            P("snd", "rcv"),
            P("snd", None, "rcv"),
            P("snd", None, "rcv"),
            P("rcv", None, "snd"),
            P("rcv", None, "snd"),
            P(),
            P(),
        ),
        out_specs=(
            P("snd", None, "rcv"),
            P("snd", None, "rcv"),
            P("rcv", None, "snd"),
            P("rcv", None, "snd"),
            P(),
            P(),
        ),
        check_vma=False,
    )
```

```python
import jax
import jax.numpy as jnp
from jax import lax
from jax.experimental import pallas as pl
from jax.experimental.pallas import tpu as pltpu
from jax.sharding import PartitionSpec as P

prior_shape = 0.3
prior_rate = 0.3
step_size = 0.5


def digamma_series(value):
    shift_sum = jnp.zeros_like(value)
    for offset in range(6):
        shift_sum = shift_sum + 1.0 / (value + float(offset))
    moved = value + 6.0
    inverse = 1.0 / moved
    inv_square = inverse * inverse
    series = (
        jnp.log(moved)
        - 0.5 * inverse
        - inv_square * (1.0 / 12.0 - inv_square * (1.0 / 120.0 - inv_square / 252.0))
    )
    return series - shift_sum


def geometric(log_shape, log_rate):
    return jnp.exp(digamma_series(jnp.exp(log_shape)) - log_rate)


def refresh(log_value, target):
    return jnp.log((1.0 - step_size) * jnp.exp(log_value) + step_size * target)


def is_pow2(n):
    return n > 0 and n & (n - 1) == 0


def swap(x, axis, n, dist):
    return lax.ppermute(x, axis, [(i, i ^ dist) for i in range(n)])


def gather_cols(x, axis, n):
    if not is_pow2(n):
        return lax.all_gather(x, axis, axis=1, tiled=True)
    me = lax.axis_index(axis)
    dist = 1
    while dist < n:
        theirs = swap(x, axis, n, dist)
        low = (me & dist) == 0
        x = jnp.where(low, jnp.concatenate([x, theirs], axis=1), jnp.concatenate([theirs, x], axis=1))
        dist *= 2
    return x


def sum_all(x, axes):
    for axis, n in axes:
        if not is_pow2(n):
            x = lax.psum(x, axis)
            continue
        dist = 1
        while dist < n:
            x = x + swap(x, axis, n, dist)
            dist *= 2
    return x


def scatter_cols(x, axis, n, extra=None):
    if not is_pow2(n):
        out = lax.psum_scatter(x, axis, scatter_dimension=1, tiled=True)
        return out, (None if extra is None else lax.psum(extra, axis))
    me = lax.axis_index(axis)
    dist = n // 2
    while dist >= 1:
        width = x.shape[1] // 2
        first, second = x[:, :width], x[:, width:]
        high = (me & dist) != 0
        keep = jnp.where(high, second, first)
        give = jnp.where(high, first, second)
        if extra is None:
            x = keep + swap(give, axis, n, dist)
        else:
            got, got_extra = swap((give, extra), axis, n, dist)
            x = keep + got
            extra = extra + got_extra
        dist //= 2
    return x, extra


def tile_kernel(snd_ref, rcv_ref, act_ref, fill_ref, counts_ref, sgeo_ref, rgeo_ref, ageo_ref,
                sacc_ref, racc_ref, aacc_ref):
    t = pl.program_id(0)
    edge = counts_ref.shape[-1]
    n_sb = sgeo_ref.shape[1] // edge
    n_rb = rgeo_ref.shape[1] // edge
    n_act = ageo_ref.shape[1]

    @pl.when(t == 0)
    def _():
        sacc_ref[...] = jnp.zeros_like(sacc_ref)
        racc_ref[...] = jnp.zeros_like(racc_ref)
        aacc_ref[...] = jnp.zeros_like(aacc_ref)

    @pl.when(t < fill_ref[0])
    def _():
        b = jnp.clip(snd_ref[t], 0, n_sb - 1)
        c = jnp.clip(rcv_ref[t], 0, n_rb - 1)
        a = jnp.clip(act_ref[t], 0, n_act - 1)
        s0 = pl.multiple_of(b * edge, edge)
        r0 = pl.multiple_of(c * edge, edge)
        send_cols = sgeo_ref[:, pl.ds(s0, edge)]
        recv_cols = rgeo_ref[:, pl.ds(r0, edge)]
        ageo = ageo_ref[...]
        hit = lax.broadcasted_iota(jnp.int32, ageo.shape, 1) == a
        act_col = jnp.sum(jnp.where(hit, ageo, 0.0), axis=1, keepdims=True)
        scaled = (send_cols.astype(jnp.float32) * act_col).astype(jnp.bfloat16)
        expected = lax.dot_general(
            scaled, recv_cols, (((0,), (0,)), ((), ())), preferred_element_type=jnp.float32
        )
        ratios = (counts_ref[0].astype(jnp.float32) / expected).astype(jnp.bfloat16)
        toward_send = lax.dot_general(
            recv_cols, ratios, (((1,), (1,)), ((), ())), preferred_element_type=jnp.float32
        )
        toward_recv = jnp.dot(scaled, ratios, preferred_element_type=jnp.float32)
        send_part = scaled.astype(jnp.float32) * toward_send
        recv_part = recv_cols.astype(jnp.float32) * toward_recv
        act_part = jnp.sum(send_part, axis=1, keepdims=True)
        sacc_ref[:, pl.ds(s0, edge)] += send_part
        racc_ref[:, pl.ds(r0, edge)] += recv_part
        aacc_ref[...] += jnp.where(hit, act_part, 0.0)


def tile_pass(counts, senders, receivers, actions, fill, sender_geo, receiver_geo, action_geo):
    n_slots, edge = counts.shape[0], counts.shape[1]
    rank = sender_geo.shape[0]
    full = lambda shape: pl.BlockSpec(shape, lambda t, *_: (0,) * len(shape))
    grid_spec = pltpu.PrefetchScalarGridSpec(
        num_scalar_prefetch=4,
        grid=(n_slots,),
        in_specs=[
            pl.BlockSpec(
                (1, edge, edge),
                lambda t, s, r, a, f: (jnp.maximum(jnp.minimum(t, f[0] - 1), 0), 0, 0),
            ),
            full(sender_geo.shape),
            full(receiver_geo.shape),
            full(action_geo.shape),
        ],
        out_specs=[
            full((rank, sender_geo.shape[1])),
            full((rank, receiver_geo.shape[1])),
            full((rank, action_geo.shape[1])),
        ],
    )
    return pl.pallas_call(
        tile_kernel,
        grid_spec=grid_spec,
        out_shape=[
            jax.ShapeDtypeStruct((rank, sender_geo.shape[1]), jnp.float32),
            jax.ShapeDtypeStruct((rank, receiver_geo.shape[1]), jnp.float32),
            jax.ShapeDtypeStruct((rank, action_geo.shape[1]), jnp.float32),
        ],
        compiler_params=pltpu.CompilerParams(dimension_semantics=("arbitrary",)),
    )(senders, receivers, actions, fill, counts, sender_geo, receiver_geo, action_geo)


def per_device(
    tile_counts,
    tile_sender,
    tile_receiver,
    tile_action,
    tile_fill,
    sender_log_shape,
    sender_log_rate,
    receiver_log_shape,
    receiver_log_rate,
    action_log_shape,
    action_log_rate,
):
    own_send_shape = sender_log_shape[0]
    own_send_rate = sender_log_rate[0]
    own_recv_shape = receiver_log_shape[0]
    own_recv_rate = receiver_log_rate[0]
    own_send_geo = geometric(own_send_shape, own_send_rate).astype(jnp.bfloat16)
    own_recv_geo = geometric(own_recv_shape, own_recv_rate).astype(jnp.bfloat16)
    n_snd = lax.psum(1, "snd")
    n_rcv = lax.psum(1, "rcv")
    sender_geo = gather_cols(own_send_geo, "rcv", n_rcv)
    receiver_geo = gather_cols(own_recv_geo, "snd", n_snd)
    action_geo = geometric(action_log_shape, action_log_rate)

    send_term, recv_term, act_term = tile_pass(
        tile_counts[0, 0],
        tile_sender[0, 0],
        tile_receiver[0, 0],
        tile_action[0, 0],
        tile_fill[0],
        sender_geo,
        receiver_geo,
        action_geo,
    )
    sender_part = jnp.sum(jnp.exp(own_send_shape - own_send_rate), axis=1)
    receiver_part = jnp.sum(jnp.exp(own_recv_shape - own_recv_rate), axis=1)
    n_act = act_term.shape[1]
    stacked = jnp.concatenate([act_term, sender_part[:, None], receiver_part[:, None]], axis=1)
    stacked = sum_all(stacked, (("snd", n_snd), ("rcv", n_rcv)))
    sender_stat, unused = scatter_cols(send_term, "rcv", n_rcv)
    receiver_stat, unused = scatter_cols(recv_term, "snd", n_snd)
    action_stat = stacked[:, :n_act]
    sender_total = stacked[:, n_act]
    receiver_total = stacked[:, n_act + 1]
    action_total = jnp.sum(jnp.exp(action_log_shape - action_log_rate), axis=1)
    new_send_shape = refresh(own_send_shape, prior_shape + sender_stat)
    new_send_rate = refresh(own_send_rate, (prior_rate + receiver_total * action_total)[:, None])
    new_recv_shape = refresh(own_recv_shape, prior_shape + receiver_stat)
    new_recv_rate = refresh(own_recv_rate, (prior_rate + sender_total * action_total)[:, None])
    new_act_shape = refresh(action_log_shape, prior_shape + action_stat)
    new_act_rate = refresh(action_log_rate, (prior_rate + sender_total * receiver_total)[:, None])
    return (
        new_send_shape[None],
        new_send_rate[None],
        new_recv_shape[None],
        new_recv_rate[None],
        new_act_shape,
        new_act_rate,
    )


def solution(mesh):
    return jax.shard_map(
        per_device,
        mesh=mesh,
        in_specs=(
            P("snd", "rcv", None, None, None),
            P("snd", "rcv", None),
            P("snd", "rcv", None),
            P("snd", "rcv", None),
            P("snd", "rcv"),
            P("snd", None, "rcv"),
            P("snd", None, "rcv"),
            P("rcv", None, "snd"),
            P("rcv", None, "snd"),
            P(),
            P(),
        ),
        out_specs=(
            P("snd", None, "rcv"),
            P("snd", None, "rcv"),
            P("rcv", None, "snd"),
            P("rcv", None, "snd"),
            P(),
            P(),
        ),
        check_vma=False,
    )
```

```python
import jax
import jax.numpy as jnp
from jax import lax
from jax.experimental import pallas as pl
from jax.experimental.pallas import tpu as pltpu
from jax.sharding import PartitionSpec as P

prior_shape = 0.3
prior_rate = 0.3
step_size = 0.5
tile_group = 4


def digamma_series(value):
    shift_sum = jnp.zeros_like(value)
    for offset in range(6):
        shift_sum = shift_sum + 1.0 / (value + float(offset))
    moved = value + 6.0
    inverse = 1.0 / moved
    inv_square = inverse * inverse
    series = (
        jnp.log(moved)
        - 0.5 * inverse
        - inv_square * (1.0 / 12.0 - inv_square * (1.0 / 120.0 - inv_square / 252.0))
    )
    return series - shift_sum


def geometric(log_shape, log_rate):
    return jnp.exp(digamma_series(jnp.exp(log_shape)) - log_rate)


def refresh(log_value, target):
    return jnp.log((1.0 - step_size) * jnp.exp(log_value) + step_size * target)


def is_pow2(n):
    return n > 0 and n & (n - 1) == 0


def swap(x, axis, n, dist):
    return lax.ppermute(x, axis, [(i, i ^ dist) for i in range(n)])


def gather_cols(x, axis, n):
    if not is_pow2(n):
        return lax.all_gather(x, axis, axis=1, tiled=True)
    me = lax.axis_index(axis)
    dist = 1
    while dist < n:
        theirs = swap(x, axis, n, dist)
        low = (me & dist) == 0
        x = jnp.where(low, jnp.concatenate([x, theirs], axis=1), jnp.concatenate([theirs, x], axis=1))
        dist *= 2
    return x


def sum_all(x, axes):
    for axis, n in axes:
        if not is_pow2(n):
            x = lax.psum(x, axis)
            continue
        dist = 1
        while dist < n:
            x = x + swap(x, axis, n, dist)
            dist *= 2
    return x


def scatter_cols(x, axis, n, extra=None):
    if not is_pow2(n):
        out = lax.psum_scatter(x, axis, scatter_dimension=1, tiled=True)
        return out, (None if extra is None else lax.psum(extra, axis))
    me = lax.axis_index(axis)
    dist = n // 2
    while dist >= 1:
        width = x.shape[1] // 2
        first, second = x[:, :width], x[:, width:]
        high = (me & dist) != 0
        keep = jnp.where(high, second, first)
        give = jnp.where(high, first, second)
        if extra is None:
            x = keep + swap(give, axis, n, dist)
        else:
            got, got_extra = swap((give, extra), axis, n, dist)
            x = keep + got
            extra = extra + got_extra
        dist //= 2
    return x, extra


def tile_kernel(snd_ref, rcv_ref, act_ref, fill_ref, counts_ref, sgeo_ref, rgeo_ref, ageo_ref,
                sacc_ref, racc_ref, aacc_ref):
    step = pl.program_id(0)
    group = counts_ref.shape[0]
    edge = counts_ref.shape[-1]
    n_sb = sgeo_ref.shape[1] // edge
    n_rb = rgeo_ref.shape[1] // edge
    n_act = ageo_ref.shape[1]

    @pl.when(step == 0)
    def _():
        sacc_ref[...] = jnp.zeros_like(sacc_ref)
        racc_ref[...] = jnp.zeros_like(racc_ref)
        aacc_ref[...] = jnp.zeros_like(aacc_ref)

    for slot in range(group):
        pl.when(step * group + slot < fill_ref[0])(
            lambda slot=slot: one_tile(step * group + slot, counts_ref.at[slot], snd_ref, rcv_ref,
                                       act_ref, sgeo_ref, rgeo_ref, ageo_ref, sacc_ref, racc_ref,
                                       aacc_ref, edge, n_sb, n_rb, n_act)
        )


def one_tile(t, tile_ref, snd_ref, rcv_ref, act_ref, sgeo_ref, rgeo_ref, ageo_ref, sacc_ref,
             racc_ref, aacc_ref, edge, n_sb, n_rb, n_act):
    b = jnp.clip(snd_ref[t], 0, n_sb - 1)
    c = jnp.clip(rcv_ref[t], 0, n_rb - 1)
    a = jnp.clip(act_ref[t], 0, n_act - 1)
    s0 = pl.multiple_of(b * edge, edge)
    r0 = pl.multiple_of(c * edge, edge)
    send_cols = sgeo_ref[:, pl.ds(s0, edge)]
    recv_cols = rgeo_ref[:, pl.ds(r0, edge)]
    ageo = ageo_ref[...]
    hit = lax.broadcasted_iota(jnp.int32, ageo.shape, 1) == a
    act_col = jnp.sum(jnp.where(hit, ageo, 0.0), axis=1, keepdims=True)
    scaled = (send_cols.astype(jnp.float32) * act_col).astype(jnp.bfloat16)
    expected = lax.dot_general(
        scaled, recv_cols, (((0,), (0,)), ((), ())), preferred_element_type=jnp.float32
    )
    ratios = (tile_ref[...].astype(jnp.float32) / expected).astype(jnp.bfloat16)
    toward_send = lax.dot_general(
        recv_cols, ratios, (((1,), (1,)), ((), ())), preferred_element_type=jnp.float32
    )
    toward_recv = jnp.dot(scaled, ratios, preferred_element_type=jnp.float32)
    send_part = scaled.astype(jnp.float32) * toward_send
    recv_part = recv_cols.astype(jnp.float32) * toward_recv
    act_part = jnp.sum(send_part, axis=1, keepdims=True)
    sacc_ref[:, pl.ds(s0, edge)] += send_part
    racc_ref[:, pl.ds(r0, edge)] += recv_part
    aacc_ref[...] += jnp.where(hit, act_part, 0.0)


def tile_pass(counts, senders, receivers, actions, fill, sender_geo, receiver_geo, action_geo):
    n_slots, edge = counts.shape[0], counts.shape[1]
    group = tile_group if n_slots % tile_group == 0 else 1
    rank = sender_geo.shape[0]
    full = lambda shape: pl.BlockSpec(shape, lambda t, *_: (0,) * len(shape))
    grid_spec = pltpu.PrefetchScalarGridSpec(
        num_scalar_prefetch=4,
        grid=(n_slots // group,),
        in_specs=[
            pl.BlockSpec(
                (group, edge, edge),
                lambda g, s, r, a, f: (jnp.minimum(g, jnp.maximum(f[0] - 1, 0) // group), 0, 0),
            ),
            full(sender_geo.shape),
            full(receiver_geo.shape),
            full(action_geo.shape),
        ],
        out_specs=[
            full((rank, sender_geo.shape[1])),
            full((rank, receiver_geo.shape[1])),
            full((rank, action_geo.shape[1])),
        ],
    )
    return pl.pallas_call(
        tile_kernel,
        grid_spec=grid_spec,
        out_shape=[
            jax.ShapeDtypeStruct((rank, sender_geo.shape[1]), jnp.float32),
            jax.ShapeDtypeStruct((rank, receiver_geo.shape[1]), jnp.float32),
            jax.ShapeDtypeStruct((rank, action_geo.shape[1]), jnp.float32),
        ],
        compiler_params=pltpu.CompilerParams(dimension_semantics=("arbitrary",)),
    )(senders, receivers, actions, fill, counts, sender_geo, receiver_geo, action_geo)


def per_device(
    tile_counts,
    tile_sender,
    tile_receiver,
    tile_action,
    tile_fill,
    sender_log_shape,
    sender_log_rate,
    receiver_log_shape,
    receiver_log_rate,
    action_log_shape,
    action_log_rate,
):
    own_send_shape = sender_log_shape[0]
    own_send_rate = sender_log_rate[0]
    own_recv_shape = receiver_log_shape[0]
    own_recv_rate = receiver_log_rate[0]
    own_send_geo = geometric(own_send_shape, own_send_rate).astype(jnp.bfloat16)
    own_recv_geo = geometric(own_recv_shape, own_recv_rate).astype(jnp.bfloat16)
    n_snd = lax.psum(1, "snd")
    n_rcv = lax.psum(1, "rcv")
    sender_geo = gather_cols(own_send_geo, "rcv", n_rcv)
    receiver_geo = gather_cols(own_recv_geo, "snd", n_snd)
    action_geo = geometric(action_log_shape, action_log_rate)

    send_term, recv_term, act_term = tile_pass(
        tile_counts[0, 0],
        tile_sender[0, 0],
        tile_receiver[0, 0],
        tile_action[0, 0],
        tile_fill[0],
        sender_geo,
        receiver_geo,
        action_geo,
    )
    sender_part = jnp.sum(jnp.exp(own_send_shape - own_send_rate), axis=1)
    receiver_part = jnp.sum(jnp.exp(own_recv_shape - own_recv_rate), axis=1)
    n_act = act_term.shape[1]
    stacked = jnp.concatenate([act_term, sender_part[:, None], receiver_part[:, None]], axis=1)
    stacked = sum_all(stacked, (("snd", n_snd), ("rcv", n_rcv)))
    sender_stat, unused = scatter_cols(send_term, "rcv", n_rcv)
    receiver_stat, unused = scatter_cols(recv_term, "snd", n_snd)
    action_stat = stacked[:, :n_act]
    sender_total = stacked[:, n_act]
    receiver_total = stacked[:, n_act + 1]
    action_total = jnp.sum(jnp.exp(action_log_shape - action_log_rate), axis=1)
    new_send_shape = refresh(own_send_shape, prior_shape + sender_stat)
    new_send_rate = refresh(own_send_rate, (prior_rate + receiver_total * action_total)[:, None])
    new_recv_shape = refresh(own_recv_shape, prior_shape + receiver_stat)
    new_recv_rate = refresh(own_recv_rate, (prior_rate + sender_total * action_total)[:, None])
    new_act_shape = refresh(action_log_shape, prior_shape + action_stat)
    new_act_rate = refresh(action_log_rate, (prior_rate + sender_total * receiver_total)[:, None])
    return (
        new_send_shape[None],
        new_send_rate[None],
        new_recv_shape[None],
        new_recv_rate[None],
        new_act_shape,
        new_act_rate,
    )


def solution(mesh):
    return jax.shard_map(
        per_device,
        mesh=mesh,
        in_specs=(
            P("snd", "rcv", None, None, None),
            P("snd", "rcv", None),
            P("snd", "rcv", None),
            P("snd", "rcv", None),
            P("snd", "rcv"),
            P("snd", None, "rcv"),
            P("snd", None, "rcv"),
            P("rcv", None, "snd"),
            P("rcv", None, "snd"),
            P(),
            P(),
        ),
        out_specs=(
            P("snd", None, "rcv"),
            P("snd", None, "rcv"),
            P("rcv", None, "snd"),
            P("rcv", None, "snd"),
            P(),
            P(),
        ),
        check_vma=False,
    )
```

```python
import jax
import jax.numpy as jnp
from jax import lax
from jax.experimental import pallas as pl
from jax.experimental.pallas import tpu as pltpu
from jax.sharding import PartitionSpec as P

prior_shape = 0.3
prior_rate = 0.3
step_size = 0.5
tile_group = 8


def digamma_series(value):
    shift_sum = jnp.zeros_like(value)
    for offset in range(6):
        shift_sum = shift_sum + 1.0 / (value + float(offset))
    moved = value + 6.0
    inverse = 1.0 / moved
    inv_square = inverse * inverse
    series = (
        jnp.log(moved)
        - 0.5 * inverse
        - inv_square * (1.0 / 12.0 - inv_square * (1.0 / 120.0 - inv_square / 252.0))
    )
    return series - shift_sum


def geometric(log_shape, log_rate):
    return jnp.exp(digamma_series(jnp.exp(log_shape)) - log_rate)


def refresh(log_value, target):
    return jnp.log((1.0 - step_size) * jnp.exp(log_value) + step_size * target)


def is_pow2(n):
    return n > 0 and n & (n - 1) == 0


def swap(x, axis, n, dist):
    return lax.ppermute(x, axis, [(i, i ^ dist) for i in range(n)])


def gather_cols(x, axis, n):
    if not is_pow2(n):
        return lax.all_gather(x, axis, axis=1, tiled=True)
    me = lax.axis_index(axis)
    dist = 1
    while dist < n:
        theirs = swap(x, axis, n, dist)
        low = (me & dist) == 0
        x = jnp.where(low, jnp.concatenate([x, theirs], axis=1), jnp.concatenate([theirs, x], axis=1))
        dist *= 2
    return x


def sum_all(x, axes):
    for axis, n in axes:
        if not is_pow2(n):
            x = lax.psum(x, axis)
            continue
        dist = 1
        while dist < n:
            x = x + swap(x, axis, n, dist)
            dist *= 2
    return x


def scatter_cols(x, axis, n, extra=None):
    if not is_pow2(n):
        out = lax.psum_scatter(x, axis, scatter_dimension=1, tiled=True)
        return out, (None if extra is None else lax.psum(extra, axis))
    me = lax.axis_index(axis)
    dist = n // 2
    while dist >= 1:
        width = x.shape[1] // 2
        first, second = x[:, :width], x[:, width:]
        high = (me & dist) != 0
        keep = jnp.where(high, second, first)
        give = jnp.where(high, first, second)
        if extra is None:
            x = keep + swap(give, axis, n, dist)
        else:
            got, got_extra = swap((give, extra), axis, n, dist)
            x = keep + got
            extra = extra + got_extra
        dist //= 2
    return x, extra


def tile_kernel(snd_ref, rcv_ref, act_ref, fill_ref, counts_ref, sgeo_ref, rgeo_ref, ageo_ref,
                sacc_ref, racc_ref, aacc_ref):
    step = pl.program_id(0)
    group = counts_ref.shape[0]
    edge = counts_ref.shape[-1]
    n_sb = sgeo_ref.shape[1] // edge
    n_rb = rgeo_ref.shape[1] // edge
    n_act = ageo_ref.shape[1]

    @pl.when(step == 0)
    def _():
        sacc_ref[...] = jnp.zeros_like(sacc_ref)
        racc_ref[...] = jnp.zeros_like(racc_ref)
        aacc_ref[...] = jnp.zeros_like(aacc_ref)

    for slot in range(group):
        pl.when(step * group + slot < fill_ref[0])(
            lambda slot=slot: one_tile(step * group + slot, counts_ref.at[slot], snd_ref, rcv_ref,
                                       act_ref, sgeo_ref, rgeo_ref, ageo_ref, sacc_ref, racc_ref,
                                       aacc_ref, edge, n_sb, n_rb, n_act)
        )


def one_tile(t, tile_ref, snd_ref, rcv_ref, act_ref, sgeo_ref, rgeo_ref, ageo_ref, sacc_ref,
             racc_ref, aacc_ref, edge, n_sb, n_rb, n_act):
    b = jnp.clip(snd_ref[t], 0, n_sb - 1)
    c = jnp.clip(rcv_ref[t], 0, n_rb - 1)
    a = jnp.clip(act_ref[t], 0, n_act - 1)
    s0 = pl.multiple_of(b * edge, edge)
    r0 = pl.multiple_of(c * edge, edge)
    send_cols = sgeo_ref[:, pl.ds(s0, edge)]
    recv_cols = rgeo_ref[:, pl.ds(r0, edge)]
    ageo = ageo_ref[...]
    hit = lax.broadcasted_iota(jnp.int32, ageo.shape, 1) == a
    act_col = jnp.sum(jnp.where(hit, ageo, 0.0), axis=1, keepdims=True)
    scaled = (send_cols.astype(jnp.float32) * act_col).astype(jnp.bfloat16)
    expected = lax.dot_general(
        scaled, recv_cols, (((0,), (0,)), ((), ())), preferred_element_type=jnp.float32
    )
    ratios = (tile_ref[...].astype(jnp.float32) / expected).astype(jnp.bfloat16)
    toward_send = lax.dot_general(
        recv_cols, ratios, (((1,), (1,)), ((), ())), preferred_element_type=jnp.float32
    )
    toward_recv = jnp.dot(scaled, ratios, preferred_element_type=jnp.float32)
    send_part = scaled.astype(jnp.float32) * toward_send
    recv_part = recv_cols.astype(jnp.float32) * toward_recv
    act_part = jnp.sum(send_part, axis=1, keepdims=True)
    sacc_ref[:, pl.ds(s0, edge)] += send_part
    racc_ref[:, pl.ds(r0, edge)] += recv_part
    aacc_ref[...] += jnp.where(hit, act_part, 0.0)


def tile_pass(counts, senders, receivers, actions, fill, sender_geo, receiver_geo, action_geo):
    n_slots, edge = counts.shape[0], counts.shape[1]
    group = tile_group if n_slots % tile_group == 0 else 1
    rank = sender_geo.shape[0]
    full = lambda shape: pl.BlockSpec(shape, lambda t, *_: (0,) * len(shape))
    grid_spec = pltpu.PrefetchScalarGridSpec(
        num_scalar_prefetch=4,
        grid=(n_slots // group,),
        in_specs=[
            pl.BlockSpec(
                (group, edge, edge),
                lambda g, s, r, a, f: (jnp.minimum(g, jnp.maximum(f[0] - 1, 0) // group), 0, 0),
            ),
            full(sender_geo.shape),
            full(receiver_geo.shape),
            full(action_geo.shape),
        ],
        out_specs=[
            full((rank, sender_geo.shape[1])),
            full((rank, receiver_geo.shape[1])),
            full((rank, action_geo.shape[1])),
        ],
    )
    return pl.pallas_call(
        tile_kernel,
        grid_spec=grid_spec,
        out_shape=[
            jax.ShapeDtypeStruct((rank, sender_geo.shape[1]), jnp.float32),
            jax.ShapeDtypeStruct((rank, receiver_geo.shape[1]), jnp.float32),
            jax.ShapeDtypeStruct((rank, action_geo.shape[1]), jnp.float32),
        ],
        compiler_params=pltpu.CompilerParams(dimension_semantics=("arbitrary",)),
    )(senders, receivers, actions, fill, counts, sender_geo, receiver_geo, action_geo)


def per_device(
    tile_counts,
    tile_sender,
    tile_receiver,
    tile_action,
    tile_fill,
    sender_log_shape,
    sender_log_rate,
    receiver_log_shape,
    receiver_log_rate,
    action_log_shape,
    action_log_rate,
):
    own_send_shape = sender_log_shape[0]
    own_send_rate = sender_log_rate[0]
    own_recv_shape = receiver_log_shape[0]
    own_recv_rate = receiver_log_rate[0]
    own_send_geo = geometric(own_send_shape, own_send_rate).astype(jnp.bfloat16)
    own_recv_geo = geometric(own_recv_shape, own_recv_rate).astype(jnp.bfloat16)
    n_snd = lax.psum(1, "snd")
    n_rcv = lax.psum(1, "rcv")
    sender_geo = gather_cols(own_send_geo, "rcv", n_rcv)
    receiver_geo = gather_cols(own_recv_geo, "snd", n_snd)
    action_geo = geometric(action_log_shape, action_log_rate)

    send_term, recv_term, act_term = tile_pass(
        tile_counts[0, 0],
        tile_sender[0, 0],
        tile_receiver[0, 0],
        tile_action[0, 0],
        tile_fill[0],
        sender_geo,
        receiver_geo,
        action_geo,
    )
    sender_part = jnp.sum(jnp.exp(own_send_shape - own_send_rate), axis=1)
    receiver_part = jnp.sum(jnp.exp(own_recv_shape - own_recv_rate), axis=1)
    n_act = act_term.shape[1]
    stacked = jnp.concatenate([act_term, sender_part[:, None], receiver_part[:, None]], axis=1)
    stacked = sum_all(stacked, (("snd", n_snd), ("rcv", n_rcv)))
    sender_stat, unused = scatter_cols(send_term, "rcv", n_rcv)
    receiver_stat, unused = scatter_cols(recv_term, "snd", n_snd)
    action_stat = stacked[:, :n_act]
    sender_total = stacked[:, n_act]
    receiver_total = stacked[:, n_act + 1]
    action_total = jnp.sum(jnp.exp(action_log_shape - action_log_rate), axis=1)
    new_send_shape = refresh(own_send_shape, prior_shape + sender_stat)
    new_send_rate = refresh(own_send_rate, (prior_rate + receiver_total * action_total)[:, None])
    new_recv_shape = refresh(own_recv_shape, prior_shape + receiver_stat)
    new_recv_rate = refresh(own_recv_rate, (prior_rate + sender_total * action_total)[:, None])
    new_act_shape = refresh(action_log_shape, prior_shape + action_stat)
    new_act_rate = refresh(action_log_rate, (prior_rate + sender_total * receiver_total)[:, None])
    return (
        new_send_shape[None],
        new_send_rate[None],
        new_recv_shape[None],
        new_recv_rate[None],
        new_act_shape,
        new_act_rate,
    )


def solution(mesh):
    return jax.shard_map(
        per_device,
        mesh=mesh,
        in_specs=(
            P("snd", "rcv", None, None, None),
            P("snd", "rcv", None),
            P("snd", "rcv", None),
            P("snd", "rcv", None),
            P("snd", "rcv"),
            P("snd", None, "rcv"),
            P("snd", None, "rcv"),
            P("rcv", None, "snd"),
            P("rcv", None, "snd"),
            P(),
            P(),
        ),
        out_specs=(
            P("snd", None, "rcv"),
            P("snd", None, "rcv"),
            P("rcv", None, "snd"),
            P("rcv", None, "snd"),
            P(),
            P(),
        ),
        check_vma=False,
    )
```

```python
import jax
import jax.numpy as jnp
from jax import lax
from jax.experimental import pallas as pl
from jax.experimental.pallas import tpu as pltpu
from jax.sharding import PartitionSpec as P

prior_shape = 0.3
prior_rate = 0.3
step_size = 0.5
tile_group = 8


def digamma_series(value):
    shift_sum = jnp.zeros_like(value)
    for offset in range(6):
        shift_sum = shift_sum + 1.0 / (value + float(offset))
    moved = value + 6.0
    inverse = 1.0 / moved
    inv_square = inverse * inverse
    series = (
        jnp.log(moved)
        - 0.5 * inverse
        - inv_square * (1.0 / 12.0 - inv_square * (1.0 / 120.0 - inv_square / 252.0))
    )
    return series - shift_sum


def geometric(log_shape, log_rate):
    return jnp.exp(digamma_series(jnp.exp(log_shape)) - log_rate)


def refresh(log_value, target):
    return jnp.log((1.0 - step_size) * jnp.exp(log_value) + step_size * target)


def is_pow2(n):
    return n > 0 and n & (n - 1) == 0


def swap(x, axis, n, dist):
    return lax.ppermute(x, axis, [(i, i ^ dist) for i in range(n)])


def gather_cols(x, axis, n):
    if not is_pow2(n):
        return lax.all_gather(x, axis, axis=1, tiled=True)
    me = lax.axis_index(axis)
    dist = 1
    while dist < n:
        theirs = swap(x, axis, n, dist)
        low = (me & dist) == 0
        x = jnp.where(low, jnp.concatenate([x, theirs], axis=1), jnp.concatenate([theirs, x], axis=1))
        dist *= 2
    return x


def sum_all(x, axes):
    for axis, n in axes:
        if not is_pow2(n):
            x = lax.psum(x, axis)
            continue
        dist = 1
        while dist < n:
            x = x + swap(x, axis, n, dist)
            dist *= 2
    return x


def scatter_cols(x, axis, n, extra=None):
    if not is_pow2(n):
        out = lax.psum_scatter(x, axis, scatter_dimension=1, tiled=True)
        return out, (None if extra is None else lax.psum(extra, axis))
    me = lax.axis_index(axis)
    dist = n // 2
    while dist >= 1:
        width = x.shape[1] // 2
        first, second = x[:, :width], x[:, width:]
        high = (me & dist) != 0
        keep = jnp.where(high, second, first)
        give = jnp.where(high, first, second)
        if extra is None:
            x = keep + swap(give, axis, n, dist)
        else:
            got, got_extra = swap((give, extra), axis, n, dist)
            x = keep + got
            extra = extra + got_extra
        dist //= 2
    return x, extra


def tile_kernel(snd_ref, rcv_ref, act_ref, fill_ref, counts_ref, sgeo_ref, rgeo_ref, ageo_ref,
                sacc_ref, racc_ref, aacc_ref):
    step = pl.program_id(0)
    group = counts_ref.shape[0]
    edge = counts_ref.shape[-1]
    n_sb = sgeo_ref.shape[1] // edge
    n_rb = rgeo_ref.shape[1] // edge
    n_act = ageo_ref.shape[1]

    @pl.when(step == 0)
    def _():
        sacc_ref[...] = jnp.zeros_like(sacc_ref)
        racc_ref[...] = jnp.zeros_like(racc_ref)
        aacc_ref[...] = jnp.zeros_like(aacc_ref)

    for slot in range(group):
        pl.when(step * group + slot < fill_ref[0])(
            lambda slot=slot: one_tile(step * group + slot, counts_ref.at[slot], snd_ref, rcv_ref,
                                       act_ref, sgeo_ref, rgeo_ref, ageo_ref, sacc_ref, racc_ref,
                                       aacc_ref, edge, n_sb, n_rb, n_act)
        )


def one_tile(t, tile_ref, snd_ref, rcv_ref, act_ref, sgeo_ref, rgeo_ref, ageo_ref, sacc_ref,
             racc_ref, aacc_ref, edge, n_sb, n_rb, n_act):
    b = jnp.clip(snd_ref[t], 0, n_sb - 1)
    c = jnp.clip(rcv_ref[t], 0, n_rb - 1)
    a = jnp.clip(act_ref[t], 0, n_act - 1)
    s0 = pl.multiple_of(b * edge, edge)
    r0 = pl.multiple_of(c * edge, edge)
    send_cols = sgeo_ref[:, pl.ds(s0, edge)]
    recv_cols = rgeo_ref[:, pl.ds(r0, edge)]
    ageo = ageo_ref[...]
    hit = lax.broadcasted_iota(jnp.int32, ageo.shape, 1) == a
    act_col = jnp.sum(jnp.where(hit, ageo, 0.0), axis=1, keepdims=True)
    scaled = (send_cols.astype(jnp.float32) * act_col).astype(jnp.bfloat16)
    expected = lax.dot_general(
        scaled, recv_cols, (((0,), (0,)), ((), ())), preferred_element_type=jnp.float32
    )
    ratios = (tile_ref[...].astype(jnp.float32) / expected).astype(jnp.bfloat16)
    toward_send = lax.dot_general(
        recv_cols, ratios, (((1,), (1,)), ((), ())), preferred_element_type=jnp.float32
    )
    toward_recv = jnp.dot(scaled, ratios, preferred_element_type=jnp.float32)
    send_part = scaled.astype(jnp.float32) * toward_send
    recv_part = recv_cols.astype(jnp.float32) * toward_recv
    act_part = jnp.sum(send_part, axis=1, keepdims=True)
    sacc_ref[:, pl.ds(s0, edge)] += send_part
    racc_ref[:, pl.ds(r0, edge)] += recv_part
    aacc_ref[...] += jnp.where(hit, act_part, 0.0)


def tile_pass(counts, senders, receivers, actions, fill, sender_geo, receiver_geo, action_geo):
    n_slots, edge = counts.shape[0], counts.shape[1]
    group = tile_group if n_slots % tile_group == 0 else 1
    rank = sender_geo.shape[0]
    full = lambda shape: pl.BlockSpec(shape, lambda t, *_: (0,) * len(shape))
    grid_spec = pltpu.PrefetchScalarGridSpec(
        num_scalar_prefetch=4,
        grid=(n_slots // group,),
        in_specs=[
            pl.BlockSpec(
                (group, edge, edge),
                lambda g, s, r, a, f: (jnp.minimum(g, jnp.maximum(f[0] - 1, 0) // group), 0, 0),
            ),
            full(sender_geo.shape),
            full(receiver_geo.shape),
            full(action_geo.shape),
        ],
        out_specs=[
            full((rank, sender_geo.shape[1])),
            full((rank, receiver_geo.shape[1])),
            full((rank, action_geo.shape[1])),
        ],
    )
    return pl.pallas_call(
        tile_kernel,
        grid_spec=grid_spec,
        out_shape=[
            jax.ShapeDtypeStruct((rank, sender_geo.shape[1]), jnp.float32),
            jax.ShapeDtypeStruct((rank, receiver_geo.shape[1]), jnp.float32),
            jax.ShapeDtypeStruct((rank, action_geo.shape[1]), jnp.float32),
        ],
        compiler_params=pltpu.CompilerParams(dimension_semantics=("arbitrary",)),
    )(senders, receivers, actions, fill, counts, sender_geo, receiver_geo, action_geo)


def per_device(
    tile_counts,
    tile_sender,
    tile_receiver,
    tile_action,
    tile_fill,
    sender_log_shape,
    sender_log_rate,
    receiver_log_shape,
    receiver_log_rate,
    action_log_shape,
    action_log_rate,
):
    own_send_shape = sender_log_shape[0]
    own_send_rate = sender_log_rate[0]
    own_recv_shape = receiver_log_shape[0]
    own_recv_rate = receiver_log_rate[0]
    own_send_geo = geometric(own_send_shape, own_send_rate).astype(jnp.bfloat16)
    own_recv_geo = geometric(own_recv_shape, own_recv_rate).astype(jnp.bfloat16)
    n_snd = lax.psum(1, "snd")
    n_rcv = lax.psum(1, "rcv")
    sender_geo = gather_cols(own_send_geo, "rcv", n_rcv)
    receiver_geo = gather_cols(own_recv_geo, "snd", n_snd)
    action_geo = geometric(action_log_shape, action_log_rate)

    send_term, recv_term, act_term = tile_pass(
        tile_counts[0, 0],
        tile_sender[0, 0],
        tile_receiver[0, 0],
        tile_action[0, 0],
        tile_fill[0],
        sender_geo,
        receiver_geo,
        action_geo,
    )
    sender_part = jnp.sum(jnp.exp(own_send_shape - own_send_rate), axis=1)
    receiver_part = jnp.sum(jnp.exp(own_recv_shape - own_recv_rate), axis=1)
    n_act = act_term.shape[1]
    stacked = jnp.concatenate([act_term, sender_part[:, None], receiver_part[:, None]], axis=1)
    half = stacked.shape[0] // 2
    stacked = jnp.concatenate(
        [
            sum_all(stacked[:half], (("snd", n_snd), ("rcv", n_rcv))),
            sum_all(stacked[half:], (("rcv", n_rcv), ("snd", n_snd))),
        ],
        axis=0,
    )
    sender_stat, unused = scatter_cols(send_term, "rcv", n_rcv)
    receiver_stat, unused = scatter_cols(recv_term, "snd", n_snd)
    action_stat = stacked[:, :n_act]
    sender_total = stacked[:, n_act]
    receiver_total = stacked[:, n_act + 1]
    action_total = jnp.sum(jnp.exp(action_log_shape - action_log_rate), axis=1)
    new_send_shape = refresh(own_send_shape, prior_shape + sender_stat)
    new_send_rate = refresh(own_send_rate, (prior_rate + receiver_total * action_total)[:, None])
    new_recv_shape = refresh(own_recv_shape, prior_shape + receiver_stat)
    new_recv_rate = refresh(own_recv_rate, (prior_rate + sender_total * action_total)[:, None])
    new_act_shape = refresh(action_log_shape, prior_shape + action_stat)
    new_act_rate = refresh(action_log_rate, (prior_rate + sender_total * receiver_total)[:, None])
    return (
        new_send_shape[None],
        new_send_rate[None],
        new_recv_shape[None],
        new_recv_rate[None],
        new_act_shape,
        new_act_rate,
    )


def solution(mesh):
    return jax.shard_map(
        per_device,
        mesh=mesh,
        in_specs=(
            P("snd", "rcv", None, None, None),
            P("snd", "rcv", None),
            P("snd", "rcv", None),
            P("snd", "rcv", None),
            P("snd", "rcv"),
            P("snd", None, "rcv"),
            P("snd", None, "rcv"),
            P("rcv", None, "snd"),
            P("rcv", None, "snd"),
            P(),
            P(),
        ),
        out_specs=(
            P("snd", None, "rcv"),
            P("snd", None, "rcv"),
            P("rcv", None, "snd"),
            P("rcv", None, "snd"),
            P(),
            P(),
        ),
        check_vma=False,
    )
```

```python
import jax
import jax.numpy as jnp
from jax import lax
from jax.experimental import pallas as pl
from jax.experimental.pallas import tpu as pltpu
from jax.sharding import PartitionSpec as P

prior_shape = 0.3
prior_rate = 0.3
step_size = 0.5
tile_group = 8


def digamma_series(value):
    shift_sum = jnp.zeros_like(value)
    for offset in range(6):
        shift_sum = shift_sum + 1.0 / (value + float(offset))
    moved = value + 6.0
    inverse = 1.0 / moved
    inv_square = inverse * inverse
    series = (
        jnp.log(moved)
        - 0.5 * inverse
        - inv_square * (1.0 / 12.0 - inv_square * (1.0 / 120.0 - inv_square / 252.0))
    )
    return series - shift_sum


def geometric(log_shape, log_rate):
    return jnp.exp(digamma_series(jnp.exp(log_shape)) - log_rate)


def refresh(log_value, target):
    return jnp.log((1.0 - step_size) * jnp.exp(log_value) + step_size * target)


def is_pow2(n):
    return n > 0 and n & (n - 1) == 0


def swap(x, axis, n, dist):
    return lax.ppermute(x, axis, [(i, i ^ dist) for i in range(n)])


def blocks_of(x, count):
    width = x.shape[1] // count
    return [x[:, i * width:(i + 1) * width] for i in range(count)]


def gather_cols(x, axis, n):
    if not is_pow2(n):
        return lax.all_gather(x, axis, axis=1, tiled=True)
    me = lax.axis_index(axis)
    count = 1
    dist = n // 2
    while dist >= 1:
        theirs = swap(x, axis, n, dist)
        low = (me & dist) == 0
        first = jnp.where(low, x, theirs)
        second = jnp.where(low, theirs, x)
        pairs = zip(blocks_of(first, count), blocks_of(second, count))
        x = jnp.concatenate([blk for pair in pairs for blk in pair], axis=1)
        count *= 2
        dist //= 2
    return x


def sum_all(x, axes):
    for axis, n in axes:
        if not is_pow2(n):
            x = lax.psum(x, axis)
            continue
        dist = 1
        while dist < n:
            x = x + swap(x, axis, n, dist)
            dist *= 2
    return x


def scatter_cols(x, axis, n):
    if not is_pow2(n):
        return lax.psum_scatter(x, axis, scatter_dimension=1, tiled=True)
    me = lax.axis_index(axis)
    count = n
    dist = 1
    while dist < n:
        parts = blocks_of(x, count)
        even = jnp.concatenate(parts[0::2], axis=1)
        odd = jnp.concatenate(parts[1::2], axis=1)
        high = (me & dist) != 0
        keep = jnp.where(high, odd, even)
        give = jnp.where(high, even, odd)
        x = keep + swap(give, axis, n, dist)
        count //= 2
        dist *= 2
    return x


def tile_kernel(snd_ref, rcv_ref, act_ref, fill_ref, counts_ref, sgeo_ref, rgeo_ref, ageo_ref,
                sacc_ref, racc_ref, aacc_ref):
    step = pl.program_id(0)
    group = counts_ref.shape[0]
    edge = counts_ref.shape[-1]
    n_sb = sgeo_ref.shape[1] // edge
    n_rb = rgeo_ref.shape[1] // edge
    n_act = ageo_ref.shape[1]

    @pl.when(step == 0)
    def _():
        sacc_ref[...] = jnp.zeros_like(sacc_ref)
        racc_ref[...] = jnp.zeros_like(racc_ref)
        aacc_ref[...] = jnp.zeros_like(aacc_ref)

    for slot in range(group):
        pl.when(step * group + slot < fill_ref[0])(
            lambda slot=slot: one_tile(step * group + slot, counts_ref.at[slot], snd_ref, rcv_ref,
                                       act_ref, sgeo_ref, rgeo_ref, ageo_ref, sacc_ref, racc_ref,
                                       aacc_ref, edge, n_sb, n_rb, n_act)
        )


def one_tile(t, tile_ref, snd_ref, rcv_ref, act_ref, sgeo_ref, rgeo_ref, ageo_ref, sacc_ref,
             racc_ref, aacc_ref, edge, n_sb, n_rb, n_act):
    b = jnp.clip(snd_ref[t], 0, n_sb - 1)
    c = jnp.clip(rcv_ref[t], 0, n_rb - 1)
    a = jnp.clip(act_ref[t], 0, n_act - 1)
    s0 = pl.multiple_of(b * edge, edge)
    r0 = pl.multiple_of(c * edge, edge)
    send_cols = sgeo_ref[:, pl.ds(s0, edge)]
    recv_cols = rgeo_ref[:, pl.ds(r0, edge)]
    ageo = ageo_ref[...]
    hit = lax.broadcasted_iota(jnp.int32, ageo.shape, 1) == a
    act_col = jnp.sum(jnp.where(hit, ageo, 0.0), axis=1, keepdims=True)
    scaled = (send_cols.astype(jnp.float32) * act_col).astype(jnp.bfloat16)
    expected = lax.dot_general(
        scaled, recv_cols, (((0,), (0,)), ((), ())), preferred_element_type=jnp.float32
    )
    ratios = (tile_ref[...].astype(jnp.float32) / expected).astype(jnp.bfloat16)
    toward_send = lax.dot_general(
        recv_cols, ratios, (((1,), (1,)), ((), ())), preferred_element_type=jnp.float32
    )
    toward_recv = jnp.dot(scaled, ratios, preferred_element_type=jnp.float32)
    send_part = scaled.astype(jnp.float32) * toward_send
    recv_part = recv_cols.astype(jnp.float32) * toward_recv
    act_part = jnp.sum(send_part, axis=1, keepdims=True)
    sacc_ref[:, pl.ds(s0, edge)] += send_part
    racc_ref[:, pl.ds(r0, edge)] += recv_part
    aacc_ref[...] += jnp.where(hit, act_part, 0.0)


def tile_pass(counts, senders, receivers, actions, fill, sender_geo, receiver_geo, action_geo):
    n_slots, edge = counts.shape[0], counts.shape[1]
    group = tile_group if n_slots % tile_group == 0 else 1
    rank = sender_geo.shape[0]
    full = lambda shape: pl.BlockSpec(shape, lambda t, *_: (0,) * len(shape))
    grid_spec = pltpu.PrefetchScalarGridSpec(
        num_scalar_prefetch=4,
        grid=(n_slots // group,),
        in_specs=[
            pl.BlockSpec(
                (group, edge, edge),
                lambda g, s, r, a, f: (jnp.minimum(g, jnp.maximum(f[0] - 1, 0) // group), 0, 0),
            ),
            full(sender_geo.shape),
            full(receiver_geo.shape),
            full(action_geo.shape),
        ],
        out_specs=[
            full((rank, sender_geo.shape[1])),
            full((rank, receiver_geo.shape[1])),
            full((rank, action_geo.shape[1])),
        ],
    )
    return pl.pallas_call(
        tile_kernel,
        grid_spec=grid_spec,
        out_shape=[
            jax.ShapeDtypeStruct((rank, sender_geo.shape[1]), jnp.float32),
            jax.ShapeDtypeStruct((rank, receiver_geo.shape[1]), jnp.float32),
            jax.ShapeDtypeStruct((rank, action_geo.shape[1]), jnp.float32),
        ],
        compiler_params=pltpu.CompilerParams(dimension_semantics=("arbitrary",)),
    )(senders, receivers, actions, fill, counts, sender_geo, receiver_geo, action_geo)


def per_device(
    tile_counts,
    tile_sender,
    tile_receiver,
    tile_action,
    tile_fill,
    sender_log_shape,
    sender_log_rate,
    receiver_log_shape,
    receiver_log_rate,
    action_log_shape,
    action_log_rate,
):
    own_send_shape = sender_log_shape[0]
    own_send_rate = sender_log_rate[0]
    own_recv_shape = receiver_log_shape[0]
    own_recv_rate = receiver_log_rate[0]
    own_send_geo = geometric(own_send_shape, own_send_rate).astype(jnp.bfloat16)
    own_recv_geo = geometric(own_recv_shape, own_recv_rate).astype(jnp.bfloat16)
    n_snd = lax.psum(1, "snd")
    n_rcv = lax.psum(1, "rcv")
    sender_geo = gather_cols(own_send_geo, "rcv", n_rcv)
    receiver_geo = gather_cols(own_recv_geo, "snd", n_snd)
    action_geo = geometric(action_log_shape, action_log_rate)

    send_term, recv_term, act_term = tile_pass(
        tile_counts[0, 0],
        tile_sender[0, 0],
        tile_receiver[0, 0],
        tile_action[0, 0],
        tile_fill[0],
        sender_geo,
        receiver_geo,
        action_geo,
    )
    sender_part = jnp.sum(jnp.exp(own_send_shape - own_send_rate), axis=1)
    receiver_part = jnp.sum(jnp.exp(own_recv_shape - own_recv_rate), axis=1)
    n_act = act_term.shape[1]
    stacked = jnp.concatenate([act_term, sender_part[:, None], receiver_part[:, None]], axis=1)
    stacked = sum_all(stacked, (("snd", n_snd), ("rcv", n_rcv)))
    sender_stat = scatter_cols(send_term, "rcv", n_rcv)
    receiver_stat = scatter_cols(recv_term, "snd", n_snd)
    action_stat = stacked[:, :n_act]
    sender_total = stacked[:, n_act]
    receiver_total = stacked[:, n_act + 1]
    action_total = jnp.sum(jnp.exp(action_log_shape - action_log_rate), axis=1)
    new_send_shape = refresh(own_send_shape, prior_shape + sender_stat)
    new_send_rate = refresh(own_send_rate, (prior_rate + receiver_total * action_total)[:, None])
    new_recv_shape = refresh(own_recv_shape, prior_shape + receiver_stat)
    new_recv_rate = refresh(own_recv_rate, (prior_rate + sender_total * action_total)[:, None])
    new_act_shape = refresh(action_log_shape, prior_shape + action_stat)
    new_act_rate = refresh(action_log_rate, (prior_rate + sender_total * receiver_total)[:, None])
    return (
        new_send_shape[None],
        new_send_rate[None],
        new_recv_shape[None],
        new_recv_rate[None],
        new_act_shape,
        new_act_rate,
    )


def solution(mesh):
    return jax.shard_map(
        per_device,
        mesh=mesh,
        in_specs=(
            P("snd", "rcv", None, None, None),
            P("snd", "rcv", None),
            P("snd", "rcv", None),
            P("snd", "rcv", None),
            P("snd", "rcv"),
            P("snd", None, "rcv"),
            P("snd", None, "rcv"),
            P("rcv", None, "snd"),
            P("rcv", None, "snd"),
            P(),
            P(),
        ),
        out_specs=(
            P("snd", None, "rcv"),
            P("snd", None, "rcv"),
            P("rcv", None, "snd"),
            P("rcv", None, "snd"),
            P(),
            P(),
        ),
        check_vma=False,
    )
```

```python
import jax
import jax.numpy as jnp
from jax import lax
from jax.experimental import pallas as pl
from jax.experimental.pallas import tpu as pltpu
from jax.sharding import PartitionSpec as P

prior_shape = 0.3
prior_rate = 0.3
step_size = 0.5
tile_group = 8


def digamma_series(value):
    shift_sum = jnp.zeros_like(value)
    for offset in range(6):
        shift_sum = shift_sum + 1.0 / (value + float(offset))
    moved = value + 6.0
    inverse = 1.0 / moved
    inv_square = inverse * inverse
    series = (
        jnp.log(moved)
        - 0.5 * inverse
        - inv_square * (1.0 / 12.0 - inv_square * (1.0 / 120.0 - inv_square / 252.0))
    )
    return series - shift_sum


def geometric(log_shape, log_rate):
    return jnp.exp(digamma_series(jnp.exp(log_shape)) - log_rate)


def refresh(log_value, target):
    return jnp.log((1.0 - step_size) * jnp.exp(log_value) + step_size * target)


def is_pow2(n):
    return n > 0 and n & (n - 1) == 0


def swap(x, axis, n, dist):
    return lax.ppermute(x, axis, [(i, i ^ dist) for i in range(n)])


def blocks_of(x, count):
    width = x.shape[1] // count
    return [x[:, i * width:(i + 1) * width] for i in range(count)]


def gather_cols(x, axis, n):
    if not is_pow2(n):
        return lax.all_gather(x, axis, axis=1, tiled=True)
    me = lax.axis_index(axis)
    count = 1
    dist = n // 2
    while dist >= 1:
        theirs = swap(x, axis, n, dist)
        low = (me & dist) == 0
        first = jnp.where(low, x, theirs)
        second = jnp.where(low, theirs, x)
        pairs = zip(blocks_of(first, count), blocks_of(second, count))
        x = jnp.concatenate([blk for pair in pairs for blk in pair], axis=1)
        count *= 2
        dist //= 2
    return x


def sum_all(x, axes):
    for axis, n in axes:
        if not is_pow2(n):
            x = lax.psum(x, axis)
            continue
        dist = 1
        while dist < n:
            x = x + swap(x, axis, n, dist)
            dist *= 2
    return x


def scatter_cols(x, axis, n, extra):
    if not is_pow2(n):
        return lax.psum_scatter(x, axis, scatter_dimension=1, tiled=True), lax.psum(extra, axis)
    me = lax.axis_index(axis)
    count = n
    dist = 1
    while dist < n:
        parts = blocks_of(x, count)
        even = jnp.concatenate(parts[0::2], axis=1)
        odd = jnp.concatenate(parts[1::2], axis=1)
        high = (me & dist) != 0
        keep = jnp.where(high, odd, even)
        give = jnp.where(high, even, odd)
        got = swap(jnp.concatenate([give, extra], axis=1), axis, n, dist)
        x = keep + got[:, :keep.shape[1]]
        extra = extra + got[:, keep.shape[1]:]
        count //= 2
        dist *= 2
    return x, extra


def tile_kernel(snd_ref, rcv_ref, act_ref, fill_ref, counts_ref, sgeo_ref, rgeo_ref, ageo_ref,
                sacc_ref, racc_ref, aacc_ref):
    step = pl.program_id(0)
    group = counts_ref.shape[0]
    edge = counts_ref.shape[-1]
    n_sb = sgeo_ref.shape[1] // edge
    n_rb = rgeo_ref.shape[1] // edge
    n_act = ageo_ref.shape[1]

    @pl.when(step == 0)
    def _():
        sacc_ref[...] = jnp.zeros_like(sacc_ref)
        racc_ref[...] = jnp.zeros_like(racc_ref)
        aacc_ref[...] = jnp.zeros_like(aacc_ref)

    for slot in range(group):
        pl.when(step * group + slot < fill_ref[0])(
            lambda slot=slot: one_tile(step * group + slot, counts_ref.at[slot], snd_ref, rcv_ref,
                                       act_ref, sgeo_ref, rgeo_ref, ageo_ref, sacc_ref, racc_ref,
                                       aacc_ref, edge, n_sb, n_rb, n_act)
        )


def one_tile(t, tile_ref, snd_ref, rcv_ref, act_ref, sgeo_ref, rgeo_ref, ageo_ref, sacc_ref,
             racc_ref, aacc_ref, edge, n_sb, n_rb, n_act):
    b = jnp.clip(snd_ref[t], 0, n_sb - 1)
    c = jnp.clip(rcv_ref[t], 0, n_rb - 1)
    a = jnp.clip(act_ref[t], 0, n_act - 1)
    s0 = pl.multiple_of(b * edge, edge)
    r0 = pl.multiple_of(c * edge, edge)
    send_cols = sgeo_ref[:, pl.ds(s0, edge)]
    recv_cols = rgeo_ref[:, pl.ds(r0, edge)]
    ageo = ageo_ref[...]
    hit = lax.broadcasted_iota(jnp.int32, ageo.shape, 1) == a
    act_col = jnp.sum(jnp.where(hit, ageo, 0.0), axis=1, keepdims=True)
    scaled = (send_cols.astype(jnp.float32) * act_col).astype(jnp.bfloat16)
    expected = lax.dot_general(
        scaled, recv_cols, (((0,), (0,)), ((), ())), preferred_element_type=jnp.float32
    )
    ratios = (tile_ref[...].astype(jnp.float32) / expected).astype(jnp.bfloat16)
    toward_send = lax.dot_general(
        recv_cols, ratios, (((1,), (1,)), ((), ())), preferred_element_type=jnp.float32
    )
    toward_recv = jnp.dot(scaled, ratios, preferred_element_type=jnp.float32)
    send_part = scaled.astype(jnp.float32) * toward_send
    recv_part = recv_cols.astype(jnp.float32) * toward_recv
    act_part = jnp.sum(send_part, axis=1, keepdims=True)
    sacc_ref[:, pl.ds(s0, edge)] += send_part
    racc_ref[:, pl.ds(r0, edge)] += recv_part
    aacc_ref[...] += jnp.where(hit, act_part, 0.0)


def tile_pass(counts, senders, receivers, actions, fill, sender_geo, receiver_geo, action_geo):
    n_slots, edge = counts.shape[0], counts.shape[1]
    group = tile_group if n_slots % tile_group == 0 else 1
    rank = sender_geo.shape[0]
    full = lambda shape: pl.BlockSpec(shape, lambda t, *_: (0,) * len(shape))
    grid_spec = pltpu.PrefetchScalarGridSpec(
        num_scalar_prefetch=4,
        grid=(n_slots // group,),
        in_specs=[
            pl.BlockSpec(
                (group, edge, edge),
                lambda g, s, r, a, f: (jnp.minimum(g, jnp.maximum(f[0] - 1, 0) // group), 0, 0),
            ),
            full(sender_geo.shape),
            full(receiver_geo.shape),
            full(action_geo.shape),
        ],
        out_specs=[
            full((rank, sender_geo.shape[1])),
            full((rank, receiver_geo.shape[1])),
            full((rank, action_geo.shape[1])),
        ],
    )
    return pl.pallas_call(
        tile_kernel,
        grid_spec=grid_spec,
        out_shape=[
            jax.ShapeDtypeStruct((rank, sender_geo.shape[1]), jnp.float32),
            jax.ShapeDtypeStruct((rank, receiver_geo.shape[1]), jnp.float32),
            jax.ShapeDtypeStruct((rank, action_geo.shape[1]), jnp.float32),
        ],
        compiler_params=pltpu.CompilerParams(dimension_semantics=("arbitrary",)),
    )(senders, receivers, actions, fill, counts, sender_geo, receiver_geo, action_geo)


def per_device(
    tile_counts,
    tile_sender,
    tile_receiver,
    tile_action,
    tile_fill,
    sender_log_shape,
    sender_log_rate,
    receiver_log_shape,
    receiver_log_rate,
    action_log_shape,
    action_log_rate,
):
    own_send_shape = sender_log_shape[0]
    own_send_rate = sender_log_rate[0]
    own_recv_shape = receiver_log_shape[0]
    own_recv_rate = receiver_log_rate[0]
    own_send_geo = geometric(own_send_shape, own_send_rate).astype(jnp.bfloat16)
    own_recv_geo = geometric(own_recv_shape, own_recv_rate).astype(jnp.bfloat16)
    n_snd = lax.psum(1, "snd")
    n_rcv = lax.psum(1, "rcv")
    sender_geo = gather_cols(own_send_geo, "rcv", n_rcv)
    receiver_geo = gather_cols(own_recv_geo, "snd", n_snd)
    action_geo = geometric(action_log_shape, action_log_rate)

    send_term, recv_term, act_term = tile_pass(
        tile_counts[0, 0],
        tile_sender[0, 0],
        tile_receiver[0, 0],
        tile_action[0, 0],
        tile_fill[0],
        sender_geo,
        receiver_geo,
        action_geo,
    )
    sender_part = jnp.sum(jnp.exp(own_send_shape - own_send_rate), axis=1)
    receiver_part = jnp.sum(jnp.exp(own_recv_shape - own_recv_rate), axis=1)
    n_act = act_term.shape[1]
    pad = -(n_act + 2) % 128
    stacked = jnp.concatenate(
        [act_term, sender_part[:, None], receiver_part[:, None], jnp.zeros((act_term.shape[0], pad), jnp.float32)],
        axis=1,
    )
    receiver_stat, stacked = scatter_cols(recv_term, "snd", n_snd, stacked)
    sender_stat, stacked = scatter_cols(send_term, "rcv", n_rcv, stacked)
    action_stat = stacked[:, :n_act]
    sender_total = stacked[:, n_act]
    receiver_total = stacked[:, n_act + 1]
    action_total = jnp.sum(jnp.exp(action_log_shape - action_log_rate), axis=1)
    new_send_shape = refresh(own_send_shape, prior_shape + sender_stat)
    new_send_rate = refresh(own_send_rate, (prior_rate + receiver_total * action_total)[:, None])
    new_recv_shape = refresh(own_recv_shape, prior_shape + receiver_stat)
    new_recv_rate = refresh(own_recv_rate, (prior_rate + sender_total * action_total)[:, None])
    new_act_shape = refresh(action_log_shape, prior_shape + action_stat)
    new_act_rate = refresh(action_log_rate, (prior_rate + sender_total * receiver_total)[:, None])
    return (
        new_send_shape[None],
        new_send_rate[None],
        new_recv_shape[None],
        new_recv_rate[None],
        new_act_shape,
        new_act_rate,
    )


def solution(mesh):
    return jax.shard_map(
        per_device,
        mesh=mesh,
        in_specs=(
            P("snd", "rcv", None, None, None),
            P("snd", "rcv", None),
            P("snd", "rcv", None),
            P("snd", "rcv", None),
            P("snd", "rcv"),
            P("snd", None, "rcv"),
            P("snd", None, "rcv"),
            P("rcv", None, "snd"),
            P("rcv", None, "snd"),
            P(),
            P(),
        ),
        out_specs=(
            P("snd", None, "rcv"),
            P("snd", None, "rcv"),
            P("rcv", None, "snd"),
            P("rcv", None, "snd"),
            P(),
            P(),
        ),
        check_vma=False,
    )
```

```python
import jax
import jax.numpy as jnp
from jax import lax
from jax.experimental import pallas as pl
from jax.experimental.pallas import tpu as pltpu
from jax.sharding import PartitionSpec as P

prior_shape = 0.3
prior_rate = 0.3
step_size = 0.5
tile_group = 8


def digamma_series(value):
    shift_sum = jnp.zeros_like(value)
    for offset in range(6):
        shift_sum = shift_sum + 1.0 / (value + float(offset))
    moved = value + 6.0
    inverse = 1.0 / moved
    inv_square = inverse * inverse
    series = (
        jnp.log(moved)
        - 0.5 * inverse
        - inv_square * (1.0 / 12.0 - inv_square * (1.0 / 120.0 - inv_square / 252.0))
    )
    return series - shift_sum


def geometric(log_shape, log_rate):
    return jnp.exp(digamma_series(jnp.exp(log_shape)) - log_rate)


def refresh(log_value, target):
    return jnp.log((1.0 - step_size) * jnp.exp(log_value) + step_size * target)


def is_pow2(n):
    return n > 0 and n & (n - 1) == 0


def swap(x, axis, n, dist):
    return lax.ppermute(x, axis, [(i, i ^ dist) for i in range(n)])


def blocks_of(x, count):
    width = x.shape[1] // count
    return [x[:, i * width:(i + 1) * width] for i in range(count)]


def gather_cols(x, axis, n):
    if not is_pow2(n):
        return lax.all_gather(x, axis, axis=1, tiled=True)
    me = lax.axis_index(axis)
    count = 1
    dist = n // 2
    while dist >= 1:
        theirs = swap(x, axis, n, dist)
        low = (me & dist) == 0
        first = jnp.where(low, x, theirs)
        second = jnp.where(low, theirs, x)
        pairs = zip(blocks_of(first, count), blocks_of(second, count))
        x = jnp.concatenate([blk for pair in pairs for blk in pair], axis=1)
        count *= 2
        dist //= 2
    return x


def sum_all(x, axes):
    for axis, n in axes:
        if not is_pow2(n):
            x = lax.psum(x, axis)
            continue
        dist = 1
        while dist < n:
            x = x + swap(x, axis, n, dist)
            dist *= 2
    return x


def scatter_cols(x, axis, n):
    if not is_pow2(n):
        return lax.psum_scatter(x, axis, scatter_dimension=1, tiled=True)
    me = lax.axis_index(axis)
    count = n
    dist = 1
    while dist < n:
        parts = blocks_of(x, count)
        even = jnp.concatenate(parts[0::2], axis=1)
        odd = jnp.concatenate(parts[1::2], axis=1)
        high = (me & dist) != 0
        keep = jnp.where(high, odd, even)
        give = jnp.where(high, even, odd)
        x = keep + swap(give, axis, n, dist)
        count //= 2
        dist *= 2
    return x


def tile_kernel(snd_ref, rcv_ref, act_ref, fill_ref, counts_ref, scaled_ref, scaled_t_ref,
                rgeo_ref, sacc_ref, racc_ref, aacc_ref):
    step = pl.program_id(0)
    group = counts_ref.shape[0]
    edge = counts_ref.shape[-1]
    n_sb = sacc_ref.shape[1] // edge
    n_rb = rgeo_ref.shape[1] // edge
    n_act = aacc_ref.shape[1]

    @pl.when(step == 0)
    def _():
        sacc_ref[...] = jnp.zeros_like(sacc_ref)
        racc_ref[...] = jnp.zeros_like(racc_ref)
        aacc_ref[...] = jnp.zeros_like(aacc_ref)

    for slot in range(group):
        pl.when(step * group + slot < fill_ref[0])(
            lambda slot=slot: one_tile(step * group + slot, slot, counts_ref, scaled_ref, scaled_t_ref,
                                       snd_ref, rcv_ref, act_ref, rgeo_ref, sacc_ref, racc_ref,
                                       aacc_ref, edge, n_sb, n_rb, n_act)
        )


def one_tile(t, slot, counts_ref, scaled_ref, scaled_t_ref, snd_ref, rcv_ref, act_ref, rgeo_ref,
             sacc_ref, racc_ref, aacc_ref, edge, n_sb, n_rb, n_act):
    b = jnp.clip(snd_ref[t], 0, n_sb - 1)
    c = jnp.clip(rcv_ref[t], 0, n_rb - 1)
    a = jnp.clip(act_ref[t], 0, n_act - 1)
    s0 = pl.multiple_of(b * edge, edge)
    r0 = pl.multiple_of(c * edge, edge)
    recv_cols = rgeo_ref[:, pl.ds(r0, edge)]
    scaled = scaled_ref[slot]
    expected = jnp.dot(scaled_t_ref[slot], recv_cols, preferred_element_type=jnp.float32)
    ratios = (counts_ref[slot].astype(jnp.float32) / expected).astype(jnp.bfloat16)
    toward_send = lax.dot_general(
        recv_cols, ratios, (((1,), (1,)), ((), ())), preferred_element_type=jnp.float32
    )
    toward_recv = jnp.dot(scaled, ratios, preferred_element_type=jnp.float32)
    send_part = scaled.astype(jnp.float32) * toward_send
    recv_part = recv_cols.astype(jnp.float32) * toward_recv
    act_part = jnp.sum(send_part, axis=1, keepdims=True)
    sacc_ref[:, pl.ds(s0, edge)] += send_part
    racc_ref[:, pl.ds(r0, edge)] += recv_part
    hit = lax.broadcasted_iota(jnp.int32, aacc_ref.shape, 1) == a
    aacc_ref[...] += jnp.where(hit, act_part, 0.0)


def tile_pass(counts, senders, receivers, actions, fill, sender_geo, receiver_geo, action_geo):
    n_slots, edge = counts.shape[0], counts.shape[1]
    group = tile_group if n_slots % tile_group == 0 else 1
    rank, n_act = action_geo.shape
    n_sb = sender_geo.shape[1] // edge
    send_blocks = jnp.take(sender_geo.reshape(rank, n_sb, edge), senders, axis=1, mode="clip")
    weights = jnp.take(action_geo, actions, axis=1, mode="clip")
    scaled = (send_blocks.astype(jnp.float32) * weights[:, :, None]).astype(jnp.bfloat16)
    scaled_all = jnp.transpose(scaled, (1, 0, 2))
    scaled_t_all = jnp.transpose(scaled, (1, 2, 0))
    full = lambda shape: pl.BlockSpec(shape, lambda t, *_: (0,) * len(shape))
    slot_block = lambda g, s, r, a, f: (jnp.minimum(g, jnp.maximum(f[0] - 1, 0) // group), 0, 0)
    out_shapes = [
        (rank, sender_geo.shape[1]),
        (rank, receiver_geo.shape[1]),
        (rank, n_act),
    ]
    grid_spec = pltpu.PrefetchScalarGridSpec(
        num_scalar_prefetch=4,
        grid=(n_slots // group,),
        in_specs=[
            pl.BlockSpec((group, edge, edge), slot_block),
            pl.BlockSpec((group, rank, edge), slot_block),
            pl.BlockSpec((group, edge, rank), slot_block),
            full(receiver_geo.shape),
        ],
        out_specs=[full(shape) for shape in out_shapes],
    )
    return pl.pallas_call(
        tile_kernel,
        grid_spec=grid_spec,
        out_shape=[jax.ShapeDtypeStruct(shape, jnp.float32) for shape in out_shapes],
        compiler_params=pltpu.CompilerParams(dimension_semantics=("arbitrary",)),
    )(senders, receivers, actions, fill, counts, scaled_all, scaled_t_all, receiver_geo)


def per_device(
    tile_counts,
    tile_sender,
    tile_receiver,
    tile_action,
    tile_fill,
    sender_log_shape,
    sender_log_rate,
    receiver_log_shape,
    receiver_log_rate,
    action_log_shape,
    action_log_rate,
):
    own_send_shape = sender_log_shape[0]
    own_send_rate = sender_log_rate[0]
    own_recv_shape = receiver_log_shape[0]
    own_recv_rate = receiver_log_rate[0]
    own_send_geo = geometric(own_send_shape, own_send_rate).astype(jnp.bfloat16)
    own_recv_geo = geometric(own_recv_shape, own_recv_rate).astype(jnp.bfloat16)
    n_snd = lax.psum(1, "snd")
    n_rcv = lax.psum(1, "rcv")
    sender_geo = gather_cols(own_send_geo, "rcv", n_rcv)
    receiver_geo = gather_cols(own_recv_geo, "snd", n_snd)
    action_geo = geometric(action_log_shape, action_log_rate)

    send_term, recv_term, act_term = tile_pass(
        tile_counts[0, 0],
        tile_sender[0, 0],
        tile_receiver[0, 0],
        tile_action[0, 0],
        tile_fill[0],
        sender_geo,
        receiver_geo,
        action_geo,
    )
    sender_part = jnp.sum(jnp.exp(own_send_shape - own_send_rate), axis=1)
    receiver_part = jnp.sum(jnp.exp(own_recv_shape - own_recv_rate), axis=1)
    n_act = act_term.shape[1]
    stacked = jnp.concatenate([act_term, sender_part[:, None], receiver_part[:, None]], axis=1)
    stacked = sum_all(stacked, (("snd", n_snd), ("rcv", n_rcv)))
    sender_stat = scatter_cols(send_term, "rcv", n_rcv)
    receiver_stat = scatter_cols(recv_term, "snd", n_snd)
    action_stat = stacked[:, :n_act]
    sender_total = stacked[:, n_act]
    receiver_total = stacked[:, n_act + 1]
    action_total = jnp.sum(jnp.exp(action_log_shape - action_log_rate), axis=1)
    new_send_shape = refresh(own_send_shape, prior_shape + sender_stat)
    new_send_rate = refresh(own_send_rate, (prior_rate + receiver_total * action_total)[:, None])
    new_recv_shape = refresh(own_recv_shape, prior_shape + receiver_stat)
    new_recv_rate = refresh(own_recv_rate, (prior_rate + sender_total * action_total)[:, None])
    new_act_shape = refresh(action_log_shape, prior_shape + action_stat)
    new_act_rate = refresh(action_log_rate, (prior_rate + sender_total * receiver_total)[:, None])
    return (
        new_send_shape[None],
        new_send_rate[None],
        new_recv_shape[None],
        new_recv_rate[None],
        new_act_shape,
        new_act_rate,
    )


def solution(mesh):
    return jax.shard_map(
        per_device,
        mesh=mesh,
        in_specs=(
            P("snd", "rcv", None, None, None),
            P("snd", "rcv", None),
            P("snd", "rcv", None),
            P("snd", "rcv", None),
            P("snd", "rcv"),
            P("snd", None, "rcv"),
            P("snd", None, "rcv"),
            P("rcv", None, "snd"),
            P("rcv", None, "snd"),
            P(),
            P(),
        ),
        out_specs=(
            P("snd", None, "rcv"),
            P("snd", None, "rcv"),
            P("rcv", None, "snd"),
            P("rcv", None, "snd"),
            P(),
            P(),
        ),
        check_vma=False,
    )
```

```python
import jax
import jax.numpy as jnp
from jax import lax
from jax.experimental import pallas as pl
from jax.experimental.pallas import tpu as pltpu
from jax.sharding import PartitionSpec as P

prior_shape = 0.3
prior_rate = 0.3
step_size = 0.5
tile_group = 8


def digamma_series(value):
    shift_sum = jnp.zeros_like(value)
    for offset in range(6):
        shift_sum = shift_sum + 1.0 / (value + float(offset))
    moved = value + 6.0
    inverse = 1.0 / moved
    inv_square = inverse * inverse
    series = (
        jnp.log(moved)
        - 0.5 * inverse
        - inv_square * (1.0 / 12.0 - inv_square * (1.0 / 120.0 - inv_square / 252.0))
    )
    return series - shift_sum


def geometric(log_shape, log_rate):
    return jnp.exp(digamma_series(jnp.exp(log_shape)) - log_rate)


def refresh(log_value, target):
    return jnp.log((1.0 - step_size) * jnp.exp(log_value) + step_size * target)


def is_pow2(n):
    return n > 0 and n & (n - 1) == 0


def swap(x, axis, n, dist):
    return lax.ppermute(x, axis, [(i, i ^ dist) for i in range(n)])


def blocks_of(x, count):
    width = x.shape[1] // count
    return [x[:, i * width:(i + 1) * width] for i in range(count)]


def gather_cols(x, axis, n):
    if not is_pow2(n):
        return lax.all_gather(x, axis, axis=1, tiled=True)
    me = lax.axis_index(axis)
    count = 1
    dist = n // 2
    while dist >= 1:
        theirs = swap(x, axis, n, dist)
        low = (me & dist) == 0
        first = jnp.where(low, x, theirs)
        second = jnp.where(low, theirs, x)
        pairs = zip(blocks_of(first, count), blocks_of(second, count))
        x = jnp.concatenate([blk for pair in pairs for blk in pair], axis=1)
        count *= 2
        dist //= 2
    return x


def sum_all(x, axes):
    for axis, n in axes:
        if not is_pow2(n):
            x = lax.psum(x, axis)
            continue
        dist = 1
        while dist < n:
            x = x + swap(x, axis, n, dist)
            dist *= 2
    return x


def scatter_cols(x, axis, n):
    if not is_pow2(n):
        return lax.psum_scatter(x, axis, scatter_dimension=1, tiled=True)
    me = lax.axis_index(axis)
    count = n
    dist = 1
    while dist < n:
        parts = blocks_of(x, count)
        even = jnp.concatenate(parts[0::2], axis=1)
        odd = jnp.concatenate(parts[1::2], axis=1)
        high = (me & dist) != 0
        keep = jnp.where(high, odd, even)
        give = jnp.where(high, even, odd)
        x = keep + swap(give, axis, n, dist)
        count //= 2
        dist *= 2
    return x


def tile_kernel(snd_ref, rcv_ref, act_ref, fill_ref, counts_ref, scaled_ref, scaled_t_ref,
                rgeo_ref, sacc_ref, racc_ref, aacc_ref):
    step = pl.program_id(0)
    group = counts_ref.shape[0]
    edge = counts_ref.shape[-1]
    n_sb = sacc_ref.shape[1] // edge
    n_rb = rgeo_ref.shape[1] // edge
    n_act = aacc_ref.shape[1]

    @pl.when(step == 0)
    def _():
        sacc_ref[...] = jnp.zeros_like(sacc_ref)
        racc_ref[...] = jnp.zeros_like(racc_ref)
        aacc_ref[...] = jnp.zeros_like(aacc_ref)

    for slot in range(group):
        pl.when(step * group + slot < fill_ref[0])(
            lambda slot=slot: one_tile(step * group + slot, slot, counts_ref, scaled_ref, scaled_t_ref,
                                       snd_ref, rcv_ref, act_ref, rgeo_ref, sacc_ref, racc_ref,
                                       aacc_ref, edge, n_sb, n_rb, n_act)
        )


def one_tile(t, slot, counts_ref, scaled_ref, scaled_t_ref, snd_ref, rcv_ref, act_ref, rgeo_ref,
             sacc_ref, racc_ref, aacc_ref, edge, n_sb, n_rb, n_act):
    b = jnp.clip(snd_ref[t], 0, n_sb - 1)
    c = jnp.clip(rcv_ref[t], 0, n_rb - 1)
    a = jnp.clip(act_ref[t], 0, n_act - 1)
    s0 = pl.multiple_of(b * edge, edge)
    r0 = pl.multiple_of(c * edge, edge)
    recv_cols = rgeo_ref[:, pl.ds(r0, edge)]
    scaled = scaled_ref[slot]
    expected = jnp.dot(scaled_t_ref[slot], recv_cols, preferred_element_type=jnp.float32)
    ratios = (counts_ref[slot].astype(jnp.float32) / expected).astype(jnp.bfloat16)
    toward_send = lax.dot_general(
        recv_cols, ratios, (((1,), (1,)), ((), ())), preferred_element_type=jnp.float32
    )
    toward_recv = jnp.dot(scaled, ratios, preferred_element_type=jnp.float32)
    send_part = scaled.astype(jnp.float32) * toward_send
    recv_part = recv_cols.astype(jnp.float32) * toward_recv
    act_part = jnp.sum(send_part, axis=1, keepdims=True)
    sacc_ref[:, pl.ds(s0, edge)] += send_part
    racc_ref[:, pl.ds(r0, edge)] += recv_part
    hit = lax.broadcasted_iota(jnp.int32, aacc_ref.shape, 1) == a
    aacc_ref[...] += jnp.where(hit, act_part, 0.0)


def tile_pass(counts, senders, receivers, actions, fill, sender_geo, receiver_geo, action_geo):
    n_slots, edge = counts.shape[0], counts.shape[1]
    group = tile_group if n_slots % tile_group == 0 else 1
    rank, n_act = action_geo.shape
    n_sb = sender_geo.shape[1] // edge
    send_blocks = sender_geo.reshape(rank, n_sb, edge).transpose(1, 0, 2)
    send_blocks_t = sender_geo.T.reshape(n_sb, edge, rank)
    weights = jnp.take(action_geo.T, actions, axis=0, mode="clip")
    picked = jnp.take(send_blocks, senders, axis=0, mode="clip").astype(jnp.float32)
    picked_t = jnp.take(send_blocks_t, senders, axis=0, mode="clip").astype(jnp.float32)
    scaled_all = (picked * weights[:, :, None]).astype(jnp.bfloat16)
    scaled_t_all = (picked_t * weights[:, None, :]).astype(jnp.bfloat16)
    full = lambda shape: pl.BlockSpec(shape, lambda t, *_: (0,) * len(shape))
    slot_block = lambda g, s, r, a, f: (jnp.minimum(g, jnp.maximum(f[0] - 1, 0) // group), 0, 0)
    out_shapes = [
        (rank, sender_geo.shape[1]),
        (rank, receiver_geo.shape[1]),
        (rank, n_act),
    ]
    grid_spec = pltpu.PrefetchScalarGridSpec(
        num_scalar_prefetch=4,
        grid=(n_slots // group,),
        in_specs=[
            pl.BlockSpec((group, edge, edge), slot_block),
            pl.BlockSpec((group, rank, edge), slot_block),
            pl.BlockSpec((group, edge, rank), slot_block),
            full(receiver_geo.shape),
        ],
        out_specs=[full(shape) for shape in out_shapes],
    )
    return pl.pallas_call(
        tile_kernel,
        grid_spec=grid_spec,
        out_shape=[jax.ShapeDtypeStruct(shape, jnp.float32) for shape in out_shapes],
        compiler_params=pltpu.CompilerParams(dimension_semantics=("arbitrary",)),
    )(senders, receivers, actions, fill, counts, scaled_all, scaled_t_all, receiver_geo)


def per_device(
    tile_counts,
    tile_sender,
    tile_receiver,
    tile_action,
    tile_fill,
    sender_log_shape,
    sender_log_rate,
    receiver_log_shape,
    receiver_log_rate,
    action_log_shape,
    action_log_rate,
):
    own_send_shape = sender_log_shape[0]
    own_send_rate = sender_log_rate[0]
    own_recv_shape = receiver_log_shape[0]
    own_recv_rate = receiver_log_rate[0]
    own_send_geo = geometric(own_send_shape, own_send_rate).astype(jnp.bfloat16)
    own_recv_geo = geometric(own_recv_shape, own_recv_rate).astype(jnp.bfloat16)
    n_snd = lax.psum(1, "snd")
    n_rcv = lax.psum(1, "rcv")
    sender_geo = gather_cols(own_send_geo, "rcv", n_rcv)
    receiver_geo = gather_cols(own_recv_geo, "snd", n_snd)
    action_geo = geometric(action_log_shape, action_log_rate)

    send_term, recv_term, act_term = tile_pass(
        tile_counts[0, 0],
        tile_sender[0, 0],
        tile_receiver[0, 0],
        tile_action[0, 0],
        tile_fill[0],
        sender_geo,
        receiver_geo,
        action_geo,
    )
    sender_part = jnp.sum(jnp.exp(own_send_shape - own_send_rate), axis=1)
    receiver_part = jnp.sum(jnp.exp(own_recv_shape - own_recv_rate), axis=1)
    n_act = act_term.shape[1]
    stacked = jnp.concatenate([act_term, sender_part[:, None], receiver_part[:, None]], axis=1)
    stacked = sum_all(stacked, (("snd", n_snd), ("rcv", n_rcv)))
    sender_stat = scatter_cols(send_term, "rcv", n_rcv)
    receiver_stat = scatter_cols(recv_term, "snd", n_snd)
    action_stat = stacked[:, :n_act]
    sender_total = stacked[:, n_act]
    receiver_total = stacked[:, n_act + 1]
    action_total = jnp.sum(jnp.exp(action_log_shape - action_log_rate), axis=1)
    new_send_shape = refresh(own_send_shape, prior_shape + sender_stat)
    new_send_rate = refresh(own_send_rate, (prior_rate + receiver_total * action_total)[:, None])
    new_recv_shape = refresh(own_recv_shape, prior_shape + receiver_stat)
    new_recv_rate = refresh(own_recv_rate, (prior_rate + sender_total * action_total)[:, None])
    new_act_shape = refresh(action_log_shape, prior_shape + action_stat)
    new_act_rate = refresh(action_log_rate, (prior_rate + sender_total * receiver_total)[:, None])
    return (
        new_send_shape[None],
        new_send_rate[None],
        new_recv_shape[None],
        new_recv_rate[None],
        new_act_shape,
        new_act_rate,
    )


def solution(mesh):
    return jax.shard_map(
        per_device,
        mesh=mesh,
        in_specs=(
            P("snd", "rcv", None, None, None),
            P("snd", "rcv", None),
            P("snd", "rcv", None),
            P("snd", "rcv", None),
            P("snd", "rcv"),
            P("snd", None, "rcv"),
            P("snd", None, "rcv"),
            P("rcv", None, "snd"),
            P("rcv", None, "snd"),
            P(),
            P(),
        ),
        out_specs=(
            P("snd", None, "rcv"),
            P("snd", None, "rcv"),
            P("rcv", None, "snd"),
            P("rcv", None, "snd"),
            P(),
            P(),
        ),
        check_vma=False,
    )
```

```python
import jax
import jax.numpy as jnp
from jax import lax
from jax.experimental import pallas as pl
from jax.experimental.pallas import tpu as pltpu
from jax.sharding import PartitionSpec as P

prior_shape = 0.3
prior_rate = 0.3
step_size = 0.5
tile_group = 8


def digamma_series(value):
    shift_sum = jnp.zeros_like(value)
    for offset in range(6):
        shift_sum = shift_sum + 1.0 / (value + float(offset))
    moved = value + 6.0
    inverse = 1.0 / moved
    inv_square = inverse * inverse
    series = (
        jnp.log(moved)
        - 0.5 * inverse
        - inv_square * (1.0 / 12.0 - inv_square * (1.0 / 120.0 - inv_square / 252.0))
    )
    return series - shift_sum


def geometric(log_shape, log_rate):
    return jnp.exp(digamma_series(jnp.exp(log_shape)) - log_rate)


def refresh(log_value, target):
    return jnp.log((1.0 - step_size) * jnp.exp(log_value) + step_size * target)


def is_pow2(n):
    return n > 0 and n & (n - 1) == 0


def swap(x, axis, n, dist):
    return lax.ppermute(x, axis, [(i, i ^ dist) for i in range(n)])


def blocks_of(x, count):
    width = x.shape[1] // count
    return [x[:, i * width:(i + 1) * width] for i in range(count)]


def gather_cols(x, axis, n, hold=()):
    if not is_pow2(n):
        return lax.all_gather(x, axis, axis=1, tiled=True), hold
    me = lax.axis_index(axis)
    count = 1
    dist = n // 2
    while dist >= 1:
        theirs = swap(x, axis, n, dist)
        if count == 1:
            theirs, hold = lax.optimization_barrier((theirs, hold))
        low = (me & dist) == 0
        first = jnp.where(low, x, theirs)
        second = jnp.where(low, theirs, x)
        pairs = zip(blocks_of(first, count), blocks_of(second, count))
        x = jnp.concatenate([blk for pair in pairs for blk in pair], axis=1)
        count *= 2
        dist //= 2
    return x, hold


def sum_all(x, axes):
    for axis, n in axes:
        if not is_pow2(n):
            x = lax.psum(x, axis)
            continue
        dist = 1
        while dist < n:
            x = x + swap(x, axis, n, dist)
            dist *= 2
    return x


def scatter_cols(x, axis, n):
    if not is_pow2(n):
        return lax.psum_scatter(x, axis, scatter_dimension=1, tiled=True)
    me = lax.axis_index(axis)
    count = n
    dist = 1
    while dist < n:
        parts = blocks_of(x, count)
        even = jnp.concatenate(parts[0::2], axis=1)
        odd = jnp.concatenate(parts[1::2], axis=1)
        high = (me & dist) != 0
        keep = jnp.where(high, odd, even)
        give = jnp.where(high, even, odd)
        x = keep + swap(give, axis, n, dist)
        count //= 2
        dist *= 2
    return x


def tile_kernel(snd_ref, rcv_ref, act_ref, fill_ref, counts_ref, sgeo_ref, rgeo_ref, ageo_ref,
                sacc_ref, racc_ref, aacc_ref):
    step = pl.program_id(0)
    group = counts_ref.shape[0]
    edge = counts_ref.shape[-1]
    n_sb = sgeo_ref.shape[1] // edge
    n_rb = rgeo_ref.shape[1] // edge
    n_act = ageo_ref.shape[1]

    @pl.when(step == 0)
    def _():
        sacc_ref[...] = jnp.zeros_like(sacc_ref)
        racc_ref[...] = jnp.zeros_like(racc_ref)
        aacc_ref[...] = jnp.zeros_like(aacc_ref)

    for slot in range(group):
        pl.when(step * group + slot < fill_ref[0])(
            lambda slot=slot: one_tile(step * group + slot, counts_ref.at[slot], snd_ref, rcv_ref,
                                       act_ref, sgeo_ref, rgeo_ref, ageo_ref, sacc_ref, racc_ref,
                                       aacc_ref, edge, n_sb, n_rb, n_act)
        )


def one_tile(t, tile_ref, snd_ref, rcv_ref, act_ref, sgeo_ref, rgeo_ref, ageo_ref, sacc_ref,
             racc_ref, aacc_ref, edge, n_sb, n_rb, n_act):
    b = jnp.clip(snd_ref[t], 0, n_sb - 1)
    c = jnp.clip(rcv_ref[t], 0, n_rb - 1)
    a = jnp.clip(act_ref[t], 0, n_act - 1)
    s0 = pl.multiple_of(b * edge, edge)
    r0 = pl.multiple_of(c * edge, edge)
    send_cols = sgeo_ref[:, pl.ds(s0, edge)]
    recv_cols = rgeo_ref[:, pl.ds(r0, edge)]
    ageo = ageo_ref[...]
    hit = lax.broadcasted_iota(jnp.int32, ageo.shape, 1) == a
    act_col = jnp.sum(jnp.where(hit, ageo, 0.0), axis=1, keepdims=True)
    scaled = (send_cols.astype(jnp.float32) * act_col).astype(jnp.bfloat16)
    expected = lax.dot_general(
        scaled, recv_cols, (((0,), (0,)), ((), ())), preferred_element_type=jnp.float32
    )
    ratios = (tile_ref[...].astype(jnp.float32) / expected).astype(jnp.bfloat16)
    toward_send = lax.dot_general(
        recv_cols, ratios, (((1,), (1,)), ((), ())), preferred_element_type=jnp.float32
    )
    toward_recv = jnp.dot(scaled, ratios, preferred_element_type=jnp.float32)
    send_part = scaled.astype(jnp.float32) * toward_send
    recv_part = recv_cols.astype(jnp.float32) * toward_recv
    act_part = jnp.sum(send_part, axis=1, keepdims=True)
    sacc_ref[:, pl.ds(s0, edge)] += send_part
    racc_ref[:, pl.ds(r0, edge)] += recv_part
    aacc_ref[...] += jnp.where(hit, act_part, 0.0)


def tile_pass(counts, senders, receivers, actions, fill, sender_geo, receiver_geo, action_geo):
    n_slots, edge = counts.shape[0], counts.shape[1]
    group = tile_group if n_slots % tile_group == 0 else 1
    rank = sender_geo.shape[0]
    full = lambda shape: pl.BlockSpec(shape, lambda t, *_: (0,) * len(shape))
    grid_spec = pltpu.PrefetchScalarGridSpec(
        num_scalar_prefetch=4,
        grid=(n_slots // group,),
        in_specs=[
            pl.BlockSpec(
                (group, edge, edge),
                lambda g, s, r, a, f: (jnp.minimum(g, jnp.maximum(f[0] - 1, 0) // group), 0, 0),
            ),
            full(sender_geo.shape),
            full(receiver_geo.shape),
            full(action_geo.shape),
        ],
        out_specs=[
            full((rank, sender_geo.shape[1])),
            full((rank, receiver_geo.shape[1])),
            full((rank, action_geo.shape[1])),
        ],
    )
    return pl.pallas_call(
        tile_kernel,
        grid_spec=grid_spec,
        out_shape=[
            jax.ShapeDtypeStruct((rank, sender_geo.shape[1]), jnp.float32),
            jax.ShapeDtypeStruct((rank, receiver_geo.shape[1]), jnp.float32),
            jax.ShapeDtypeStruct((rank, action_geo.shape[1]), jnp.float32),
        ],
        compiler_params=pltpu.CompilerParams(dimension_semantics=("arbitrary",)),
    )(senders, receivers, actions, fill, counts, sender_geo, receiver_geo, action_geo)


def per_device(
    tile_counts,
    tile_sender,
    tile_receiver,
    tile_action,
    tile_fill,
    sender_log_shape,
    sender_log_rate,
    receiver_log_shape,
    receiver_log_rate,
    action_log_shape,
    action_log_rate,
):
    own_send_shape = sender_log_shape[0]
    own_send_rate = sender_log_rate[0]
    own_recv_shape = receiver_log_shape[0]
    own_recv_rate = receiver_log_rate[0]
    own_recv_geo = geometric(own_recv_shape, own_recv_rate).astype(jnp.bfloat16)
    n_snd = lax.psum(1, "snd")
    n_rcv = lax.psum(1, "rcv")
    receiver_geo, (held_shape, held_rate) = gather_cols(
        own_recv_geo, "snd", n_snd, (own_send_shape, own_send_rate)
    )
    own_send_geo = geometric(held_shape, held_rate).astype(jnp.bfloat16)
    sender_geo, unused = gather_cols(own_send_geo, "rcv", n_rcv)
    action_geo = geometric(action_log_shape, action_log_rate)

    send_term, recv_term, act_term = tile_pass(
        tile_counts[0, 0],
        tile_sender[0, 0],
        tile_receiver[0, 0],
        tile_action[0, 0],
        tile_fill[0],
        sender_geo,
        receiver_geo,
        action_geo,
    )
    sender_part = jnp.sum(jnp.exp(own_send_shape - own_send_rate), axis=1)
    receiver_part = jnp.sum(jnp.exp(own_recv_shape - own_recv_rate), axis=1)
    n_act = act_term.shape[1]
    stacked = jnp.concatenate([act_term, sender_part[:, None], receiver_part[:, None]], axis=1)
    stacked = sum_all(stacked, (("snd", n_snd), ("rcv", n_rcv)))
    sender_stat = scatter_cols(send_term, "rcv", n_rcv)
    receiver_stat = scatter_cols(recv_term, "snd", n_snd)
    action_stat = stacked[:, :n_act]
    sender_total = stacked[:, n_act]
    receiver_total = stacked[:, n_act + 1]
    action_total = jnp.sum(jnp.exp(action_log_shape - action_log_rate), axis=1)
    new_send_shape = refresh(own_send_shape, prior_shape + sender_stat)
    new_send_rate = refresh(own_send_rate, (prior_rate + receiver_total * action_total)[:, None])
    new_recv_shape = refresh(own_recv_shape, prior_shape + receiver_stat)
    new_recv_rate = refresh(own_recv_rate, (prior_rate + sender_total * action_total)[:, None])
    new_act_shape = refresh(action_log_shape, prior_shape + action_stat)
    new_act_rate = refresh(action_log_rate, (prior_rate + sender_total * receiver_total)[:, None])
    return (
        new_send_shape[None],
        new_send_rate[None],
        new_recv_shape[None],
        new_recv_rate[None],
        new_act_shape,
        new_act_rate,
    )


def solution(mesh):
    return jax.shard_map(
        per_device,
        mesh=mesh,
        in_specs=(
            P("snd", "rcv", None, None, None),
            P("snd", "rcv", None),
            P("snd", "rcv", None),
            P("snd", "rcv", None),
            P("snd", "rcv"),
            P("snd", None, "rcv"),
            P("snd", None, "rcv"),
            P("rcv", None, "snd"),
            P("rcv", None, "snd"),
            P(),
            P(),
        ),
        out_specs=(
            P("snd", None, "rcv"),
            P("snd", None, "rcv"),
            P("rcv", None, "snd"),
            P("rcv", None, "snd"),
            P(),
            P(),
        ),
        check_vma=False,
    )
```

```python
import jax
import jax.numpy as jnp
from jax import lax
from jax.experimental import pallas as pl
from jax.experimental.pallas import tpu as pltpu
from jax.sharding import PartitionSpec as P

prior_shape = 0.3
prior_rate = 0.3
step_size = 0.5
tile_group = 8


def digamma_series(value):
    shift_sum = jnp.zeros_like(value)
    for offset in range(6):
        shift_sum = shift_sum + 1.0 / (value + float(offset))
    moved = value + 6.0
    inverse = 1.0 / moved
    inv_square = inverse * inverse
    series = (
        jnp.log(moved)
        - 0.5 * inverse
        - inv_square * (1.0 / 12.0 - inv_square * (1.0 / 120.0 - inv_square / 252.0))
    )
    return series - shift_sum


def geometric(log_shape, log_rate):
    return jnp.exp(digamma_series(jnp.exp(log_shape)) - log_rate)


def refresh(log_value, target):
    return jnp.log((1.0 - step_size) * jnp.exp(log_value) + step_size * target)


def is_pow2(n):
    return n > 0 and n & (n - 1) == 0


def swap(x, axis, n, dist):
    return lax.ppermute(x, axis, [(i, i ^ dist) for i in range(n)])


def blocks_of(x, count):
    width = x.shape[1] // count
    return [x[:, i * width:(i + 1) * width] for i in range(count)]


def gather_cols(x, axis, n):
    if not is_pow2(n):
        return lax.all_gather(x, axis, axis=1, tiled=True)
    me = lax.axis_index(axis)
    count = 1
    dist = n // 2
    while dist >= 1:
        theirs = swap(x, axis, n, dist)
        low = (me & dist) == 0
        first = jnp.where(low, x, theirs)
        second = jnp.where(low, theirs, x)
        pairs = zip(blocks_of(first, count), blocks_of(second, count))
        x = jnp.concatenate([blk for pair in pairs for blk in pair], axis=1)
        count *= 2
        dist //= 2
    return x


def sum_all(x, axes):
    for axis, n in axes:
        if not is_pow2(n):
            x = lax.psum(x, axis)
            continue
        dist = 1
        while dist < n:
            x = x + swap(x, axis, n, dist)
            dist *= 2
    return x


def scatter_cols(x, axis, n):
    if not is_pow2(n):
        return lax.psum_scatter(x, axis, scatter_dimension=1, tiled=True)
    me = lax.axis_index(axis)
    count = n
    dist = 1
    while dist < n:
        parts = blocks_of(x, count)
        even = jnp.concatenate(parts[0::2], axis=1)
        odd = jnp.concatenate(parts[1::2], axis=1)
        high = (me & dist) != 0
        keep = jnp.where(high, odd, even)
        give = jnp.where(high, even, odd)
        x = keep + swap(give, axis, n, dist)
        count //= 2
        dist *= 2
    return x


def tile_kernel(snd_ref, rcv_ref, act_ref, fill_ref, counts_ref, sgeo_ref, rgeo_ref, ageo_ref,
                sacc_ref, racc_ref, aacc_ref):
    step = pl.program_id(0)
    group = counts_ref.shape[0]
    edge = counts_ref.shape[-1]
    n_sb = sgeo_ref.shape[1] // edge
    n_rb = rgeo_ref.shape[1] // edge
    n_act = ageo_ref.shape[1]

    @pl.when(step == 0)
    def _():
        sacc_ref[...] = jnp.zeros_like(sacc_ref)
        racc_ref[...] = jnp.zeros_like(racc_ref)
        aacc_ref[...] = jnp.zeros_like(aacc_ref)

    for slot in range(group):
        pl.when(step * group + slot < fill_ref[0])(
            lambda slot=slot: one_tile(step * group + slot, counts_ref.at[slot], snd_ref, rcv_ref,
                                       act_ref, sgeo_ref, rgeo_ref, ageo_ref, sacc_ref, racc_ref,
                                       aacc_ref, edge, n_sb, n_rb, n_act)
        )


def one_tile(t, tile_ref, snd_ref, rcv_ref, act_ref, sgeo_ref, rgeo_ref, ageo_ref, sacc_ref,
             racc_ref, aacc_ref, edge, n_sb, n_rb, n_act):
    b = jnp.clip(snd_ref[t], 0, n_sb - 1)
    c = jnp.clip(rcv_ref[t], 0, n_rb - 1)
    a = jnp.clip(act_ref[t], 0, n_act - 1)
    s0 = pl.multiple_of(b * edge, edge)
    r0 = pl.multiple_of(c * edge, edge)
    send_cols = sgeo_ref[:, pl.ds(s0, edge)]
    recv_cols = rgeo_ref[:, pl.ds(r0, edge)]
    ageo = ageo_ref[...]
    hit = lax.broadcasted_iota(jnp.int32, ageo.shape, 1) == a
    act_col = jnp.sum(jnp.where(hit, ageo, 0.0), axis=1, keepdims=True)
    scaled = (send_cols.astype(jnp.float32) * act_col).astype(jnp.bfloat16)
    expected = lax.dot_general(
        scaled, recv_cols, (((0,), (0,)), ((), ())), preferred_element_type=jnp.float32
    )
    ratios = (tile_ref[...].astype(jnp.float32) / expected).astype(jnp.bfloat16)
    toward_send = lax.dot_general(
        recv_cols, ratios, (((1,), (1,)), ((), ())), preferred_element_type=jnp.float32
    )
    toward_recv = jnp.dot(scaled, ratios, preferred_element_type=jnp.float32)
    send_part = scaled.astype(jnp.float32) * toward_send
    recv_part = recv_cols.astype(jnp.float32) * toward_recv
    act_part = jnp.sum(send_part, axis=1, keepdims=True)
    sacc_ref[:, pl.ds(s0, edge)] += send_part
    racc_ref[:, pl.ds(r0, edge)] += recv_part
    aacc_ref[...] += jnp.where(hit, act_part, 0.0)


def tile_pass(counts, senders, receivers, actions, fill, sender_geo, receiver_geo, action_geo):
    n_slots, edge = counts.shape[0], counts.shape[1]
    group = tile_group if n_slots % tile_group == 0 else 1
    rank = sender_geo.shape[0]
    full = lambda shape: pl.BlockSpec(shape, lambda t, *_: (0,) * len(shape))
    grid_spec = pltpu.PrefetchScalarGridSpec(
        num_scalar_prefetch=4,
        grid=(n_slots // group,),
        in_specs=[
            pl.BlockSpec(
                (group, edge, edge),
                lambda g, s, r, a, f: (jnp.minimum(g, jnp.maximum(f[0] - 1, 0) // group), 0, 0),
            ),
            full(sender_geo.shape),
            full(receiver_geo.shape),
            full(action_geo.shape),
        ],
        out_specs=[
            full((rank, sender_geo.shape[1])),
            full((rank, receiver_geo.shape[1])),
            full((rank, action_geo.shape[1])),
        ],
    )
    return pl.pallas_call(
        tile_kernel,
        grid_spec=grid_spec,
        out_shape=[
            jax.ShapeDtypeStruct((rank, sender_geo.shape[1]), jnp.float32),
            jax.ShapeDtypeStruct((rank, receiver_geo.shape[1]), jnp.float32),
            jax.ShapeDtypeStruct((rank, action_geo.shape[1]), jnp.float32),
        ],
        compiler_params=pltpu.CompilerParams(dimension_semantics=("arbitrary",)),
    )(senders, receivers, actions, fill, counts, sender_geo, receiver_geo, action_geo)


def per_device(
    tile_counts,
    tile_sender,
    tile_receiver,
    tile_action,
    tile_fill,
    sender_log_shape,
    sender_log_rate,
    receiver_log_shape,
    receiver_log_rate,
    action_log_shape,
    action_log_rate,
):
    own_send_shape = sender_log_shape[0]
    own_send_rate = sender_log_rate[0]
    own_recv_shape = receiver_log_shape[0]
    own_recv_rate = receiver_log_rate[0]
    own_send_geo = geometric(own_send_shape, own_send_rate).astype(jnp.bfloat16)
    own_recv_geo = geometric(own_recv_shape, own_recv_rate).astype(jnp.bfloat16)
    n_snd = lax.psum(1, "snd")
    n_rcv = lax.psum(1, "rcv")
    sender_geo = gather_cols(own_send_geo, "rcv", n_rcv)
    receiver_geo = gather_cols(own_recv_geo, "snd", n_snd)
    action_geo = geometric(action_log_shape, action_log_rate)

    send_term, recv_term, act_term = tile_pass(
        tile_counts[0, 0],
        tile_sender[0, 0],
        tile_receiver[0, 0],
        tile_action[0, 0],
        tile_fill[0],
        sender_geo,
        receiver_geo,
        action_geo,
    )
    sender_part = jnp.sum(jnp.exp(own_send_shape - own_send_rate), axis=1)
    receiver_part = jnp.sum(jnp.exp(own_recv_shape - own_recv_rate), axis=1)
    n_act = act_term.shape[1]
    stacked = jnp.concatenate([act_term, sender_part[:, None], receiver_part[:, None]], axis=1)
    stacked = sum_all(stacked, (("rcv", n_rcv), ("snd", n_snd)))
    sender_stat = scatter_cols(send_term, "rcv", n_rcv)
    receiver_stat = scatter_cols(recv_term, "snd", n_snd)
    action_stat = stacked[:, :n_act]
    sender_total = stacked[:, n_act]
    receiver_total = stacked[:, n_act + 1]
    action_total = jnp.sum(jnp.exp(action_log_shape - action_log_rate), axis=1)
    new_send_shape = refresh(own_send_shape, prior_shape + sender_stat)
    new_send_rate = refresh(own_send_rate, (prior_rate + receiver_total * action_total)[:, None])
    new_recv_shape = refresh(own_recv_shape, prior_shape + receiver_stat)
    new_recv_rate = refresh(own_recv_rate, (prior_rate + sender_total * action_total)[:, None])
    new_act_shape = refresh(action_log_shape, prior_shape + action_stat)
    new_act_rate = refresh(action_log_rate, (prior_rate + sender_total * receiver_total)[:, None])
    return (
        new_send_shape[None],
        new_send_rate[None],
        new_recv_shape[None],
        new_recv_rate[None],
        new_act_shape,
        new_act_rate,
    )


def solution(mesh):
    return jax.shard_map(
        per_device,
        mesh=mesh,
        in_specs=(
            P("snd", "rcv", None, None, None),
            P("snd", "rcv", None),
            P("snd", "rcv", None),
            P("snd", "rcv", None),
            P("snd", "rcv"),
            P("snd", None, "rcv"),
            P("snd", None, "rcv"),
            P("rcv", None, "snd"),
            P("rcv", None, "snd"),
            P(),
            P(),
        ),
        out_specs=(
            P("snd", None, "rcv"),
            P("snd", None, "rcv"),
            P("rcv", None, "snd"),
            P("rcv", None, "snd"),
            P(),
            P(),
        ),
        check_vma=False,
    )
```

```python
import jax
import jax.numpy as jnp
from jax import lax
from jax.experimental import pallas as pl
from jax.experimental.pallas import tpu as pltpu
from jax.sharding import PartitionSpec as P

prior_shape = 0.3
prior_rate = 0.3
step_size = 0.5
tile_group = 8


def digamma_series(value):
    shift_sum = jnp.zeros_like(value)
    for offset in range(6):
        shift_sum = shift_sum + 1.0 / (value + float(offset))
    moved = value + 6.0
    inverse = 1.0 / moved
    inv_square = inverse * inverse
    series = (
        jnp.log(moved)
        - 0.5 * inverse
        - inv_square * (1.0 / 12.0 - inv_square * (1.0 / 120.0 - inv_square / 252.0))
    )
    return series - shift_sum


def geometric(log_shape, log_rate):
    return jnp.exp(digamma_series(jnp.exp(log_shape)) - log_rate)


def refresh(log_value, target):
    return jnp.log((1.0 - step_size) * jnp.exp(log_value) + step_size * target)


def is_pow2(n):
    return n > 0 and n & (n - 1) == 0


def swap(x, axis, n, dist):
    return lax.ppermute(x, axis, [(i, i ^ dist) for i in range(n)])


def blocks_of(x, count):
    width = x.shape[1] // count
    return [x[:, i * width:(i + 1) * width] for i in range(count)]


def gather_cols(x, axis, n):
    if not is_pow2(n):
        return lax.all_gather(x, axis, axis=1, tiled=True)
    me = lax.axis_index(axis)
    count = 1
    dist = n // 2
    while dist >= 1:
        theirs = swap(x, axis, n, dist)
        low = (me & dist) == 0
        first = jnp.where(low, x, theirs)
        second = jnp.where(low, theirs, x)
        pairs = zip(blocks_of(first, count), blocks_of(second, count))
        x = jnp.concatenate([blk for pair in pairs for blk in pair], axis=1)
        count *= 2
        dist //= 2
    return x


def sum_all(x, axes, hold=()):
    first = True
    for axis, n in axes:
        if not is_pow2(n):
            x = lax.psum(x, axis)
            continue
        dist = 1
        while dist < n:
            x = x + swap(x, axis, n, dist)
            if first:
                x, hold = lax.optimization_barrier((x, hold))
                first = False
            dist *= 2
    return x, hold


def scatter_cols(x, axis, n):
    if not is_pow2(n):
        return lax.psum_scatter(x, axis, scatter_dimension=1, tiled=True)
    me = lax.axis_index(axis)
    count = n
    dist = 1
    while dist < n:
        parts = blocks_of(x, count)
        even = jnp.concatenate(parts[0::2], axis=1)
        odd = jnp.concatenate(parts[1::2], axis=1)
        high = (me & dist) != 0
        keep = jnp.where(high, odd, even)
        give = jnp.where(high, even, odd)
        x = keep + swap(give, axis, n, dist)
        count //= 2
        dist *= 2
    return x


def tile_kernel(snd_ref, rcv_ref, act_ref, fill_ref, counts_ref, sgeo_ref, rgeo_ref, ageo_ref,
                sacc_ref, racc_ref, aacc_ref):
    step = pl.program_id(0)
    group = counts_ref.shape[0]
    edge = counts_ref.shape[-1]
    n_sb = sgeo_ref.shape[1] // edge
    n_rb = rgeo_ref.shape[1] // edge
    n_act = ageo_ref.shape[1]

    @pl.when(step == 0)
    def _():
        sacc_ref[...] = jnp.zeros_like(sacc_ref)
        racc_ref[...] = jnp.zeros_like(racc_ref)
        aacc_ref[...] = jnp.zeros_like(aacc_ref)

    for slot in range(group):
        pl.when(step * group + slot < fill_ref[0])(
            lambda slot=slot: one_tile(step * group + slot, counts_ref.at[slot], snd_ref, rcv_ref,
                                       act_ref, sgeo_ref, rgeo_ref, ageo_ref, sacc_ref, racc_ref,
                                       aacc_ref, edge, n_sb, n_rb, n_act)
        )


def one_tile(t, tile_ref, snd_ref, rcv_ref, act_ref, sgeo_ref, rgeo_ref, ageo_ref, sacc_ref,
             racc_ref, aacc_ref, edge, n_sb, n_rb, n_act):
    b = jnp.clip(snd_ref[t], 0, n_sb - 1)
    c = jnp.clip(rcv_ref[t], 0, n_rb - 1)
    a = jnp.clip(act_ref[t], 0, n_act - 1)
    s0 = pl.multiple_of(b * edge, edge)
    r0 = pl.multiple_of(c * edge, edge)
    send_cols = sgeo_ref[:, pl.ds(s0, edge)]
    recv_cols = rgeo_ref[:, pl.ds(r0, edge)]
    ageo = ageo_ref[...]
    hit = lax.broadcasted_iota(jnp.int32, ageo.shape, 1) == a
    act_col = jnp.sum(jnp.where(hit, ageo, 0.0), axis=1, keepdims=True)
    scaled = (send_cols.astype(jnp.float32) * act_col).astype(jnp.bfloat16)
    expected = lax.dot_general(
        scaled, recv_cols, (((0,), (0,)), ((), ())), preferred_element_type=jnp.float32
    )
    ratios = (tile_ref[...].astype(jnp.float32) / expected).astype(jnp.bfloat16)
    toward_send = lax.dot_general(
        recv_cols, ratios, (((1,), (1,)), ((), ())), preferred_element_type=jnp.float32
    )
    toward_recv = jnp.dot(scaled, ratios, preferred_element_type=jnp.float32)
    send_part = scaled.astype(jnp.float32) * toward_send
    recv_part = recv_cols.astype(jnp.float32) * toward_recv
    act_part = jnp.sum(send_part, axis=1, keepdims=True)
    sacc_ref[:, pl.ds(s0, edge)] += send_part
    racc_ref[:, pl.ds(r0, edge)] += recv_part
    aacc_ref[...] += jnp.where(hit, act_part, 0.0)


def tile_pass(counts, senders, receivers, actions, fill, sender_geo, receiver_geo, action_geo):
    n_slots, edge = counts.shape[0], counts.shape[1]
    group = tile_group if n_slots % tile_group == 0 else 1
    rank = sender_geo.shape[0]
    full = lambda shape: pl.BlockSpec(shape, lambda t, *_: (0,) * len(shape))
    grid_spec = pltpu.PrefetchScalarGridSpec(
        num_scalar_prefetch=4,
        grid=(n_slots // group,),
        in_specs=[
            pl.BlockSpec(
                (group, edge, edge),
                lambda g, s, r, a, f: (jnp.minimum(g, jnp.maximum(f[0] - 1, 0) // group), 0, 0),
            ),
            full(sender_geo.shape),
            full(receiver_geo.shape),
            full(action_geo.shape),
        ],
        out_specs=[
            full((rank, sender_geo.shape[1])),
            full((rank, receiver_geo.shape[1])),
            full((rank, action_geo.shape[1])),
        ],
    )
    return pl.pallas_call(
        tile_kernel,
        grid_spec=grid_spec,
        out_shape=[
            jax.ShapeDtypeStruct((rank, sender_geo.shape[1]), jnp.float32),
            jax.ShapeDtypeStruct((rank, receiver_geo.shape[1]), jnp.float32),
            jax.ShapeDtypeStruct((rank, action_geo.shape[1]), jnp.float32),
        ],
        compiler_params=pltpu.CompilerParams(dimension_semantics=("arbitrary",)),
    )(senders, receivers, actions, fill, counts, sender_geo, receiver_geo, action_geo)


def per_device(
    tile_counts,
    tile_sender,
    tile_receiver,
    tile_action,
    tile_fill,
    sender_log_shape,
    sender_log_rate,
    receiver_log_shape,
    receiver_log_rate,
    action_log_shape,
    action_log_rate,
):
    own_send_shape = sender_log_shape[0]
    own_send_rate = sender_log_rate[0]
    own_recv_shape = receiver_log_shape[0]
    own_recv_rate = receiver_log_rate[0]
    own_send_geo = geometric(own_send_shape, own_send_rate).astype(jnp.bfloat16)
    own_recv_geo = geometric(own_recv_shape, own_recv_rate).astype(jnp.bfloat16)
    n_snd = lax.psum(1, "snd")
    n_rcv = lax.psum(1, "rcv")
    sender_geo = gather_cols(own_send_geo, "rcv", n_rcv)
    receiver_geo = gather_cols(own_recv_geo, "snd", n_snd)
    action_geo = geometric(action_log_shape, action_log_rate)

    send_term, recv_term, act_term = tile_pass(
        tile_counts[0, 0],
        tile_sender[0, 0],
        tile_receiver[0, 0],
        tile_action[0, 0],
        tile_fill[0],
        sender_geo,
        receiver_geo,
        action_geo,
    )
    sender_part = jnp.sum(jnp.exp(own_send_shape - own_send_rate), axis=1)
    receiver_part = jnp.sum(jnp.exp(own_recv_shape - own_recv_rate), axis=1)
    n_act = act_term.shape[1]
    stacked = jnp.concatenate([act_term, sender_part[:, None], receiver_part[:, None]], axis=1)
    stacked, (send_term, recv_term) = sum_all(
        stacked, (("rcv", n_rcv), ("snd", n_snd)), (send_term, recv_term)
    )
    sender_stat = scatter_cols(send_term, "rcv", n_rcv)
    receiver_stat = scatter_cols(recv_term, "snd", n_snd)
    action_stat = stacked[:, :n_act]
    sender_total = stacked[:, n_act]
    receiver_total = stacked[:, n_act + 1]
    action_total = jnp.sum(jnp.exp(action_log_shape - action_log_rate), axis=1)
    new_send_shape = refresh(own_send_shape, prior_shape + sender_stat)
    new_send_rate = refresh(own_send_rate, (prior_rate + receiver_total * action_total)[:, None])
    new_recv_shape = refresh(own_recv_shape, prior_shape + receiver_stat)
    new_recv_rate = refresh(own_recv_rate, (prior_rate + sender_total * action_total)[:, None])
    new_act_shape = refresh(action_log_shape, prior_shape + action_stat)
    new_act_rate = refresh(action_log_rate, (prior_rate + sender_total * receiver_total)[:, None])
    return (
        new_send_shape[None],
        new_send_rate[None],
        new_recv_shape[None],
        new_recv_rate[None],
        new_act_shape,
        new_act_rate,
    )


def solution(mesh):
    return jax.shard_map(
        per_device,
        mesh=mesh,
        in_specs=(
            P("snd", "rcv", None, None, None),
            P("snd", "rcv", None),
            P("snd", "rcv", None),
            P("snd", "rcv", None),
            P("snd", "rcv"),
            P("snd", None, "rcv"),
            P("snd", None, "rcv"),
            P("rcv", None, "snd"),
            P("rcv", None, "snd"),
            P(),
            P(),
        ),
        out_specs=(
            P("snd", None, "rcv"),
            P("snd", None, "rcv"),
            P("rcv", None, "snd"),
            P("rcv", None, "snd"),
            P(),
            P(),
        ),
        check_vma=False,
    )
```

```python
import jax
import jax.numpy as jnp
from jax import lax
from jax.experimental import pallas as pl
from jax.experimental.pallas import tpu as pltpu
from jax.sharding import PartitionSpec as P

prior_shape = 0.3
prior_rate = 0.3
step_size = 0.5
tile_group = 8


def digamma_series(value):
    shift_sum = jnp.zeros_like(value)
    for offset in range(6):
        shift_sum = shift_sum + 1.0 / (value + float(offset))
    moved = value + 6.0
    inverse = 1.0 / moved
    inv_square = inverse * inverse
    series = (
        jnp.log(moved)
        - 0.5 * inverse
        - inv_square * (1.0 / 12.0 - inv_square * (1.0 / 120.0 - inv_square / 252.0))
    )
    return series - shift_sum


def geometric(log_shape, log_rate):
    return jnp.exp(digamma_series(jnp.exp(log_shape)) - log_rate)


def refresh(log_value, target):
    return jnp.log((1.0 - step_size) * jnp.exp(log_value) + step_size * target)


def is_pow2(n):
    return n > 0 and n & (n - 1) == 0


def swap(x, axis, n, dist):
    return lax.ppermute(x, axis, [(i, i ^ dist) for i in range(n)])


def blocks_of(x, count):
    width = x.shape[1] // count
    return [x[:, i * width:(i + 1) * width] for i in range(count)]


def gather_cols(x, axis, n):
    if not is_pow2(n):
        return lax.all_gather(x, axis, axis=1, tiled=True)
    me = lax.axis_index(axis)
    count = 1
    dist = n // 2
    while dist >= 1:
        theirs = swap(x, axis, n, dist)
        low = (me & dist) == 0
        first = jnp.where(low, x, theirs)
        second = jnp.where(low, theirs, x)
        pairs = zip(blocks_of(first, count), blocks_of(second, count))
        x = jnp.concatenate([blk for pair in pairs for blk in pair], axis=1)
        count *= 2
        dist //= 2
    return x


def sum_all(x, axes):
    for axis, n in axes:
        if not is_pow2(n):
            x = lax.psum(x, axis)
            continue
        dist = 1
        while dist < n:
            x = x + swap(x, axis, n, dist)
            dist *= 2
    return x


def scatter_cols(x, axis, n):
    if not is_pow2(n):
        return lax.psum_scatter(x, axis, scatter_dimension=1, tiled=True)
    me = lax.axis_index(axis)
    count = n
    dist = 1
    while dist < n:
        parts = blocks_of(x, count)
        even = jnp.concatenate(parts[0::2], axis=1)
        odd = jnp.concatenate(parts[1::2], axis=1)
        high = (me & dist) != 0
        keep = jnp.where(high, odd, even)
        give = jnp.where(high, even, odd)
        x = keep + swap(give, axis, n, dist)
        count //= 2
        dist *= 2
    return x


def tile_kernel(snd_ref, rcv_ref, act_ref, fill_ref, counts_ref, weight_ref, sgeo_ref, rgeo_ref,
                sacc_ref, racc_ref, aacc_ref):
    step = pl.program_id(0)
    group = counts_ref.shape[0]
    edge = counts_ref.shape[-1]
    n_sb = sgeo_ref.shape[1] // edge
    n_rb = rgeo_ref.shape[1] // edge
    n_act = aacc_ref.shape[1]

    @pl.when(step == 0)
    def _():
        sacc_ref[...] = jnp.zeros_like(sacc_ref)
        racc_ref[...] = jnp.zeros_like(racc_ref)
        aacc_ref[...] = jnp.zeros_like(aacc_ref)

    for slot in range(group):
        pl.when(step * group + slot < fill_ref[0])(
            lambda slot=slot: one_tile(step * group + slot, counts_ref.at[slot], weight_ref.at[slot],
                                       snd_ref, rcv_ref, act_ref, sgeo_ref, rgeo_ref, sacc_ref,
                                       racc_ref, aacc_ref, edge, n_sb, n_rb, n_act)
        )


def one_tile(t, tile_ref, weight_ref, snd_ref, rcv_ref, act_ref, sgeo_ref, rgeo_ref, sacc_ref,
             racc_ref, aacc_ref, edge, n_sb, n_rb, n_act):
    b = jnp.clip(snd_ref[t], 0, n_sb - 1)
    c = jnp.clip(rcv_ref[t], 0, n_rb - 1)
    a = jnp.clip(act_ref[t], 0, n_act - 1)
    s0 = pl.multiple_of(b * edge, edge)
    r0 = pl.multiple_of(c * edge, edge)
    send_cols = sgeo_ref[:, pl.ds(s0, edge)]
    recv_cols = rgeo_ref[:, pl.ds(r0, edge)]
    hit = lax.broadcasted_iota(jnp.int32, aacc_ref.shape, 1) == a
    scaled = (send_cols.astype(jnp.float32) * weight_ref[...]).astype(jnp.bfloat16)
    expected = lax.dot_general(
        scaled, recv_cols, (((0,), (0,)), ((), ())), preferred_element_type=jnp.float32
    )
    ratios = (tile_ref[...].astype(jnp.float32) / expected).astype(jnp.bfloat16)
    toward_send = lax.dot_general(
        recv_cols, ratios, (((1,), (1,)), ((), ())), preferred_element_type=jnp.float32
    )
    toward_recv = jnp.dot(scaled, ratios, preferred_element_type=jnp.float32)
    send_part = scaled.astype(jnp.float32) * toward_send
    recv_part = recv_cols.astype(jnp.float32) * toward_recv
    act_part = jnp.sum(send_part, axis=1, keepdims=True)
    sacc_ref[:, pl.ds(s0, edge)] += send_part
    racc_ref[:, pl.ds(r0, edge)] += recv_part
    aacc_ref[...] += jnp.where(hit, act_part, 0.0)


def tile_pass(counts, senders, receivers, actions, fill, sender_geo, receiver_geo, action_geo):
    n_slots, edge = counts.shape[0], counts.shape[1]
    group = tile_group if n_slots % tile_group == 0 else 1
    rank = sender_geo.shape[0]
    weights = jnp.take(action_geo, actions, axis=1, mode="clip").T[:, :, None]
    full = lambda shape: pl.BlockSpec(shape, lambda t, *_: (0,) * len(shape))
    slot_block = lambda g, s, r, a, f: (jnp.minimum(g, jnp.maximum(f[0] - 1, 0) // group), 0, 0)
    grid_spec = pltpu.PrefetchScalarGridSpec(
        num_scalar_prefetch=4,
        grid=(n_slots // group,),
        in_specs=[
            pl.BlockSpec((group, edge, edge), slot_block),
            pl.BlockSpec((group, rank, 1), slot_block),
            full(sender_geo.shape),
            full(receiver_geo.shape),
        ],
        out_specs=[
            full((rank, sender_geo.shape[1])),
            full((rank, receiver_geo.shape[1])),
            full((rank, action_geo.shape[1])),
        ],
    )
    return pl.pallas_call(
        tile_kernel,
        grid_spec=grid_spec,
        out_shape=[
            jax.ShapeDtypeStruct((rank, sender_geo.shape[1]), jnp.float32),
            jax.ShapeDtypeStruct((rank, receiver_geo.shape[1]), jnp.float32),
            jax.ShapeDtypeStruct((rank, action_geo.shape[1]), jnp.float32),
        ],
        compiler_params=pltpu.CompilerParams(dimension_semantics=("arbitrary",)),
    )(senders, receivers, actions, fill, counts, weights, sender_geo, receiver_geo)


def per_device(
    tile_counts,
    tile_sender,
    tile_receiver,
    tile_action,
    tile_fill,
    sender_log_shape,
    sender_log_rate,
    receiver_log_shape,
    receiver_log_rate,
    action_log_shape,
    action_log_rate,
):
    own_send_shape = sender_log_shape[0]
    own_send_rate = sender_log_rate[0]
    own_recv_shape = receiver_log_shape[0]
    own_recv_rate = receiver_log_rate[0]
    own_send_geo = geometric(own_send_shape, own_send_rate).astype(jnp.bfloat16)
    own_recv_geo = geometric(own_recv_shape, own_recv_rate).astype(jnp.bfloat16)
    n_snd = lax.psum(1, "snd")
    n_rcv = lax.psum(1, "rcv")
    sender_geo = gather_cols(own_send_geo, "rcv", n_rcv)
    receiver_geo = gather_cols(own_recv_geo, "snd", n_snd)
    action_geo = geometric(action_log_shape, action_log_rate)

    send_term, recv_term, act_term = tile_pass(
        tile_counts[0, 0],
        tile_sender[0, 0],
        tile_receiver[0, 0],
        tile_action[0, 0],
        tile_fill[0],
        sender_geo,
        receiver_geo,
        action_geo,
    )
    sender_part = jnp.sum(jnp.exp(own_send_shape - own_send_rate), axis=1)
    receiver_part = jnp.sum(jnp.exp(own_recv_shape - own_recv_rate), axis=1)
    n_act = act_term.shape[1]
    stacked = jnp.concatenate([act_term, sender_part[:, None], receiver_part[:, None]], axis=1)
    stacked = sum_all(stacked, (("rcv", n_rcv), ("snd", n_snd)))
    sender_stat = scatter_cols(send_term, "rcv", n_rcv)
    receiver_stat = scatter_cols(recv_term, "snd", n_snd)
    action_stat = stacked[:, :n_act]
    sender_total = stacked[:, n_act]
    receiver_total = stacked[:, n_act + 1]
    action_total = jnp.sum(jnp.exp(action_log_shape - action_log_rate), axis=1)
    new_send_shape = refresh(own_send_shape, prior_shape + sender_stat)
    new_send_rate = refresh(own_send_rate, (prior_rate + receiver_total * action_total)[:, None])
    new_recv_shape = refresh(own_recv_shape, prior_shape + receiver_stat)
    new_recv_rate = refresh(own_recv_rate, (prior_rate + sender_total * action_total)[:, None])
    new_act_shape = refresh(action_log_shape, prior_shape + action_stat)
    new_act_rate = refresh(action_log_rate, (prior_rate + sender_total * receiver_total)[:, None])
    return (
        new_send_shape[None],
        new_send_rate[None],
        new_recv_shape[None],
        new_recv_rate[None],
        new_act_shape,
        new_act_rate,
    )


def solution(mesh):
    return jax.shard_map(
        per_device,
        mesh=mesh,
        in_specs=(
            P("snd", "rcv", None, None, None),
            P("snd", "rcv", None),
            P("snd", "rcv", None),
            P("snd", "rcv", None),
            P("snd", "rcv"),
            P("snd", None, "rcv"),
            P("snd", None, "rcv"),
            P("rcv", None, "snd"),
            P("rcv", None, "snd"),
            P(),
            P(),
        ),
        out_specs=(
            P("snd", None, "rcv"),
            P("snd", None, "rcv"),
            P("rcv", None, "snd"),
            P("rcv", None, "snd"),
            P(),
            P(),
        ),
        check_vma=False,
    )
```

```python
import jax
import jax.numpy as jnp
from jax import lax
from jax.experimental import pallas as pl
from jax.experimental.pallas import tpu as pltpu
from jax.sharding import PartitionSpec as P

prior_shape = 0.3
prior_rate = 0.3
step_size = 0.5
tile_group = 8


def digamma_series(value):
    shift_sum = jnp.zeros_like(value)
    for offset in range(6):
        shift_sum = shift_sum + 1.0 / (value + float(offset))
    moved = value + 6.0
    inverse = 1.0 / moved
    inv_square = inverse * inverse
    series = (
        jnp.log(moved)
        - 0.5 * inverse
        - inv_square * (1.0 / 12.0 - inv_square * (1.0 / 120.0 - inv_square / 252.0))
    )
    return series - shift_sum


def geometric(log_shape, log_rate):
    return jnp.exp(digamma_series(jnp.exp(log_shape)) - log_rate)


def refresh(log_value, target):
    return jnp.log((1.0 - step_size) * jnp.exp(log_value) + step_size * target)


def is_pow2(n):
    return n > 0 and n & (n - 1) == 0


def swap(x, axis, n, dist):
    return lax.ppermute(x, axis, [(i, i ^ dist) for i in range(n)])


def blocks_of(x, count):
    width = x.shape[1] // count
    return [x[:, i * width:(i + 1) * width] for i in range(count)]


def gather_cols(x, axis, n):
    if not is_pow2(n):
        return lax.all_gather(x, axis, axis=1, tiled=True)
    me = lax.axis_index(axis)
    count = 1
    dist = n // 2
    while dist >= 1:
        theirs = swap(x, axis, n, dist)
        low = (me & dist) == 0
        first = jnp.where(low, x, theirs)
        second = jnp.where(low, theirs, x)
        pairs = zip(blocks_of(first, count), blocks_of(second, count))
        x = jnp.concatenate([blk for pair in pairs for blk in pair], axis=1)
        count *= 2
        dist //= 2
    return x


def sum_all(x, axes):
    for axis, n in axes:
        if not is_pow2(n):
            x = lax.psum(x, axis)
            continue
        dist = 1
        while dist < n:
            x = x + swap(x, axis, n, dist)
            dist *= 2
    return x


def scatter_cols(x, axis, n):
    if not is_pow2(n):
        return lax.psum_scatter(x, axis, scatter_dimension=1, tiled=True)
    me = lax.axis_index(axis)
    count = n
    dist = 1
    while dist < n:
        parts = blocks_of(x, count)
        even = jnp.concatenate(parts[0::2], axis=1)
        odd = jnp.concatenate(parts[1::2], axis=1)
        high = (me & dist) != 0
        keep = jnp.where(high, odd, even)
        give = jnp.where(high, even, odd)
        x = keep + swap(give, axis, n, dist)
        count //= 2
        dist *= 2
    return x


def tile_kernel(snd_ref, rcv_ref, act_ref, fill_ref, counts_ref, sgeo_ref, rgeo_ref, ageo_ref,
                sacc_ref, racc_ref, aacc_ref):
    step = pl.program_id(0)
    group = counts_ref.shape[0]
    edge = counts_ref.shape[-1]
    n_sb = sgeo_ref.shape[1] // edge
    n_rb = rgeo_ref.shape[1] // edge
    n_act = ageo_ref.shape[1]

    @pl.when(step == 0)
    def _():
        sacc_ref[...] = jnp.zeros_like(sacc_ref)
        racc_ref[...] = jnp.zeros_like(racc_ref)
        aacc_ref[...] = jnp.zeros_like(aacc_ref)

    for slot in range(group):
        pl.when(step * group + slot < fill_ref[0])(
            lambda slot=slot: one_tile(step * group + slot, counts_ref.at[slot], snd_ref, rcv_ref,
                                       act_ref, sgeo_ref, rgeo_ref, ageo_ref, sacc_ref, racc_ref,
                                       aacc_ref, edge, n_sb, n_rb, n_act)
        )


def one_tile(t, tile_ref, snd_ref, rcv_ref, act_ref, sgeo_ref, rgeo_ref, ageo_ref, sacc_ref,
             racc_ref, aacc_ref, edge, n_sb, n_rb, n_act):
    b = jnp.clip(snd_ref[t], 0, n_sb - 1)
    c = jnp.clip(rcv_ref[t], 0, n_rb - 1)
    a = jnp.clip(act_ref[t], 0, n_act - 1)
    s0 = pl.multiple_of(b * edge, edge)
    r0 = pl.multiple_of(c * edge, edge)
    send_cols = sgeo_ref[:, pl.ds(s0, edge)]
    recv_cols = rgeo_ref[:, pl.ds(r0, edge)]
    ageo = ageo_ref[...]
    hit = lax.broadcasted_iota(jnp.int32, ageo.shape, 1) == a
    act_col = jnp.sum(jnp.where(hit, ageo, 0.0), axis=1, keepdims=True)
    scaled = (send_cols.astype(jnp.float32) * act_col).astype(jnp.bfloat16)
    expected = lax.dot_general(
        scaled, recv_cols, (((0,), (0,)), ((), ())), preferred_element_type=jnp.float32
    )
    ratios = (tile_ref[...].astype(jnp.float32) / expected).astype(jnp.bfloat16)
    toward_send = lax.dot_general(
        recv_cols, ratios, (((1,), (1,)), ((), ())), preferred_element_type=jnp.float32
    )
    toward_recv = jnp.dot(scaled, ratios, preferred_element_type=jnp.float32)
    send_part = scaled.astype(jnp.float32) * toward_send
    recv_part = recv_cols.astype(jnp.float32) * toward_recv
    act_part = jnp.sum(send_part, axis=1, keepdims=True)
    sacc_ref[:, pl.ds(s0, edge)] += send_part
    racc_ref[:, pl.ds(r0, edge)] += recv_part
    aacc_ref[...] += jnp.where(hit, act_part, 0.0)


def tile_pass(counts, senders, receivers, actions, fill, sender_geo, receiver_geo, action_geo):
    n_slots, edge = counts.shape[0], counts.shape[1]
    group = tile_group if n_slots % tile_group == 0 else 1
    rank = sender_geo.shape[0]
    full = lambda shape: pl.BlockSpec(shape, lambda t, *_: (0,) * len(shape))
    grid_spec = pltpu.PrefetchScalarGridSpec(
        num_scalar_prefetch=4,
        grid=(n_slots // group,),
        in_specs=[
            pl.BlockSpec(
                (group, edge, edge),
                lambda g, s, r, a, f: (jnp.minimum(g, jnp.maximum(f[0] - 1, 0) // group), 0, 0),
            ),
            full(sender_geo.shape),
            full(receiver_geo.shape),
            full(action_geo.shape),
        ],
        out_specs=[
            full((rank, sender_geo.shape[1])),
            full((rank, receiver_geo.shape[1])),
            full((rank, action_geo.shape[1])),
        ],
    )
    return pl.pallas_call(
        tile_kernel,
        grid_spec=grid_spec,
        out_shape=[
            jax.ShapeDtypeStruct((rank, sender_geo.shape[1]), jnp.float32),
            jax.ShapeDtypeStruct((rank, receiver_geo.shape[1]), jnp.float32),
            jax.ShapeDtypeStruct((rank, action_geo.shape[1]), jnp.float32),
        ],
        compiler_params=pltpu.CompilerParams(dimension_semantics=("arbitrary",)),
    )(senders, receivers, actions, fill, counts, sender_geo, receiver_geo, action_geo)


def tail_kernel(stk_ref, act_shape_ref, act_rate_ref, send_rate_ref, recv_rate_ref, act_total_ref,
                new_act_shape_ref, new_act_rate_ref, new_send_rate_ref, new_recv_rate_ref):
    n_act = act_shape_ref.shape[1]
    stk = stk_ref[...]
    sender_total = stk[:, n_act:n_act + 1]
    receiver_total = stk[:, n_act + 1:n_act + 2]
    action_total = act_total_ref[...]
    new_act_shape_ref[...] = refresh(act_shape_ref[...], prior_shape + stk[:, :n_act])
    new_act_rate_ref[...] = refresh(act_rate_ref[...], prior_rate + sender_total * receiver_total)
    new_send_rate_ref[...] = refresh(send_rate_ref[...], prior_rate + receiver_total * action_total)
    new_recv_rate_ref[...] = refresh(recv_rate_ref[...], prior_rate + sender_total * action_total)


def per_device(
    tile_counts,
    tile_sender,
    tile_receiver,
    tile_action,
    tile_fill,
    sender_log_shape,
    sender_log_rate,
    receiver_log_shape,
    receiver_log_rate,
    action_log_shape,
    action_log_rate,
):
    own_send_shape = sender_log_shape[0]
    own_send_rate = sender_log_rate[0]
    own_recv_shape = receiver_log_shape[0]
    own_recv_rate = receiver_log_rate[0]
    own_send_geo = geometric(own_send_shape, own_send_rate).astype(jnp.bfloat16)
    own_recv_geo = geometric(own_recv_shape, own_recv_rate).astype(jnp.bfloat16)
    n_snd = lax.psum(1, "snd")
    n_rcv = lax.psum(1, "rcv")
    sender_geo = gather_cols(own_send_geo, "rcv", n_rcv)
    receiver_geo = gather_cols(own_recv_geo, "snd", n_snd)
    action_geo = geometric(action_log_shape, action_log_rate)

    send_term, recv_term, act_term = tile_pass(
        tile_counts[0, 0],
        tile_sender[0, 0],
        tile_receiver[0, 0],
        tile_action[0, 0],
        tile_fill[0],
        sender_geo,
        receiver_geo,
        action_geo,
    )
    sender_part = jnp.sum(jnp.exp(own_send_shape - own_send_rate), axis=1)
    receiver_part = jnp.sum(jnp.exp(own_recv_shape - own_recv_rate), axis=1)
    n_act = act_term.shape[1]
    stacked = jnp.concatenate([act_term, sender_part[:, None], receiver_part[:, None]], axis=1)
    stacked = sum_all(stacked, (("rcv", n_rcv), ("snd", n_snd)))
    sender_stat = scatter_cols(send_term, "rcv", n_rcv)
    receiver_stat = scatter_cols(recv_term, "snd", n_snd)
    action_total = jnp.sum(jnp.exp(action_log_shape - action_log_rate), axis=1, keepdims=True)
    new_send_shape = refresh(own_send_shape, prior_shape + sender_stat)
    new_recv_shape = refresh(own_recv_shape, prior_shape + receiver_stat)
    new_act_shape, new_act_rate, new_send_rate, new_recv_rate = pl.pallas_call(
        tail_kernel,
        out_shape=[
            jax.ShapeDtypeStruct(action_log_shape.shape, jnp.float32),
            jax.ShapeDtypeStruct(action_log_rate.shape, jnp.float32),
            jax.ShapeDtypeStruct(own_send_rate.shape, jnp.float32),
            jax.ShapeDtypeStruct(own_recv_rate.shape, jnp.float32),
        ],
    )(stacked, action_log_shape, action_log_rate, own_send_rate, own_recv_rate, action_total)
    return (
        new_send_shape[None],
        new_send_rate[None],
        new_recv_shape[None],
        new_recv_rate[None],
        new_act_shape,
        new_act_rate,
    )


def solution(mesh):
    return jax.shard_map(
        per_device,
        mesh=mesh,
        in_specs=(
            P("snd", "rcv", None, None, None),
            P("snd", "rcv", None),
            P("snd", "rcv", None),
            P("snd", "rcv", None),
            P("snd", "rcv"),
            P("snd", None, "rcv"),
            P("snd", None, "rcv"),
            P("rcv", None, "snd"),
            P("rcv", None, "snd"),
            P(),
            P(),
        ),
        out_specs=(
            P("snd", None, "rcv"),
            P("snd", None, "rcv"),
            P("rcv", None, "snd"),
            P("rcv", None, "snd"),
            P(),
            P(),
        ),
        check_vma=False,
    )
```

```python
import jax
import jax.numpy as jnp
from jax import lax
from jax.experimental import pallas as pl
from jax.experimental.pallas import tpu as pltpu
from jax.sharding import PartitionSpec as P

prior_shape = 0.3
prior_rate = 0.3
step_size = 0.5
tile_group = 8


def digamma_series(value):
    shift_sum = jnp.zeros_like(value)
    for offset in range(6):
        shift_sum = shift_sum + 1.0 / (value + float(offset))
    moved = value + 6.0
    inverse = 1.0 / moved
    inv_square = inverse * inverse
    series = (
        jnp.log(moved)
        - 0.5 * inverse
        - inv_square * (1.0 / 12.0 - inv_square * (1.0 / 120.0 - inv_square / 252.0))
    )
    return series - shift_sum


def geometric(log_shape, log_rate):
    return jnp.exp(digamma_series(jnp.exp(log_shape)) - log_rate)


def refresh(log_value, target):
    return jnp.log((1.0 - step_size) * jnp.exp(log_value) + step_size * target)


def is_pow2(n):
    return n > 0 and n & (n - 1) == 0


def swap(x, axis, n, dist):
    return lax.ppermute(x, axis, [(i, i ^ dist) for i in range(n)])


def blocks_of(x, count):
    width = x.shape[1] // count
    return [x[:, i * width:(i + 1) * width] for i in range(count)]


def gather_cols(x, axis, n):
    if not is_pow2(n):
        return lax.all_gather(x, axis, axis=1, tiled=True)
    me = lax.axis_index(axis)
    count = 1
    dist = n // 2
    while dist >= 1:
        theirs = swap(x, axis, n, dist)
        low = (me & dist) == 0
        first = jnp.where(low, x, theirs)
        second = jnp.where(low, theirs, x)
        pairs = zip(blocks_of(first, count), blocks_of(second, count))
        x = jnp.concatenate([blk for pair in pairs for blk in pair], axis=1)
        count *= 2
        dist //= 2
    return x


def sum_all(x, axes):
    got = jnp.zeros_like(x)
    for axis, n in axes:
        if not is_pow2(n):
            x = lax.psum(x + got, axis)
            got = jnp.zeros_like(x)
            continue
        dist = 1
        while dist < n:
            x = x + got
            got = swap(x, axis, n, dist)
            dist *= 2
    return x, got


def scatter_cols(x, axis, n):
    if not is_pow2(n):
        return lax.psum_scatter(x, axis, scatter_dimension=1, tiled=True)
    me = lax.axis_index(axis)
    count = n
    dist = 1
    while dist < n:
        parts = blocks_of(x, count)
        even = jnp.concatenate(parts[0::2], axis=1)
        odd = jnp.concatenate(parts[1::2], axis=1)
        high = (me & dist) != 0
        keep = jnp.where(high, odd, even)
        give = jnp.where(high, even, odd)
        x = keep + swap(give, axis, n, dist)
        count //= 2
        dist *= 2
    return x


def tile_kernel(snd_ref, rcv_ref, act_ref, fill_ref, counts_ref, sgeo_ref, rgeo_ref, ageo_ref,
                sacc_ref, racc_ref, aacc_ref):
    step = pl.program_id(0)
    group = counts_ref.shape[0]
    edge = counts_ref.shape[-1]
    n_sb = sgeo_ref.shape[1] // edge
    n_rb = rgeo_ref.shape[1] // edge
    n_act = ageo_ref.shape[1]

    @pl.when(step == 0)
    def _():
        sacc_ref[...] = jnp.zeros_like(sacc_ref)
        racc_ref[...] = jnp.zeros_like(racc_ref)
        aacc_ref[...] = jnp.zeros_like(aacc_ref)

    for slot in range(group):
        pl.when(step * group + slot < fill_ref[0])(
            lambda slot=slot: one_tile(step * group + slot, counts_ref.at[slot], snd_ref, rcv_ref,
                                       act_ref, sgeo_ref, rgeo_ref, ageo_ref, sacc_ref, racc_ref,
                                       aacc_ref, edge, n_sb, n_rb, n_act)
        )


def one_tile(t, tile_ref, snd_ref, rcv_ref, act_ref, sgeo_ref, rgeo_ref, ageo_ref, sacc_ref,
             racc_ref, aacc_ref, edge, n_sb, n_rb, n_act):
    b = jnp.clip(snd_ref[t], 0, n_sb - 1)
    c = jnp.clip(rcv_ref[t], 0, n_rb - 1)
    a = jnp.clip(act_ref[t], 0, n_act - 1)
    s0 = pl.multiple_of(b * edge, edge)
    r0 = pl.multiple_of(c * edge, edge)
    send_cols = sgeo_ref[:, pl.ds(s0, edge)]
    recv_cols = rgeo_ref[:, pl.ds(r0, edge)]
    ageo = ageo_ref[...]
    hit = lax.broadcasted_iota(jnp.int32, ageo.shape, 1) == a
    act_col = jnp.sum(jnp.where(hit, ageo, 0.0), axis=1, keepdims=True)
    scaled = (send_cols.astype(jnp.float32) * act_col).astype(jnp.bfloat16)
    expected = lax.dot_general(
        scaled, recv_cols, (((0,), (0,)), ((), ())), preferred_element_type=jnp.float32
    )
    ratios = (tile_ref[...].astype(jnp.float32) / expected).astype(jnp.bfloat16)
    toward_send = lax.dot_general(
        recv_cols, ratios, (((1,), (1,)), ((), ())), preferred_element_type=jnp.float32
    )
    toward_recv = jnp.dot(scaled, ratios, preferred_element_type=jnp.float32)
    send_part = scaled.astype(jnp.float32) * toward_send
    recv_part = recv_cols.astype(jnp.float32) * toward_recv
    act_part = jnp.sum(send_part, axis=1, keepdims=True)
    sacc_ref[:, pl.ds(s0, edge)] += send_part
    racc_ref[:, pl.ds(r0, edge)] += recv_part
    aacc_ref[...] += jnp.where(hit, act_part, 0.0)


def tile_pass(counts, senders, receivers, actions, fill, sender_geo, receiver_geo, action_geo):
    n_slots, edge = counts.shape[0], counts.shape[1]
    group = tile_group if n_slots % tile_group == 0 else 1
    rank = sender_geo.shape[0]
    full = lambda shape: pl.BlockSpec(shape, lambda t, *_: (0,) * len(shape))
    grid_spec = pltpu.PrefetchScalarGridSpec(
        num_scalar_prefetch=4,
        grid=(n_slots // group,),
        in_specs=[
            pl.BlockSpec(
                (group, edge, edge),
                lambda g, s, r, a, f: (jnp.minimum(g, jnp.maximum(f[0] - 1, 0) // group), 0, 0),
            ),
            full(sender_geo.shape),
            full(receiver_geo.shape),
            full(action_geo.shape),
        ],
        out_specs=[
            full((rank, sender_geo.shape[1])),
            full((rank, receiver_geo.shape[1])),
            full((rank, action_geo.shape[1])),
        ],
    )
    return pl.pallas_call(
        tile_kernel,
        grid_spec=grid_spec,
        out_shape=[
            jax.ShapeDtypeStruct((rank, sender_geo.shape[1]), jnp.float32),
            jax.ShapeDtypeStruct((rank, receiver_geo.shape[1]), jnp.float32),
            jax.ShapeDtypeStruct((rank, action_geo.shape[1]), jnp.float32),
        ],
        compiler_params=pltpu.CompilerParams(dimension_semantics=("arbitrary",)),
    )(senders, receivers, actions, fill, counts, sender_geo, receiver_geo, action_geo)


def tail_kernel(stk_ref, got_ref, act_shape_ref, act_rate_ref, send_rate_ref, recv_rate_ref,
                act_total_ref, new_act_shape_ref, new_act_rate_ref, new_send_rate_ref,
                new_recv_rate_ref):
    n_act = act_shape_ref.shape[1]
    stk = stk_ref[...] + got_ref[...]
    sender_total = stk[:, n_act:n_act + 1]
    receiver_total = stk[:, n_act + 1:n_act + 2]
    action_total = act_total_ref[...]
    new_act_shape_ref[...] = refresh(act_shape_ref[...], prior_shape + stk[:, :n_act])
    new_act_rate_ref[...] = refresh(act_rate_ref[...], prior_rate + sender_total * receiver_total)
    new_send_rate_ref[...] = refresh(send_rate_ref[...], prior_rate + receiver_total * action_total)
    new_recv_rate_ref[...] = refresh(recv_rate_ref[...], prior_rate + sender_total * action_total)


def per_device(
    tile_counts,
    tile_sender,
    tile_receiver,
    tile_action,
    tile_fill,
    sender_log_shape,
    sender_log_rate,
    receiver_log_shape,
    receiver_log_rate,
    action_log_shape,
    action_log_rate,
):
    own_send_shape = sender_log_shape[0]
    own_send_rate = sender_log_rate[0]
    own_recv_shape = receiver_log_shape[0]
    own_recv_rate = receiver_log_rate[0]
    own_send_geo = geometric(own_send_shape, own_send_rate).astype(jnp.bfloat16)
    own_recv_geo = geometric(own_recv_shape, own_recv_rate).astype(jnp.bfloat16)
    n_snd = lax.psum(1, "snd")
    n_rcv = lax.psum(1, "rcv")
    sender_geo = gather_cols(own_send_geo, "rcv", n_rcv)
    receiver_geo = gather_cols(own_recv_geo, "snd", n_snd)
    action_geo = geometric(action_log_shape, action_log_rate)

    send_term, recv_term, act_term = tile_pass(
        tile_counts[0, 0],
        tile_sender[0, 0],
        tile_receiver[0, 0],
        tile_action[0, 0],
        tile_fill[0],
        sender_geo,
        receiver_geo,
        action_geo,
    )
    sender_part = jnp.sum(jnp.exp(own_send_shape - own_send_rate), axis=1)
    receiver_part = jnp.sum(jnp.exp(own_recv_shape - own_recv_rate), axis=1)
    n_act = act_term.shape[1]
    stacked = jnp.concatenate([act_term, sender_part[:, None], receiver_part[:, None]], axis=1)
    stacked, received = sum_all(stacked, (("rcv", n_rcv), ("snd", n_snd)))
    sender_stat = scatter_cols(send_term, "rcv", n_rcv)
    receiver_stat = scatter_cols(recv_term, "snd", n_snd)
    action_total = jnp.sum(jnp.exp(action_log_shape - action_log_rate), axis=1, keepdims=True)
    new_send_shape = refresh(own_send_shape, prior_shape + sender_stat)
    new_recv_shape = refresh(own_recv_shape, prior_shape + receiver_stat)
    new_act_shape, new_act_rate, new_send_rate, new_recv_rate = pl.pallas_call(
        tail_kernel,
        out_shape=[
            jax.ShapeDtypeStruct(action_log_shape.shape, jnp.float32),
            jax.ShapeDtypeStruct(action_log_rate.shape, jnp.float32),
            jax.ShapeDtypeStruct(own_send_rate.shape, jnp.float32),
            jax.ShapeDtypeStruct(own_recv_rate.shape, jnp.float32),
        ],
    )(stacked, received, action_log_shape, action_log_rate, own_send_rate, own_recv_rate, action_total)
    return (
        new_send_shape[None],
        new_send_rate[None],
        new_recv_shape[None],
        new_recv_rate[None],
        new_act_shape,
        new_act_rate,
    )


def solution(mesh):
    return jax.shard_map(
        per_device,
        mesh=mesh,
        in_specs=(
            P("snd", "rcv", None, None, None),
            P("snd", "rcv", None),
            P("snd", "rcv", None),
            P("snd", "rcv", None),
            P("snd", "rcv"),
            P("snd", None, "rcv"),
            P("snd", None, "rcv"),
            P("rcv", None, "snd"),
            P("rcv", None, "snd"),
            P(),
            P(),
        ),
        out_specs=(
            P("snd", None, "rcv"),
            P("snd", None, "rcv"),
            P("rcv", None, "snd"),
            P("rcv", None, "snd"),
            P(),
            P(),
        ),
        check_vma=False,
    )
```

```python
import jax
import jax.numpy as jnp
from jax import lax
from jax.experimental import pallas as pl
from jax.experimental.pallas import tpu as pltpu
from jax.sharding import PartitionSpec as P

prior_shape = 0.3
prior_rate = 0.3
step_size = 0.5
tile_group = 8


def digamma_series(value):
    shift_sum = jnp.zeros_like(value)
    for offset in range(6):
        shift_sum = shift_sum + 1.0 / (value + float(offset))
    moved = value + 6.0
    inverse = 1.0 / moved
    inv_square = inverse * inverse
    series = (
        jnp.log(moved)
        - 0.5 * inverse
        - inv_square * (1.0 / 12.0 - inv_square * (1.0 / 120.0 - inv_square / 252.0))
    )
    return series - shift_sum


def geometric(log_shape, log_rate):
    return jnp.exp(digamma_series(jnp.exp(log_shape)) - log_rate)


def refresh(log_value, target):
    return jnp.log((1.0 - step_size) * jnp.exp(log_value) + step_size * target)


def is_pow2(n):
    return n > 0 and n & (n - 1) == 0


def swap(x, axis, n, dist):
    return lax.ppermute(x, axis, [(i, i ^ dist) for i in range(n)])


def blocks_of(x, count):
    width = x.shape[1] // count
    return [x[:, i * width:(i + 1) * width] for i in range(count)]


def gather_cols(x, axis, n):
    if not is_pow2(n):
        return lax.all_gather(x, axis, axis=1, tiled=True)
    me = lax.axis_index(axis)
    count = 1
    dist = n // 2
    while dist >= 1:
        theirs = swap(x, axis, n, dist)
        low = (me & dist) == 0
        first = jnp.where(low, x, theirs)
        second = jnp.where(low, theirs, x)
        pairs = zip(blocks_of(first, count), blocks_of(second, count))
        x = jnp.concatenate([blk for pair in pairs for blk in pair], axis=1)
        count *= 2
        dist //= 2
    return x


def sum_all(x, axes):
    got = jnp.zeros_like(x)
    for axis, n in axes:
        if not is_pow2(n):
            x = lax.psum(x + got, axis)
            got = jnp.zeros_like(x)
            continue
        dist = 1
        while dist < n:
            x = x + got
            got = swap(x, axis, n, dist)
            dist *= 2
    return x, got


def scatter_cols(x, axis, n):
    if not is_pow2(n):
        return lax.psum_scatter(x, axis, scatter_dimension=1, tiled=True)
    me = lax.axis_index(axis)
    count = n
    dist = 1
    while dist < n:
        parts = blocks_of(x, count)
        even = jnp.concatenate(parts[0::2], axis=1)
        odd = jnp.concatenate(parts[1::2], axis=1)
        high = (me & dist) != 0
        keep = jnp.where(high, odd, even)
        give = jnp.where(high, even, odd)
        x = keep + swap(give, axis, n, dist)
        count //= 2
        dist *= 2
    return x


def tile_kernel(snd_ref, rcv_ref, act_ref, fill_ref, counts_ref, sgeo_ref, rgeo_ref, ageo_ref,
                totals_ref, sacc_ref, racc_ref, aacc_ref):
    step = pl.program_id(0)
    group = counts_ref.shape[0]
    edge = counts_ref.shape[-1]
    n_sb = sgeo_ref.shape[1] // edge
    n_rb = rgeo_ref.shape[1] // edge
    n_act = ageo_ref.shape[1]

    @pl.when(step == 0)
    def _():
        sacc_ref[...] = jnp.zeros_like(sacc_ref)
        racc_ref[...] = jnp.zeros_like(racc_ref)
        aacc_ref[:, :n_act] = jnp.zeros((aacc_ref.shape[0], n_act), jnp.float32)
        aacc_ref[:, n_act:] = totals_ref[...]

    for slot in range(group):
        pl.when(step * group + slot < fill_ref[0])(
            lambda slot=slot: one_tile(step * group + slot, counts_ref.at[slot], snd_ref, rcv_ref,
                                       act_ref, sgeo_ref, rgeo_ref, ageo_ref, sacc_ref, racc_ref,
                                       aacc_ref, edge, n_sb, n_rb, n_act)
        )


def one_tile(t, tile_ref, snd_ref, rcv_ref, act_ref, sgeo_ref, rgeo_ref, ageo_ref, sacc_ref,
             racc_ref, aacc_ref, edge, n_sb, n_rb, n_act):
    b = jnp.clip(snd_ref[t], 0, n_sb - 1)
    c = jnp.clip(rcv_ref[t], 0, n_rb - 1)
    a = jnp.clip(act_ref[t], 0, n_act - 1)
    s0 = pl.multiple_of(b * edge, edge)
    r0 = pl.multiple_of(c * edge, edge)
    send_cols = sgeo_ref[:, pl.ds(s0, edge)]
    recv_cols = rgeo_ref[:, pl.ds(r0, edge)]
    ageo = ageo_ref[...]
    hit = lax.broadcasted_iota(jnp.int32, ageo.shape, 1) == a
    act_col = jnp.sum(jnp.where(hit, ageo, 0.0), axis=1, keepdims=True)
    scaled = (send_cols.astype(jnp.float32) * act_col).astype(jnp.bfloat16)
    expected = lax.dot_general(
        scaled, recv_cols, (((0,), (0,)), ((), ())), preferred_element_type=jnp.float32
    )
    ratios = (tile_ref[...].astype(jnp.float32) / expected).astype(jnp.bfloat16)
    toward_send = lax.dot_general(
        recv_cols, ratios, (((1,), (1,)), ((), ())), preferred_element_type=jnp.float32
    )
    toward_recv = jnp.dot(scaled, ratios, preferred_element_type=jnp.float32)
    send_part = scaled.astype(jnp.float32) * toward_send
    recv_part = recv_cols.astype(jnp.float32) * toward_recv
    act_part = jnp.sum(send_part, axis=1, keepdims=True)
    sacc_ref[:, pl.ds(s0, edge)] += send_part
    racc_ref[:, pl.ds(r0, edge)] += recv_part
    aacc_ref[:, :n_act] += jnp.where(hit, act_part, 0.0)


def tile_pass(counts, senders, receivers, actions, fill, sender_geo, receiver_geo, action_geo, totals):
    n_slots, edge = counts.shape[0], counts.shape[1]
    group = tile_group if n_slots % tile_group == 0 else 1
    rank = sender_geo.shape[0]
    full = lambda shape: pl.BlockSpec(shape, lambda t, *_: (0,) * len(shape))
    grid_spec = pltpu.PrefetchScalarGridSpec(
        num_scalar_prefetch=4,
        grid=(n_slots // group,),
        in_specs=[
            pl.BlockSpec(
                (group, edge, edge),
                lambda g, s, r, a, f: (jnp.minimum(g, jnp.maximum(f[0] - 1, 0) // group), 0, 0),
            ),
            full(sender_geo.shape),
            full(receiver_geo.shape),
            full(action_geo.shape),
            full(totals.shape),
        ],
        out_specs=[
            full((rank, sender_geo.shape[1])),
            full((rank, receiver_geo.shape[1])),
            full((rank, action_geo.shape[1] + totals.shape[1])),
        ],
    )
    return pl.pallas_call(
        tile_kernel,
        grid_spec=grid_spec,
        out_shape=[
            jax.ShapeDtypeStruct((rank, sender_geo.shape[1]), jnp.float32),
            jax.ShapeDtypeStruct((rank, receiver_geo.shape[1]), jnp.float32),
            jax.ShapeDtypeStruct((rank, action_geo.shape[1] + totals.shape[1]), jnp.float32),
        ],
        compiler_params=pltpu.CompilerParams(dimension_semantics=("arbitrary",)),
    )(senders, receivers, actions, fill, counts, sender_geo, receiver_geo, action_geo, totals)


def tail_kernel(stk_ref, got_ref, act_shape_ref, act_rate_ref, send_rate_ref, recv_rate_ref,
                act_total_ref, new_act_shape_ref, new_act_rate_ref, new_send_rate_ref,
                new_recv_rate_ref):
    n_act = act_shape_ref.shape[1]
    stk = stk_ref[...] + got_ref[...]
    sender_total = stk[:, n_act:n_act + 1]
    receiver_total = stk[:, n_act + 1:n_act + 2]
    action_total = act_total_ref[...]
    new_act_shape_ref[...] = refresh(act_shape_ref[...], prior_shape + stk[:, :n_act])
    new_act_rate_ref[...] = refresh(act_rate_ref[...], prior_rate + sender_total * receiver_total)
    new_send_rate_ref[...] = refresh(send_rate_ref[...], prior_rate + receiver_total * action_total)
    new_recv_rate_ref[...] = refresh(recv_rate_ref[...], prior_rate + sender_total * action_total)


def per_device(
    tile_counts,
    tile_sender,
    tile_receiver,
    tile_action,
    tile_fill,
    sender_log_shape,
    sender_log_rate,
    receiver_log_shape,
    receiver_log_rate,
    action_log_shape,
    action_log_rate,
):
    own_send_shape = sender_log_shape[0]
    own_send_rate = sender_log_rate[0]
    own_recv_shape = receiver_log_shape[0]
    own_recv_rate = receiver_log_rate[0]
    own_send_geo = geometric(own_send_shape, own_send_rate).astype(jnp.bfloat16)
    own_recv_geo = geometric(own_recv_shape, own_recv_rate).astype(jnp.bfloat16)
    n_snd = lax.psum(1, "snd")
    n_rcv = lax.psum(1, "rcv")
    sender_geo = gather_cols(own_send_geo, "rcv", n_rcv)
    receiver_geo = gather_cols(own_recv_geo, "snd", n_snd)
    action_geo = geometric(action_log_shape, action_log_rate)

    sender_part = jnp.sum(jnp.exp(own_send_shape - own_send_rate), axis=1, keepdims=True)
    receiver_part = jnp.sum(jnp.exp(own_recv_shape - own_recv_rate), axis=1, keepdims=True)
    totals = jnp.concatenate(
        [sender_part, receiver_part, jnp.zeros((sender_part.shape[0], 126), jnp.float32)], axis=1
    )
    send_term, recv_term, stacked = tile_pass(
        tile_counts[0, 0],
        tile_sender[0, 0],
        tile_receiver[0, 0],
        tile_action[0, 0],
        tile_fill[0],
        sender_geo,
        receiver_geo,
        action_geo,
        totals,
    )
    stacked, received = sum_all(stacked, (("rcv", n_rcv), ("snd", n_snd)))
    sender_stat = scatter_cols(send_term, "rcv", n_rcv)
    receiver_stat = scatter_cols(recv_term, "snd", n_snd)
    action_total = jnp.sum(jnp.exp(action_log_shape - action_log_rate), axis=1, keepdims=True)
    new_send_shape = refresh(own_send_shape, prior_shape + sender_stat)
    new_recv_shape = refresh(own_recv_shape, prior_shape + receiver_stat)
    new_act_shape, new_act_rate, new_send_rate, new_recv_rate = pl.pallas_call(
        tail_kernel,
        out_shape=[
            jax.ShapeDtypeStruct(action_log_shape.shape, jnp.float32),
            jax.ShapeDtypeStruct(action_log_rate.shape, jnp.float32),
            jax.ShapeDtypeStruct(own_send_rate.shape, jnp.float32),
            jax.ShapeDtypeStruct(own_recv_rate.shape, jnp.float32),
        ],
    )(stacked, received, action_log_shape, action_log_rate, own_send_rate, own_recv_rate, action_total)
    return (
        new_send_shape[None],
        new_send_rate[None],
        new_recv_shape[None],
        new_recv_rate[None],
        new_act_shape,
        new_act_rate,
    )


def solution(mesh):
    return jax.shard_map(
        per_device,
        mesh=mesh,
        in_specs=(
            P("snd", "rcv", None, None, None),
            P("snd", "rcv", None),
            P("snd", "rcv", None),
            P("snd", "rcv", None),
            P("snd", "rcv"),
            P("snd", None, "rcv"),
            P("snd", None, "rcv"),
            P("rcv", None, "snd"),
            P("rcv", None, "snd"),
            P(),
            P(),
        ),
        out_specs=(
            P("snd", None, "rcv"),
            P("snd", None, "rcv"),
            P("rcv", None, "snd"),
            P("rcv", None, "snd"),
            P(),
            P(),
        ),
        check_vma=False,
    )
```

```python
import jax
import jax.numpy as jnp
from jax import lax
from jax.experimental import pallas as pl
from jax.experimental.pallas import tpu as pltpu
from jax.sharding import PartitionSpec as P

prior_shape = 0.3
prior_rate = 0.3
step_size = 0.5
tile_group = 8


def digamma_series(value):
    shift_sum = jnp.zeros_like(value)
    for offset in range(6):
        shift_sum = shift_sum + 1.0 / (value + float(offset))
    moved = value + 6.0
    inverse = 1.0 / moved
    inv_square = inverse * inverse
    series = (
        jnp.log(moved)
        - 0.5 * inverse
        - inv_square * (1.0 / 12.0 - inv_square * (1.0 / 120.0 - inv_square / 252.0))
    )
    return series - shift_sum


def geometric(log_shape, log_rate):
    return jnp.exp(digamma_series(jnp.exp(log_shape)) - log_rate)


def refresh(log_value, target):
    return jnp.log((1.0 - step_size) * jnp.exp(log_value) + step_size * target)


def is_pow2(n):
    return n > 0 and n & (n - 1) == 0


def swap(x, axis, n, dist):
    return lax.ppermute(x, axis, [(i, i ^ dist) for i in range(n)])


def blocks_of(x, count):
    width = x.shape[1] // count
    return [x[:, i * width:(i + 1) * width] for i in range(count)]


def gather_cols(x, axis, n):
    if not is_pow2(n):
        return lax.all_gather(x, axis, axis=1, tiled=True)
    me = lax.axis_index(axis)
    count = 1
    dist = n // 2
    while dist >= 1:
        theirs = swap(x, axis, n, dist)
        low = (me & dist) == 0
        first = jnp.where(low, x, theirs)
        second = jnp.where(low, theirs, x)
        pairs = zip(blocks_of(first, count), blocks_of(second, count))
        x = jnp.concatenate([blk for pair in pairs for blk in pair], axis=1)
        count *= 2
        dist //= 2
    return x


def sum_all(x, axes):
    got = jnp.zeros_like(x)
    for axis, n in axes:
        if not is_pow2(n):
            x = lax.psum(x + got, axis)
            got = jnp.zeros_like(x)
            continue
        dist = 1
        while dist < n:
            x = x + got
            got = swap(x, axis, n, dist)
            dist *= 2
    return x, got


def scatter_cols(x, axis, n):
    if not is_pow2(n):
        return lax.psum_scatter(x, axis, scatter_dimension=1, tiled=True)
    me = lax.axis_index(axis)
    count = n
    dist = 1
    while dist < n:
        parts = blocks_of(x, count)
        even = jnp.concatenate(parts[0::2], axis=1)
        odd = jnp.concatenate(parts[1::2], axis=1)
        high = (me & dist) != 0
        keep = jnp.where(high, odd, even)
        give = jnp.where(high, even, odd)
        x = keep + swap(give, axis, n, dist)
        count //= 2
        dist *= 2
    return x


def tile_kernel(snd_ref, rcv_ref, act_ref, fill_ref, counts_ref, sgeo_ref, rgeo_ref, ageo_ref,
                sacc_ref, racc_ref, aacc_ref):
    step = pl.program_id(0)
    group = counts_ref.shape[0]
    edge = counts_ref.shape[-1]
    n_sb = sgeo_ref.shape[1] // edge
    n_rb = rgeo_ref.shape[1] // edge
    n_act = ageo_ref.shape[1]

    @pl.when(step == 0)
    def _():
        sacc_ref[...] = jnp.zeros_like(sacc_ref)
        racc_ref[...] = jnp.zeros_like(racc_ref)
        aacc_ref[...] = jnp.zeros_like(aacc_ref)

    for slot in range(group):
        pl.when(step * group + slot < fill_ref[0])(
            lambda slot=slot: one_tile(step * group + slot, counts_ref.at[slot], snd_ref, rcv_ref,
                                       act_ref, sgeo_ref, rgeo_ref, ageo_ref, sacc_ref, racc_ref,
                                       aacc_ref, edge, n_sb, n_rb, n_act)
        )


def one_tile(t, tile_ref, snd_ref, rcv_ref, act_ref, sgeo_ref, rgeo_ref, ageo_ref, sacc_ref,
             racc_ref, aacc_ref, edge, n_sb, n_rb, n_act):
    b = jnp.clip(snd_ref[t], 0, n_sb - 1)
    c = jnp.clip(rcv_ref[t], 0, n_rb - 1)
    a = jnp.clip(act_ref[t], 0, n_act - 1)
    s0 = pl.multiple_of(b * edge, edge)
    r0 = pl.multiple_of(c * edge, edge)
    send_cols = sgeo_ref[:, pl.ds(s0, edge)]
    recv_cols = rgeo_ref[:, pl.ds(r0, edge)]
    ageo = ageo_ref[...]
    hit = lax.broadcasted_iota(jnp.int32, ageo.shape, 1) == a
    act_col = jnp.sum(jnp.where(hit, ageo, 0.0), axis=1, keepdims=True)
    scaled = (send_cols.astype(jnp.float32) * act_col).astype(jnp.bfloat16)
    expected = lax.dot_general(
        scaled, recv_cols, (((0,), (0,)), ((), ())), preferred_element_type=jnp.float32
    )
    ratios = (tile_ref[...].astype(jnp.float32) / expected).astype(jnp.bfloat16)
    toward_send = lax.dot_general(
        recv_cols, ratios, (((1,), (1,)), ((), ())), preferred_element_type=jnp.float32
    )
    toward_recv = jnp.dot(scaled, ratios, preferred_element_type=jnp.float32)
    send_part = scaled.astype(jnp.float32) * toward_send
    recv_part = recv_cols.astype(jnp.float32) * toward_recv
    act_part = jnp.sum(send_part, axis=1, keepdims=True)
    sacc_ref[:, pl.ds(s0, edge)] += send_part
    racc_ref[:, pl.ds(r0, edge)] += recv_part
    aacc_ref[...] += jnp.where(hit, act_part, 0.0)


def tile_pass(counts, senders, receivers, actions, fill, sender_geo, receiver_geo, action_geo):
    n_slots, edge = counts.shape[0], counts.shape[1]
    group = tile_group if n_slots % tile_group == 0 else 1
    rank = sender_geo.shape[0]
    full = lambda shape: pl.BlockSpec(shape, lambda t, *_: (0,) * len(shape))
    grid_spec = pltpu.PrefetchScalarGridSpec(
        num_scalar_prefetch=4,
        grid=(n_slots // group,),
        in_specs=[
            pl.BlockSpec(
                (group, edge, edge),
                lambda g, s, r, a, f: (jnp.minimum(g, jnp.maximum(f[0] - 1, 0) // group), 0, 0),
            ),
            full(sender_geo.shape),
            full(receiver_geo.shape),
            full(action_geo.shape),
        ],
        out_specs=[
            full((rank, sender_geo.shape[1])),
            full((rank, receiver_geo.shape[1])),
            full((rank, action_geo.shape[1])),
        ],
    )
    return pl.pallas_call(
        tile_kernel,
        grid_spec=grid_spec,
        out_shape=[
            jax.ShapeDtypeStruct((rank, sender_geo.shape[1]), jnp.float32),
            jax.ShapeDtypeStruct((rank, receiver_geo.shape[1]), jnp.float32),
            jax.ShapeDtypeStruct((rank, action_geo.shape[1]), jnp.float32),
        ],
        compiler_params=pltpu.CompilerParams(dimension_semantics=("arbitrary",)),
    )(senders, receivers, actions, fill, counts, sender_geo, receiver_geo, action_geo)


def tail_kernel(stk_ref, got_ref, act_shape_ref, act_rate_ref, send_rate_ref, recv_rate_ref,
                act_total_ref, new_act_shape_ref, new_act_rate_ref, new_send_rate_ref,
                new_recv_rate_ref):
    n_act = act_shape_ref.shape[1]
    stk = stk_ref[...] + got_ref[...]
    sender_total = stk[:, n_act:n_act + 1]
    receiver_total = stk[:, n_act + 1:n_act + 2]
    action_total = act_total_ref[...]
    new_act_shape_ref[...] = refresh(act_shape_ref[...], prior_shape + stk[:, :n_act])
    new_act_rate_ref[...] = refresh(act_rate_ref[...], prior_rate + sender_total * receiver_total)
    new_send_rate_ref[...] = refresh(send_rate_ref[...], prior_rate + receiver_total * action_total)
    new_recv_rate_ref[...] = refresh(recv_rate_ref[...], prior_rate + sender_total * action_total)


def per_device(
    tile_counts,
    tile_sender,
    tile_receiver,
    tile_action,
    tile_fill,
    sender_log_shape,
    sender_log_rate,
    receiver_log_shape,
    receiver_log_rate,
    action_log_shape,
    action_log_rate,
):
    own_send_shape = sender_log_shape[0]
    own_send_rate = sender_log_rate[0]
    own_recv_shape = receiver_log_shape[0]
    own_recv_rate = receiver_log_rate[0]
    own_recv_geo = geometric(own_recv_shape, own_recv_rate).astype(jnp.bfloat16)
    own_recv_geo, send_shape_after, send_rate_after = lax.optimization_barrier(
        (own_recv_geo, own_send_shape, own_send_rate)
    )
    own_send_geo = geometric(send_shape_after, send_rate_after).astype(jnp.bfloat16)
    n_snd = lax.psum(1, "snd")
    n_rcv = lax.psum(1, "rcv")
    sender_geo = gather_cols(own_send_geo, "rcv", n_rcv)
    receiver_geo = gather_cols(own_recv_geo, "snd", n_snd)
    action_geo = geometric(action_log_shape, action_log_rate)

    send_term, recv_term, act_term = tile_pass(
        tile_counts[0, 0],
        tile_sender[0, 0],
        tile_receiver[0, 0],
        tile_action[0, 0],
        tile_fill[0],
        sender_geo,
        receiver_geo,
        action_geo,
    )
    sender_part = jnp.sum(jnp.exp(own_send_shape - own_send_rate), axis=1)
    receiver_part = jnp.sum(jnp.exp(own_recv_shape - own_recv_rate), axis=1)
    n_act = act_term.shape[1]
    stacked = jnp.concatenate([act_term, sender_part[:, None], receiver_part[:, None]], axis=1)
    stacked, received = sum_all(stacked, (("rcv", n_rcv), ("snd", n_snd)))
    sender_stat = scatter_cols(send_term, "rcv", n_rcv)
    receiver_stat = scatter_cols(recv_term, "snd", n_snd)
    action_total = jnp.sum(jnp.exp(action_log_shape - action_log_rate), axis=1, keepdims=True)
    new_send_shape = refresh(own_send_shape, prior_shape + sender_stat)
    new_recv_shape = refresh(own_recv_shape, prior_shape + receiver_stat)
    new_act_shape, new_act_rate, new_send_rate, new_recv_rate = pl.pallas_call(
        tail_kernel,
        out_shape=[
            jax.ShapeDtypeStruct(action_log_shape.shape, jnp.float32),
            jax.ShapeDtypeStruct(action_log_rate.shape, jnp.float32),
            jax.ShapeDtypeStruct(own_send_rate.shape, jnp.float32),
            jax.ShapeDtypeStruct(own_recv_rate.shape, jnp.float32),
        ],
    )(stacked, received, action_log_shape, action_log_rate, own_send_rate, own_recv_rate, action_total)
    return (
        new_send_shape[None],
        new_send_rate[None],
        new_recv_shape[None],
        new_recv_rate[None],
        new_act_shape,
        new_act_rate,
    )


def solution(mesh):
    return jax.shard_map(
        per_device,
        mesh=mesh,
        in_specs=(
            P("snd", "rcv", None, None, None),
            P("snd", "rcv", None),
            P("snd", "rcv", None),
            P("snd", "rcv", None),
            P("snd", "rcv"),
            P("snd", None, "rcv"),
            P("snd", None, "rcv"),
            P("rcv", None, "snd"),
            P("rcv", None, "snd"),
            P(),
            P(),
        ),
        out_specs=(
            P("snd", None, "rcv"),
            P("snd", None, "rcv"),
            P("rcv", None, "snd"),
            P("rcv", None, "snd"),
            P(),
            P(),
        ),
        check_vma=False,
    )
```

```python
import jax
import jax.numpy as jnp
from jax import lax
from jax.experimental import pallas as pl
from jax.experimental.pallas import tpu as pltpu
from jax.sharding import PartitionSpec as P

prior_shape = 0.3
prior_rate = 0.3
step_size = 0.5
tile_group = 16


def digamma_series(value):
    shift_sum = jnp.zeros_like(value)
    for offset in range(6):
        shift_sum = shift_sum + 1.0 / (value + float(offset))
    moved = value + 6.0
    inverse = 1.0 / moved
    inv_square = inverse * inverse
    series = (
        jnp.log(moved)
        - 0.5 * inverse
        - inv_square * (1.0 / 12.0 - inv_square * (1.0 / 120.0 - inv_square / 252.0))
    )
    return series - shift_sum


def geometric(log_shape, log_rate):
    return jnp.exp(digamma_series(jnp.exp(log_shape)) - log_rate)


def refresh(log_value, target):
    return jnp.log((1.0 - step_size) * jnp.exp(log_value) + step_size * target)


def is_pow2(n):
    return n > 0 and n & (n - 1) == 0


def swap(x, axis, n, dist):
    return lax.ppermute(x, axis, [(i, i ^ dist) for i in range(n)])


def blocks_of(x, count):
    width = x.shape[1] // count
    return [x[:, i * width:(i + 1) * width] for i in range(count)]


def gather_cols(x, axis, n):
    if not is_pow2(n):
        return lax.all_gather(x, axis, axis=1, tiled=True)
    me = lax.axis_index(axis)
    count = 1
    dist = n // 2
    while dist >= 1:
        theirs = swap(x, axis, n, dist)
        low = (me & dist) == 0
        first = jnp.where(low, x, theirs)
        second = jnp.where(low, theirs, x)
        pairs = zip(blocks_of(first, count), blocks_of(second, count))
        x = jnp.concatenate([blk for pair in pairs for blk in pair], axis=1)
        count *= 2
        dist //= 2
    return x


def sum_all(x, axes):
    got = jnp.zeros_like(x)
    for axis, n in axes:
        if not is_pow2(n):
            x = lax.psum(x + got, axis)
            got = jnp.zeros_like(x)
            continue
        dist = 1
        while dist < n:
            x = x + got
            got = swap(x, axis, n, dist)
            dist *= 2
    return x, got


def scatter_cols(x, axis, n):
    if not is_pow2(n):
        return lax.psum_scatter(x, axis, scatter_dimension=1, tiled=True)
    me = lax.axis_index(axis)
    count = n
    dist = 1
    while dist < n:
        parts = blocks_of(x, count)
        even = jnp.concatenate(parts[0::2], axis=1)
        odd = jnp.concatenate(parts[1::2], axis=1)
        high = (me & dist) != 0
        keep = jnp.where(high, odd, even)
        give = jnp.where(high, even, odd)
        x = keep + swap(give, axis, n, dist)
        count //= 2
        dist *= 2
    return x


def tile_kernel(snd_ref, rcv_ref, act_ref, fill_ref, counts_ref, sgeo_ref, rgeo_ref, ageo_ref,
                sacc_ref, racc_ref, aacc_ref):
    step = pl.program_id(0)
    group = counts_ref.shape[0]
    edge = counts_ref.shape[-1]
    n_sb = sgeo_ref.shape[1] // edge
    n_rb = rgeo_ref.shape[1] // edge
    n_act = ageo_ref.shape[1]

    @pl.when(step == 0)
    def _():
        sacc_ref[...] = jnp.zeros_like(sacc_ref)
        racc_ref[...] = jnp.zeros_like(racc_ref)
        aacc_ref[...] = jnp.zeros_like(aacc_ref)

    for slot in range(group):
        pl.when(step * group + slot < fill_ref[0])(
            lambda slot=slot: one_tile(step * group + slot, counts_ref.at[slot], snd_ref, rcv_ref,
                                       act_ref, sgeo_ref, rgeo_ref, ageo_ref, sacc_ref, racc_ref,
                                       aacc_ref, edge, n_sb, n_rb, n_act)
        )


def one_tile(t, tile_ref, snd_ref, rcv_ref, act_ref, sgeo_ref, rgeo_ref, ageo_ref, sacc_ref,
             racc_ref, aacc_ref, edge, n_sb, n_rb, n_act):
    b = jnp.clip(snd_ref[t], 0, n_sb - 1)
    c = jnp.clip(rcv_ref[t], 0, n_rb - 1)
    a = jnp.clip(act_ref[t], 0, n_act - 1)
    s0 = pl.multiple_of(b * edge, edge)
    r0 = pl.multiple_of(c * edge, edge)
    send_cols = sgeo_ref[:, pl.ds(s0, edge)]
    recv_cols = rgeo_ref[:, pl.ds(r0, edge)]
    ageo = ageo_ref[...]
    hit = lax.broadcasted_iota(jnp.int32, ageo.shape, 1) == a
    act_col = jnp.sum(jnp.where(hit, ageo, 0.0), axis=1, keepdims=True)
    scaled = (send_cols.astype(jnp.float32) * act_col).astype(jnp.bfloat16)
    expected = lax.dot_general(
        scaled, recv_cols, (((0,), (0,)), ((), ())), preferred_element_type=jnp.float32
    )
    ratios = (tile_ref[...].astype(jnp.float32) / expected).astype(jnp.bfloat16)
    toward_send = lax.dot_general(
        recv_cols, ratios, (((1,), (1,)), ((), ())), preferred_element_type=jnp.float32
    )
    toward_recv = jnp.dot(scaled, ratios, preferred_element_type=jnp.float32)
    send_part = scaled.astype(jnp.float32) * toward_send
    recv_part = recv_cols.astype(jnp.float32) * toward_recv
    act_part = jnp.sum(send_part, axis=1, keepdims=True)
    sacc_ref[:, pl.ds(s0, edge)] += send_part
    racc_ref[:, pl.ds(r0, edge)] += recv_part
    aacc_ref[...] += jnp.where(hit, act_part, 0.0)


def tile_pass(counts, senders, receivers, actions, fill, sender_geo, receiver_geo, action_geo):
    n_slots, edge = counts.shape[0], counts.shape[1]
    group = tile_group if n_slots % tile_group == 0 else 1
    rank = sender_geo.shape[0]
    full = lambda shape: pl.BlockSpec(shape, lambda t, *_: (0,) * len(shape))
    grid_spec = pltpu.PrefetchScalarGridSpec(
        num_scalar_prefetch=4,
        grid=(n_slots // group,),
        in_specs=[
            pl.BlockSpec(
                (group, edge, edge),
                lambda g, s, r, a, f: (jnp.minimum(g, jnp.maximum(f[0] - 1, 0) // group), 0, 0),
            ),
            full(sender_geo.shape),
            full(receiver_geo.shape),
            full(action_geo.shape),
        ],
        out_specs=[
            full((rank, sender_geo.shape[1])),
            full((rank, receiver_geo.shape[1])),
            full((rank, action_geo.shape[1])),
        ],
    )
    return pl.pallas_call(
        tile_kernel,
        grid_spec=grid_spec,
        out_shape=[
            jax.ShapeDtypeStruct((rank, sender_geo.shape[1]), jnp.float32),
            jax.ShapeDtypeStruct((rank, receiver_geo.shape[1]), jnp.float32),
            jax.ShapeDtypeStruct((rank, action_geo.shape[1]), jnp.float32),
        ],
        compiler_params=pltpu.CompilerParams(dimension_semantics=("arbitrary",)),
    )(senders, receivers, actions, fill, counts, sender_geo, receiver_geo, action_geo)


def tail_kernel(stk_ref, got_ref, act_shape_ref, act_rate_ref, send_rate_ref, recv_rate_ref,
                act_total_ref, new_act_shape_ref, new_act_rate_ref, new_send_rate_ref,
                new_recv_rate_ref):
    n_act = act_shape_ref.shape[1]
    stk = stk_ref[...] + got_ref[...]
    sender_total = stk[:, n_act:n_act + 1]
    receiver_total = stk[:, n_act + 1:n_act + 2]
    action_total = act_total_ref[...]
    new_act_shape_ref[...] = refresh(act_shape_ref[...], prior_shape + stk[:, :n_act])
    new_act_rate_ref[...] = refresh(act_rate_ref[...], prior_rate + sender_total * receiver_total)
    new_send_rate_ref[...] = refresh(send_rate_ref[...], prior_rate + receiver_total * action_total)
    new_recv_rate_ref[...] = refresh(recv_rate_ref[...], prior_rate + sender_total * action_total)


def per_device(
    tile_counts,
    tile_sender,
    tile_receiver,
    tile_action,
    tile_fill,
    sender_log_shape,
    sender_log_rate,
    receiver_log_shape,
    receiver_log_rate,
    action_log_shape,
    action_log_rate,
):
    own_send_shape = sender_log_shape[0]
    own_send_rate = sender_log_rate[0]
    own_recv_shape = receiver_log_shape[0]
    own_recv_rate = receiver_log_rate[0]
    own_send_geo = geometric(own_send_shape, own_send_rate).astype(jnp.bfloat16)
    own_recv_geo = geometric(own_recv_shape, own_recv_rate).astype(jnp.bfloat16)
    n_snd = lax.psum(1, "snd")
    n_rcv = lax.psum(1, "rcv")
    sender_geo = gather_cols(own_send_geo, "rcv", n_rcv)
    receiver_geo = gather_cols(own_recv_geo, "snd", n_snd)
    action_geo = geometric(action_log_shape, action_log_rate)

    send_term, recv_term, act_term = tile_pass(
        tile_counts[0, 0],
        tile_sender[0, 0],
        tile_receiver[0, 0],
        tile_action[0, 0],
        tile_fill[0],
        sender_geo,
        receiver_geo,
        action_geo,
    )
    sender_part = jnp.sum(jnp.exp(own_send_shape - own_send_rate), axis=1)
    receiver_part = jnp.sum(jnp.exp(own_recv_shape - own_recv_rate), axis=1)
    n_act = act_term.shape[1]
    stacked = jnp.concatenate([act_term, sender_part[:, None], receiver_part[:, None]], axis=1)
    stacked, received = sum_all(stacked, (("rcv", n_rcv), ("snd", n_snd)))
    sender_stat = scatter_cols(send_term, "rcv", n_rcv)
    receiver_stat = scatter_cols(recv_term, "snd", n_snd)
    action_total = jnp.sum(jnp.exp(action_log_shape - action_log_rate), axis=1, keepdims=True)
    new_send_shape = refresh(own_send_shape, prior_shape + sender_stat)
    new_recv_shape = refresh(own_recv_shape, prior_shape + receiver_stat)
    new_act_shape, new_act_rate, new_send_rate, new_recv_rate = pl.pallas_call(
        tail_kernel,
        out_shape=[
            jax.ShapeDtypeStruct(action_log_shape.shape, jnp.float32),
            jax.ShapeDtypeStruct(action_log_rate.shape, jnp.float32),
            jax.ShapeDtypeStruct(own_send_rate.shape, jnp.float32),
            jax.ShapeDtypeStruct(own_recv_rate.shape, jnp.float32),
        ],
    )(stacked, received, action_log_shape, action_log_rate, own_send_rate, own_recv_rate, action_total)
    return (
        new_send_shape[None],
        new_send_rate[None],
        new_recv_shape[None],
        new_recv_rate[None],
        new_act_shape,
        new_act_rate,
    )


def solution(mesh):
    return jax.shard_map(
        per_device,
        mesh=mesh,
        in_specs=(
            P("snd", "rcv", None, None, None),
            P("snd", "rcv", None),
            P("snd", "rcv", None),
            P("snd", "rcv", None),
            P("snd", "rcv"),
            P("snd", None, "rcv"),
            P("snd", None, "rcv"),
            P("rcv", None, "snd"),
            P("rcv", None, "snd"),
            P(),
            P(),
        ),
        out_specs=(
            P("snd", None, "rcv"),
            P("snd", None, "rcv"),
            P("rcv", None, "snd"),
            P("rcv", None, "snd"),
            P(),
            P(),
        ),
        check_vma=False,
    )
```

```python
import jax
import jax.numpy as jnp
from jax import lax
from jax.experimental import pallas as pl
from jax.experimental.pallas import tpu as pltpu
from jax.sharding import PartitionSpec as P

prior_shape = 0.3
prior_rate = 0.3
step_size = 0.5
tile_group = 4


def digamma_series(value):
    shift_sum = jnp.zeros_like(value)
    for offset in range(6):
        shift_sum = shift_sum + 1.0 / (value + float(offset))
    moved = value + 6.0
    inverse = 1.0 / moved
    inv_square = inverse * inverse
    series = (
        jnp.log(moved)
        - 0.5 * inverse
        - inv_square * (1.0 / 12.0 - inv_square * (1.0 / 120.0 - inv_square / 252.0))
    )
    return series - shift_sum


def geometric(log_shape, log_rate):
    return jnp.exp(digamma_series(jnp.exp(log_shape)) - log_rate)


def refresh(log_value, target):
    return jnp.log((1.0 - step_size) * jnp.exp(log_value) + step_size * target)


def is_pow2(n):
    return n > 0 and n & (n - 1) == 0


def swap(x, axis, n, dist):
    return lax.ppermute(x, axis, [(i, i ^ dist) for i in range(n)])


def blocks_of(x, count):
    width = x.shape[1] // count
    return [x[:, i * width:(i + 1) * width] for i in range(count)]


def gather_cols(x, axis, n):
    if not is_pow2(n):
        return lax.all_gather(x, axis, axis=1, tiled=True)
    me = lax.axis_index(axis)
    count = 1
    dist = n // 2
    while dist >= 1:
        theirs = swap(x, axis, n, dist)
        low = (me & dist) == 0
        first = jnp.where(low, x, theirs)
        second = jnp.where(low, theirs, x)
        pairs = zip(blocks_of(first, count), blocks_of(second, count))
        x = jnp.concatenate([blk for pair in pairs for blk in pair], axis=1)
        count *= 2
        dist //= 2
    return x


def sum_all(x, axes):
    got = jnp.zeros_like(x)
    for axis, n in axes:
        if not is_pow2(n):
            x = lax.psum(x + got, axis)
            got = jnp.zeros_like(x)
            continue
        dist = 1
        while dist < n:
            x = x + got
            got = swap(x, axis, n, dist)
            dist *= 2
    return x, got


def scatter_cols(x, axis, n):
    if not is_pow2(n):
        return lax.psum_scatter(x, axis, scatter_dimension=1, tiled=True)
    me = lax.axis_index(axis)
    count = n
    dist = 1
    while dist < n:
        parts = blocks_of(x, count)
        even = jnp.concatenate(parts[0::2], axis=1)
        odd = jnp.concatenate(parts[1::2], axis=1)
        high = (me & dist) != 0
        keep = jnp.where(high, odd, even)
        give = jnp.where(high, even, odd)
        x = keep + swap(give, axis, n, dist)
        count //= 2
        dist *= 2
    return x


def tile_kernel(snd_ref, rcv_ref, act_ref, fill_ref, counts_ref, sgeo_ref, rgeo_ref, ageo_ref,
                sacc_ref, racc_ref, aacc_ref):
    step = pl.program_id(0)
    group = counts_ref.shape[0]
    edge = counts_ref.shape[-1]
    n_sb = sgeo_ref.shape[1] // edge
    n_rb = rgeo_ref.shape[1] // edge
    n_act = ageo_ref.shape[1]

    @pl.when(step == 0)
    def _():
        sacc_ref[...] = jnp.zeros_like(sacc_ref)
        racc_ref[...] = jnp.zeros_like(racc_ref)
        aacc_ref[...] = jnp.zeros_like(aacc_ref)

    for slot in range(group):
        pl.when(step * group + slot < fill_ref[0])(
            lambda slot=slot: one_tile(step * group + slot, counts_ref.at[slot], snd_ref, rcv_ref,
                                       act_ref, sgeo_ref, rgeo_ref, ageo_ref, sacc_ref, racc_ref,
                                       aacc_ref, edge, n_sb, n_rb, n_act)
        )


def one_tile(t, tile_ref, snd_ref, rcv_ref, act_ref, sgeo_ref, rgeo_ref, ageo_ref, sacc_ref,
             racc_ref, aacc_ref, edge, n_sb, n_rb, n_act):
    b = jnp.clip(snd_ref[t], 0, n_sb - 1)
    c = jnp.clip(rcv_ref[t], 0, n_rb - 1)
    a = jnp.clip(act_ref[t], 0, n_act - 1)
    s0 = pl.multiple_of(b * edge, edge)
    r0 = pl.multiple_of(c * edge, edge)
    send_cols = sgeo_ref[:, pl.ds(s0, edge)]
    recv_cols = rgeo_ref[:, pl.ds(r0, edge)]
    ageo = ageo_ref[...]
    hit = lax.broadcasted_iota(jnp.int32, ageo.shape, 1) == a
    act_col = jnp.sum(jnp.where(hit, ageo, 0.0), axis=1, keepdims=True)
    scaled = (send_cols.astype(jnp.float32) * act_col).astype(jnp.bfloat16)
    expected = lax.dot_general(
        scaled, recv_cols, (((0,), (0,)), ((), ())), preferred_element_type=jnp.float32
    )
    ratios = (tile_ref[...].astype(jnp.float32) / expected).astype(jnp.bfloat16)
    toward_send = lax.dot_general(
        recv_cols, ratios, (((1,), (1,)), ((), ())), preferred_element_type=jnp.float32
    )
    toward_recv = jnp.dot(scaled, ratios, preferred_element_type=jnp.float32)
    send_part = scaled.astype(jnp.float32) * toward_send
    recv_part = recv_cols.astype(jnp.float32) * toward_recv
    act_part = jnp.sum(send_part, axis=1, keepdims=True)
    sacc_ref[:, pl.ds(s0, edge)] += send_part
    racc_ref[:, pl.ds(r0, edge)] += recv_part
    aacc_ref[...] += jnp.where(hit, act_part, 0.0)


def tile_pass(counts, senders, receivers, actions, fill, sender_geo, receiver_geo, action_geo):
    n_slots, edge = counts.shape[0], counts.shape[1]
    group = tile_group if n_slots % tile_group == 0 else 1
    rank = sender_geo.shape[0]
    full = lambda shape: pl.BlockSpec(shape, lambda t, *_: (0,) * len(shape))
    grid_spec = pltpu.PrefetchScalarGridSpec(
        num_scalar_prefetch=4,
        grid=(n_slots // group,),
        in_specs=[
            pl.BlockSpec(
                (group, edge, edge),
                lambda g, s, r, a, f: (jnp.minimum(g, jnp.maximum(f[0] - 1, 0) // group), 0, 0),
            ),
            full(sender_geo.shape),
            full(receiver_geo.shape),
            full(action_geo.shape),
        ],
        out_specs=[
            full((rank, sender_geo.shape[1])),
            full((rank, receiver_geo.shape[1])),
            full((rank, action_geo.shape[1])),
        ],
    )
    return pl.pallas_call(
        tile_kernel,
        grid_spec=grid_spec,
        out_shape=[
            jax.ShapeDtypeStruct((rank, sender_geo.shape[1]), jnp.float32),
            jax.ShapeDtypeStruct((rank, receiver_geo.shape[1]), jnp.float32),
            jax.ShapeDtypeStruct((rank, action_geo.shape[1]), jnp.float32),
        ],
        compiler_params=pltpu.CompilerParams(dimension_semantics=("arbitrary",)),
    )(senders, receivers, actions, fill, counts, sender_geo, receiver_geo, action_geo)


def tail_kernel(stk_ref, got_ref, act_shape_ref, act_rate_ref, send_rate_ref, recv_rate_ref,
                act_total_ref, new_act_shape_ref, new_act_rate_ref, new_send_rate_ref,
                new_recv_rate_ref):
    n_act = act_shape_ref.shape[1]
    stk = stk_ref[...] + got_ref[...]
    sender_total = stk[:, n_act:n_act + 1]
    receiver_total = stk[:, n_act + 1:n_act + 2]
    action_total = act_total_ref[...]
    new_act_shape_ref[...] = refresh(act_shape_ref[...], prior_shape + stk[:, :n_act])
    new_act_rate_ref[...] = refresh(act_rate_ref[...], prior_rate + sender_total * receiver_total)
    new_send_rate_ref[...] = refresh(send_rate_ref[...], prior_rate + receiver_total * action_total)
    new_recv_rate_ref[...] = refresh(recv_rate_ref[...], prior_rate + sender_total * action_total)


def per_device(
    tile_counts,
    tile_sender,
    tile_receiver,
    tile_action,
    tile_fill,
    sender_log_shape,
    sender_log_rate,
    receiver_log_shape,
    receiver_log_rate,
    action_log_shape,
    action_log_rate,
):
    own_send_shape = sender_log_shape[0]
    own_send_rate = sender_log_rate[0]
    own_recv_shape = receiver_log_shape[0]
    own_recv_rate = receiver_log_rate[0]
    own_send_geo = geometric(own_send_shape, own_send_rate).astype(jnp.bfloat16)
    own_recv_geo = geometric(own_recv_shape, own_recv_rate).astype(jnp.bfloat16)
    n_snd = lax.psum(1, "snd")
    n_rcv = lax.psum(1, "rcv")
    sender_geo = gather_cols(own_send_geo, "rcv", n_rcv)
    receiver_geo = gather_cols(own_recv_geo, "snd", n_snd)
    action_geo = geometric(action_log_shape, action_log_rate)

    send_term, recv_term, act_term = tile_pass(
        tile_counts[0, 0],
        tile_sender[0, 0],
        tile_receiver[0, 0],
        tile_action[0, 0],
        tile_fill[0],
        sender_geo,
        receiver_geo,
        action_geo,
    )
    sender_part = jnp.sum(jnp.exp(own_send_shape - own_send_rate), axis=1)
    receiver_part = jnp.sum(jnp.exp(own_recv_shape - own_recv_rate), axis=1)
    n_act = act_term.shape[1]
    stacked = jnp.concatenate([act_term, sender_part[:, None], receiver_part[:, None]], axis=1)
    stacked, received = sum_all(stacked, (("rcv", n_rcv), ("snd", n_snd)))
    sender_stat = scatter_cols(send_term, "rcv", n_rcv)
    receiver_stat = scatter_cols(recv_term, "snd", n_snd)
    action_total = jnp.sum(jnp.exp(action_log_shape - action_log_rate), axis=1, keepdims=True)
    new_send_shape = refresh(own_send_shape, prior_shape + sender_stat)
    new_recv_shape = refresh(own_recv_shape, prior_shape + receiver_stat)
    new_act_shape, new_act_rate, new_send_rate, new_recv_rate = pl.pallas_call(
        tail_kernel,
        out_shape=[
            jax.ShapeDtypeStruct(action_log_shape.shape, jnp.float32),
            jax.ShapeDtypeStruct(action_log_rate.shape, jnp.float32),
            jax.ShapeDtypeStruct(own_send_rate.shape, jnp.float32),
            jax.ShapeDtypeStruct(own_recv_rate.shape, jnp.float32),
        ],
    )(stacked, received, action_log_shape, action_log_rate, own_send_rate, own_recv_rate, action_total)
    return (
        new_send_shape[None],
        new_send_rate[None],
        new_recv_shape[None],
        new_recv_rate[None],
        new_act_shape,
        new_act_rate,
    )


def solution(mesh):
    return jax.shard_map(
        per_device,
        mesh=mesh,
        in_specs=(
            P("snd", "rcv", None, None, None),
            P("snd", "rcv", None),
            P("snd", "rcv", None),
            P("snd", "rcv", None),
            P("snd", "rcv"),
            P("snd", None, "rcv"),
            P("snd", None, "rcv"),
            P("rcv", None, "snd"),
            P("rcv", None, "snd"),
            P(),
            P(),
        ),
        out_specs=(
            P("snd", None, "rcv"),
            P("snd", None, "rcv"),
            P("rcv", None, "snd"),
            P("rcv", None, "snd"),
            P(),
            P(),
        ),
        check_vma=False,
    )
```
